128 devices in a mesh: seq: 32 (over x, z_hi, y), exp: 4 (over z_lo, core).
Axes of the slice: x: 4, y: 4, z: 4 (z_hi: 2, z_lo: 2; z = z_hi * 2 + z_lo), core: 2. Of those that a mesh axis runs over, the one named last changes fastest.
Arguments:
- segment_ids: int32 [8192], replicated, may hold values from 0 to 130, as said below
- queries: bfloat16 [8192, 2048], P('seq', 'exp'), may hold values from -8 to 8
- keys: bfloat16 [8192, 2048], P('seq', 'exp'), may hold values from -8 to 8
- values: bfloat16 [8192, 2048], P('seq', 'exp'), may hold values from -6 to 6
- out_weight: bfloat16 [2048, 2048], P('exp'), may hold values from -0.125 to 0.125
- residual: bfloat16 [8192, 2048], P('seq'), may hold values from -16 to 16
- norm_gain: bfloat16 [2048], replicated, may hold values from 0.099609375 to 1.8984375
- shared_in: bfloat16 [2, 2048, 3072], P(None, None, 'exp'), may hold values from -0.125 to 0.125
- shared_out: bfloat16 [3072, 2048], P('exp'), may hold values from -0.109375 to 0.109375
- shared_gate: bfloat16 [2048], replicated, may hold values from -0.125 to 0.125
- expert_in: bfloat16 [64, 2, 2048, 1408], P('seq', None, None, 'exp'), may hold values from -0.125 to 0.125
- expert_out: bfloat16 [64, 1408, 2048], P('seq', 'exp'), may hold values from -0.15625 to 0.15625
- expert_ids: int32 [8192, 4], P('seq'), may hold values from 0 to 59, all different within a row; in each aligned block of 256 rows (0 to 255, 256 to 511, ...) at most 32 rows name the same one
- gate_weights: float32 [8192, 4], P('seq'), may hold values from 0.05 to 0.5
Outputs:
- mixed: bfloat16 [8192, 2048], P(('seq', 'exp'))
- attn_proj: bfloat16 [8192, 2048], P(('seq', 'exp'))
- key_cache: bfloat16 [8192, 2048], P('seq', 'exp')
The draws below stay inside these ranges and needn't reach their ends.
Inputs may be any that keep to these rules, and one draw needn't show every extreme that they name: `segment_ids`: never falls along the stream, starts at 0 and rises by at most one from a token to the next; there are exactly (2048) // 16 + 3 prompts; one prompt has exactly 6144 tokens, every other fewer. `expert_ids`: each row names 4 different experts; in each aligned block of 256 rows (the rows of one block of the stream) no expert is named by more than 32 rows, a bound that some block reaches.
All inputs are finite; a program needn't handle non-finite values.
Results may differ from the reference program's by a relative error of at most 0.012.
Values may be sent and summed in bfloat16 or wider, within the bound.
No kernel may reach another device: no remote copies, remote signals or barrier semaphores. Data moves between devices by JAX's collectives and lax.ppermute only.
A program may use at most 128 MiB of HBM per device.

```python
import math
import jax
import jax.numpy as jnp
import numpy as np
from jax import lax

D = 2048
HEADS = 16
HD = 128
EXPERTS = 60
EFF = 1408
SHARED = 3072
TOPK = 4
SLOTS = 64
TB = 256
CAP = 32
TOKENS = 8192
MOST = 6144
N_SEQ = 32
N_EXP = 4


def long_offset(key):
    return jax.random.randint(jax.random.fold_in(key, 11), (), 1, TOKENS - MOST)


def draw_segment_ids(key, part):
    offset = long_offset(key)
    token_index = jnp.arange(TOKENS, dtype=jnp.int32)
    inside = (token_index >= offset) & (token_index < offset + MOST)
    special = (token_index == 0) | (token_index == offset) | (token_index == offset + MOST)
    candidate = jnp.logical_not(inside) & jnp.logical_not(special)
    order_score = jax.random.permutation(jax.random.fold_in(key, 12), TOKENS).astype(jnp.int32)
    scored = jnp.where(candidate, order_score, -1)
    extra_count = (TOKENS - MOST) // 16
    chosen = lax_top(scored, extra_count)
    extra = jnp.zeros((TOKENS,), jnp.bool_).at[chosen].set(True)
    boundary = special | extra
    return jnp.cumsum(boundary.astype(jnp.int32), dtype=jnp.int32) - 1


def lax_top(scored, count):
    return jax.lax.top_k(scored, count)[1].astype(jnp.int32)


def draw_queries(key, part):
    return jnp.clip(jax.random.normal(jax.random.fold_in(key, 24), (TOKENS, HEADS * HD)), -4.0, 4.0).astype(jnp.bfloat16)


def draw_keys(key, part):
    return jnp.clip(jax.random.normal(jax.random.fold_in(key, 25), (TOKENS, HEADS * HD)), -4.0, 4.0).astype(jnp.bfloat16)


def draw_residual(key, part):
    row_scale = jnp.exp(jax.random.uniform(jax.random.fold_in(key, 32), (TOKENS, 1), minval=math.log(0.3), maxval=math.log(3.0)))
    col_scale = jnp.exp(jax.random.uniform(jax.random.fold_in(key, 33), (1, D), minval=math.log(0.5), maxval=math.log(2.0)))
    base_field = jnp.clip(jax.random.normal(jax.random.fold_in(key, 34), (TOKENS, D)), -4.0, 4.0)
    return jnp.clip(base_field * row_scale * col_scale, -16.0, 16.0).astype(jnp.bfloat16)


def block_scale(stream_key, shape, shards, smallest, top_value):
    def one(dim, shards_of):
        heights = jax.random.uniform(jax.random.fold_in(jax.random.fold_in(stream_key, 6), dim), (shards_of,), jnp.float32, smallest / len(shards), top_value / len(shards))
        return jnp.repeat(jnp.exp(heights), shape[dim] // shards_of).reshape((-1,) + (1,) * (len(shape) - dim - 1))

    loudness = one(*shards[0])
    for cut in shards[1:]:
        loudness = loudness * one(*cut)
    return loudness


def routed_block(key, own, number, rows, number_of, top, most, lean):
    ranking = jax.random.permutation(key, number_of)
    heavy_load, ordinary = shares(number_of, rows * top, most, lean, True), shares(number_of, rows * top, most, lean, False)
    places = jnp.arange(number_of)

    def named(sizes, rotation):
        used = int((sizes > 0).sum())
        fixed = max(1, used // 4)
        shifted = fixed + (places - fixed + rotation * (used - fixed)) % max(1, number_of - fixed)
        return jnp.zeros((number_of,), jnp.int32).at[ranking[jnp.where(places < fixed, places, shifted)]].set(jnp.asarray(sizes, jnp.int32))

    sizes = jnp.where(number % 4 == 0, named(heavy_load, number // 4), named(ordinary, number - number // 4 - 1))
    mixed = jax.random.permutation(jax.random.fold_in(own, 3), number_of)
    donor, receiver = mixed[0:number_of // 2 * 2:2], mixed[1:number_of // 2 * 2:2]
    room = jnp.minimum(sizes[donor] - 1, most - sizes[receiver]) // 2
    room = jnp.where((donor == ranking[0]) | (receiver == ranking[0]) | (sizes[receiver] == 0), 0, jnp.maximum(room, 0))
    shifted = jax.random.randint(jax.random.fold_in(own, 4), (number_of // 2,), 0, 1 << 20) % (room + 1)
    sizes = sizes.at[donor].add(-shifted).at[receiver].add(shifted)
    labels = jnp.searchsorted(jnp.cumsum(sizes), jnp.arange(rows * top), side="right").astype(jnp.int32)
    table = labels.reshape(top, rows).T
    table = table[jax.random.permutation(jax.random.fold_in(own, 1), rows)]
    rotation = jax.random.randint(jax.random.fold_in(own, 2), (rows, 1), 0, top)
    return jnp.take_along_axis(table, (jnp.arange(top)[None, :] + rotation) % top, axis=1)


def shares(amount, total, bound, lean, full):
    portions = [(1 << 20) // math.isqrt(standing ** lean) + 1 for standing in range(1, amount + 1)]
    largest = bound if full else min(bound, max(-(-total // amount), total * portions[0] // sum(portions)))
    least = 1 if total - largest >= amount - 1 else 0
    counts, rest = [largest] + [least] * (amount - 1), total - largest - least * (amount - 1)
    while rest > 0:
        movable = [i for i in range(1, amount) if counts[i] < largest] or [i for i in range(1, amount) if counts[i] < bound]
        whole, remaining = sum([portions[i] for i in movable]), rest
        for i in movable:
            more = min(bound - counts[i], max(1, remaining * portions[i] // whole), rest)
            counts[i] = counts[i] + more
            rest = rest - more
    return np.array(counts)


def bell_draw(own_key, dims, scale, limit, pieces=(), kind=jnp.bfloat16):
    result = scale * jax.random.normal(own_key, dims, jnp.float32)
    if pieces:
        result = result * block_scale(own_key, dims, pieces, -0.22, 0.18)
    return jnp.clip(result, -limit, limit).astype(kind)


def setup_inputs(seed: int = 0) -> dict:
    key_of = jax.random.split(jax.random.key(seed), 15)
    segment_ids = draw_segment_ids(jax.random.fold_in(key_of[14], 71), 0)
    queries = draw_queries(jax.random.fold_in(key_of[14], 71), 0)
    keys = draw_keys(jax.random.fold_in(key_of[14], 71), 0)
    values = bell_draw(key_of[3], (TOKENS, HEADS * HD), 1.0, 6.0, ((0, 32), (1, 4)))
    out_weight = bell_draw(key_of[4], (HEADS * HD, D), (HEADS * HD) ** -0.5, 0.125, ((0, 4),))
    residual = draw_residual(jax.random.fold_in(key_of[14], 71), 0)
    norm_gain = jnp.clip(1.0 + 0.18 * jax.random.normal(key_of[6], (D,), jnp.float32), 0.099609375, 1.8984375).astype(jnp.bfloat16)
    shared_in = bell_draw(key_of[7], (2, D, SHARED), D ** -0.5, 0.125, ((2, 4),))
    shared_out = bell_draw(key_of[8], (SHARED, D), SHARED ** -0.5, 0.109375, ((0, 4),))
    shared_gate = bell_draw(key_of[9], (D,), D ** -0.5, 0.125)
    expert_in = bell_draw(key_of[10], (SLOTS, 2, D, EFF), D ** -0.5, 0.125, ((0, 32), (3, 4)))
    expert_out = bell_draw(key_of[11], (SLOTS, EFF, D), EFF ** -0.5, 0.15625, ((0, 32), (1, 4)))
    expert_ids_keys = jax.random.split(jax.random.fold_in(key_of[12], 1), TOKENS // TB)
    expert_ids_turns = jax.random.permutation(jax.random.fold_in(key_of[12], 3), TOKENS // TB)
    expert_ids = jax.vmap(lambda own, number: routed_block(jax.random.fold_in(key_of[12], 2), own, number, TB, EXPERTS, TOPK, CAP, 2))(expert_ids_keys, expert_ids_turns).reshape((TOKENS, TOPK))
    gate_weights = jnp.clip(jnp.exp(math.log(0.5) - 2.3025851 * jax.random.uniform(key_of[13], (TOKENS, TOPK), jnp.float32) ** block_scale(key_of[13], (TOKENS, TOPK), ((0, 32),), -0.2, 0.2)), 0.05, 0.5)
    return dict(segment_ids=segment_ids, queries=queries, keys=keys, values=values, out_weight=out_weight, residual=residual, norm_gain=norm_gain, shared_in=shared_in, shared_out=shared_out, shared_gate=shared_gate, expert_in=expert_in, expert_out=expert_out, expert_ids=expert_ids, gate_weights=gate_weights)


rope_base = 1000000.0
neg_fill = -1e+30
norm_eps = 1e-06

def token_positions(segment_ids):
    stream_len = segment_ids.shape[0]
    token_index = jnp.arange(stream_len, dtype=jnp.int32)
    boundary = jnp.concatenate([jnp.ones((1,), jnp.bool_), segment_ids[1:] != segment_ids[:-1]])
    seg_start = lax.cummax(jnp.where(boundary, token_index, 0), axis=0)
    return (token_index - seg_start, seg_start)

def rotate(values_in, positions, head_count):
    half_dim = HD // 2
    frequency = rope_base ** (-(2.0 * jnp.arange(half_dim, dtype=jnp.float32)) / HD)
    angle_all = positions.astype(jnp.float32)[:, None] * frequency[None, :]
    cosine = jnp.cos(angle_all)[:, None, :]
    sine_part = jnp.sin(angle_all)[:, None, :]
    shaped = values_in.astype(jnp.float32).reshape(values_in.shape[0], head_count, HD)
    first_half = shaped[..., :half_dim]
    second_half = shaped[..., half_dim:]
    turned = jnp.concatenate([first_half * cosine - second_half * sine_part, second_half * cosine + first_half * sine_part], axis=-1)
    return turned.reshape(values_in.shape[0], head_count * HD).astype(jnp.bfloat16)

def rms_norm(hidden_in, norm_gain):
    mean_square = lax.optimization_barrier(jnp.mean(hidden_in * hidden_in, axis=-1, keepdims=True))
    return (hidden_in * lax.rsqrt(mean_square + norm_eps) * norm_gain.astype(jnp.float32)).astype(jnp.bfloat16)

def reference(segment_ids, queries, keys, values, out_weight, residual, norm_gain, shared_in, shared_out, shared_gate, expert_in, expert_out, expert_ids, gate_weights):
    positions, seg_start = token_positions(segment_ids)
    rotated_q = rotate(queries, positions, HEADS)
    key_cache = rotate(keys, positions, HEADS)
    block_len = math.gcd(TOKENS, 512)
    score_scale = 1.0 / math.sqrt(HD)
    token_index = jnp.arange(TOKENS, dtype=jnp.int32)

    def head_split(matrix):
        return matrix.reshape(TOKENS, HEADS, HD).transpose(1, 0, 2)

    def one_head(operands):
        head_q, head_k, head_v = operands

        def one_block(block_id):
            first_row = block_id * block_len
            query_rows = lax.dynamic_slice_in_dim(head_q, first_row, block_len, 0)
            scores = jnp.dot(query_rows, head_k.T, preferred_element_type=jnp.float32) * score_scale
            query_pos = first_row + jnp.arange(block_len, dtype=jnp.int32)
            query_seg = lax.dynamic_slice_in_dim(segment_ids, first_row, block_len, 0)
            visible = (token_index[None, :] <= query_pos[:, None]) & (segment_ids[None, :] == query_seg[:, None])
            row_max = lax.optimization_barrier(jnp.max(jnp.where(visible, scores, neg_fill), axis=-1, keepdims=True))
            weights_f = jnp.where(visible, jnp.exp(scores - row_max), 0.0)
            weights_b = weights_f.astype(jnp.bfloat16)
            summed = jnp.dot(weights_b, head_v, preferred_element_type=jnp.float32)
            return (summed / lax.optimization_barrier(jnp.sum(weights_f, axis=-1, keepdims=True))).astype(jnp.bfloat16)
        return lax.map(one_block, jnp.arange(TOKENS // block_len, dtype=jnp.int32)).reshape(TOKENS, HD)
    attended = lax.map(one_head, (head_split(rotated_q), head_split(key_cache), head_split(values)))
    attended = attended.transpose(1, 0, 2).reshape(TOKENS, HEADS * HD)
    attn_sum = jnp.dot(attended, out_weight, preferred_element_type=jnp.float32)
    attn_proj = attn_sum.astype(jnp.bfloat16)
    after_attn = residual.astype(jnp.float32) + attn_sum
    normed = rms_norm(after_attn, norm_gain)
    gate_pre = jnp.dot(normed, shared_in[0], preferred_element_type=jnp.float32)
    up_pre = jnp.dot(normed, shared_in[1], preferred_element_type=jnp.float32)
    shared_hidden = (jax.nn.silu(gate_pre) * up_pre).astype(jnp.bfloat16)
    shared_term = jnp.dot(shared_hidden, shared_out, preferred_element_type=jnp.float32)
    shared_factor = jax.nn.sigmoid(jnp.dot(normed, shared_gate, preferred_element_type=jnp.float32))
    flat_ids = expert_ids.reshape(N_SEQ, TB * TOPK)
    one_hot = (flat_ids[:, :, None] == jnp.arange(SLOTS, dtype=jnp.int32)[None, None, :]).astype(jnp.int32)
    slot_rank = lax.optimization_barrier(jnp.sum(jnp.cumsum(one_hot, axis=1, dtype=jnp.int32) * one_hot, axis=-1)) - 1
    block_id = jnp.arange(N_SEQ, dtype=jnp.int32)[:, None]
    slot_place = (flat_ids * N_SEQ + block_id) * CAP + slot_rank
    owner_row = block_id * TB + jnp.arange(TB * TOPK, dtype=jnp.int32)[None, :] // TOPK
    row_table = jnp.full((SLOTS * N_SEQ * CAP,), -1, jnp.int32).at[slot_place.reshape(-1)].set(owner_row.reshape(-1))
    gate_table = jnp.zeros((SLOTS * N_SEQ * CAP,), jnp.float32).at[slot_place.reshape(-1)].set(gate_weights.reshape(-1))
    quarter = EFF // N_EXP

    def one_expert(total_out, operands):
        weight_in, weight_out, table_rows, table_gates = operands
        valid_row = table_rows >= 0
        safe_rows = jnp.maximum(table_rows, 0)
        picked = jnp.where(valid_row[:, None], normed[safe_rows], jnp.zeros((), jnp.bfloat16))
        gate_e = jnp.dot(picked, weight_in[0], preferred_element_type=jnp.float32)
        up_e = jnp.dot(picked, weight_in[1], preferred_element_type=jnp.float32)
        hidden_e = (jax.nn.silu(gate_e) * up_e).astype(jnp.bfloat16)
        parts_out = jnp.einsum('rqe,qed->qrd', hidden_e.reshape(-1, N_EXP, quarter).astype(jnp.float32), weight_out.reshape(N_EXP, quarter, D).astype(jnp.float32))
        rounded = lax.optimization_barrier(parts_out.astype(jnp.bfloat16))
        expert_term = lax.optimization_barrier(jnp.sum(rounded.astype(jnp.float32), axis=0))
        total_out = total_out.at[safe_rows].add(table_gates[:, None] * expert_term)
        return (total_out, None)
    moe_term = lax.scan(one_expert, jnp.zeros((TOKENS, D), jnp.float32), (expert_in[:EXPERTS], expert_out[:EXPERTS], row_table.reshape(SLOTS, N_SEQ * CAP)[:EXPERTS], gate_table.reshape(SLOTS, N_SEQ * CAP)[:EXPERTS]))[0]
    mixed_out = (after_attn + shared_factor[:, None] * shared_term + moe_term).astype(jnp.bfloat16)
    return (mixed_out, attn_proj, key_cache)
```

```python
import math

import jax
import jax.numpy as jnp
from jax import lax
from jax.sharding import PartitionSpec as P

HD = 128
TOPK = 4
SLOTS = 64
CAP = 32


rope_base = 1000000.0
neg_fill = -1e30
norm_eps = 1e-06


def token_positions(segment_ids):
    stream_len = segment_ids.shape[0]
    token_index = jnp.arange(stream_len, dtype=jnp.int32)
    boundary = jnp.concatenate([jnp.ones((1,), jnp.bool_), segment_ids[1:] != segment_ids[:-1]])
    seg_start = lax.cummax(jnp.where(boundary, token_index, 0), axis=0)
    return (token_index - seg_start, seg_start)


def rotate(values_in, positions, head_count):
    half_dim = HD // 2
    frequency = rope_base ** (-(2.0 * jnp.arange(half_dim, dtype=jnp.float32)) / HD)
    angle_all = positions.astype(jnp.float32)[:, None] * frequency[None, :]
    cosine = jnp.cos(angle_all)[:, None, :]
    sine_part = jnp.sin(angle_all)[:, None, :]
    shaped = values_in.astype(jnp.float32).reshape(values_in.shape[0], head_count, HD)
    first_half = shaped[..., :half_dim]
    second_half = shaped[..., half_dim:]
    turned = jnp.concatenate(
        [
            first_half * cosine - second_half * sine_part,
            second_half * cosine + first_half * sine_part,
        ],
        axis=-1,
    )
    return turned.reshape(values_in.shape[0], head_count * HD).astype(jnp.bfloat16)


def rms_norm(hidden_in, norm_gain):
    mean_square = jnp.mean(hidden_in * hidden_in, axis=-1, keepdims=True)
    return (hidden_in * lax.rsqrt(mean_square + norm_eps) * norm_gain.astype(jnp.float32)).astype(
        jnp.bfloat16
    )


def expert_parts(incoming, expert_in, expert_out):
    expert_pre = jnp.einsum(
        "nscd,sgde->nscge", incoming, expert_in, preferred_element_type=jnp.float32
    )
    expert_hidden = (jax.nn.silu(expert_pre[..., 0, :]) * expert_pre[..., 1, :]).astype(
        jnp.bfloat16
    )
    return jnp.einsum(
        "nsce,sed->nscd", expert_hidden, expert_out, preferred_element_type=jnp.float32
    ).astype(jnp.bfloat16)


def body(
    segment_ids,
    queries,
    keys,
    values,
    out_weight,
    residual,
    norm_gain,
    shared_in,
    shared_out,
    shared_gate,
    expert_in,
    expert_out,
    expert_ids,
    gate_weights,
):
    seq_count = lax.axis_size("seq")
    exp_count = lax.axis_size("exp")
    seq_place = lax.axis_index("seq")
    exp_place = lax.axis_index("exp")
    block_len = queries.shape[0]
    stream_len = segment_ids.shape[0]
    local_heads = queries.shape[1] // HD
    block_first = seq_place * block_len
    query_seg = lax.dynamic_slice_in_dim(segment_ids, block_first, block_len, 0)
    local_start = jnp.sum((segment_ids[None, :] < query_seg[:, None]).astype(jnp.int32), axis=1)
    local_pos = block_first + jnp.arange(block_len, dtype=jnp.int32) - local_start
    rotated_q = rotate(queries, local_pos, local_heads).reshape(block_len, local_heads, HD)
    key_cache = rotate(keys, local_pos, local_heads)
    score_scale = 1.0 / math.sqrt(HD)
    query_pos = block_first + jnp.arange(block_len, dtype=jnp.int32)

    def attend(state_now, key_rows, value_rows, key_first):
        width_keys = key_rows.shape[0]
        run_max, run_sum, run_acc = state_now
        scores = (
            jnp.einsum(
                "qhd,khd->hqk",
                rotated_q,
                key_rows.reshape(width_keys, local_heads, HD),
                preferred_element_type=jnp.float32,
            )
            * score_scale
        )
        key_pos = key_first + jnp.arange(width_keys, dtype=jnp.int32)
        key_seg = lax.dynamic_slice_in_dim(
            segment_ids, jnp.clip(key_first, 0, stream_len - width_keys), width_keys, 0
        )
        visible = (
            True
            & (key_pos[None, :] <= query_pos[:, None])
            & (key_seg[None, :] == query_seg[:, None])
        )
        new_max = jnp.maximum(run_max, jnp.max(jnp.where(visible[None], scores, neg_fill), axis=-1))
        weights_f = jnp.where(visible[None], jnp.exp(scores - new_max[..., None]), 0.0)
        rescale = jnp.exp(run_max - new_max)
        weights_b = weights_f.astype(jnp.bfloat16)
        gathered = jnp.einsum(
            "hqk,khd->hqd",
            weights_b,
            value_rows.reshape(width_keys, local_heads, HD),
            preferred_element_type=jnp.float32,
        )
        return (
            new_max,
            run_sum * rescale + jnp.sum(weights_f, axis=-1),
            run_acc * rescale[..., None] + gathered,
        )

    init_state = (
        jnp.full((local_heads, block_len), neg_fill, jnp.float32),
        jnp.zeros((local_heads, block_len), jnp.float32),
        jnp.zeros((local_heads, block_len, HD), jnp.float32),
    )
    pieces = (
        lax.all_gather(key_cache, "seq", axis=0, tiled=True),
        lax.all_gather(values, "seq", axis=0, tiled=True),
    )
    piece_len = pieces[0].shape[0]
    step_len = math.gcd(piece_len, 512)

    def inner_step(step_id, state_in):
        row_start = step_id * step_len
        key_rows = lax.dynamic_slice_in_dim(pieces[0], row_start, step_len, 0)
        value_rows = lax.dynamic_slice_in_dim(pieces[1], row_start, step_len, 0)
        return attend(state_in, key_rows, value_rows, row_start)

    first_chunk = local_start[0] // step_len
    end_chunk = (block_first + block_len + step_len - 1) // step_len
    final_state = lax.fori_loop(first_chunk, end_chunk, inner_step, init_state)
    run_max, run_sum, run_acc = final_state
    attended = (
        (run_acc / run_sum[..., None])
        .transpose(1, 0, 2)
        .reshape(block_len, local_heads * HD)
        .astype(jnp.bfloat16)
    )
    attn_part = jnp.dot(attended, out_weight, preferred_element_type=jnp.float32)
    row_count = block_len // exp_count
    row_first = exp_place * row_count
    residual_f = residual.astype(jnp.float32)
    attn_sum = lax.psum(attn_part.astype(jnp.bfloat16), "exp").astype(jnp.float32)
    after_attn = residual_f + attn_sum
    normed = rms_norm(after_attn, norm_gain)
    attn_rows = lax.dynamic_slice_in_dim(attn_sum, row_first, row_count, 0).astype(jnp.bfloat16)
    after_rows = lax.dynamic_slice_in_dim(after_attn, row_first, row_count, 0)
    shared_pre = jnp.einsum("td,gde->tge", normed, shared_in, preferred_element_type=jnp.float32)
    shared_hidden = (jax.nn.silu(shared_pre[:, 0]) * shared_pre[:, 1]).astype(jnp.bfloat16)
    shared_term = jnp.dot(shared_hidden, shared_out, preferred_element_type=jnp.float32)
    shared_factor = jax.nn.sigmoid(jnp.dot(normed, shared_gate, preferred_element_type=jnp.float32))
    flat_ids = expert_ids.reshape(-1)
    one_hot = (flat_ids[:, None] == jnp.arange(SLOTS, dtype=jnp.int32)[None, :]).astype(jnp.int32)
    slot_rank = jnp.sum(jnp.cumsum(one_hot, axis=0) * one_hot, axis=1) - 1
    slot_place = flat_ids * CAP + slot_rank
    owner_row = jnp.arange(flat_ids.shape[0], dtype=jnp.int32) // TOPK
    source_row = jnp.full((SLOTS * CAP,), -1, jnp.int32).at[slot_place].set(owner_row)
    slot_local = SLOTS // seq_count
    model_width = normed.shape[1]
    outgoing = jnp.where(
        (source_row >= 0)[:, None], normed[jnp.maximum(source_row, 0)], jnp.zeros((), jnp.bfloat16)
    ).reshape(seq_count, slot_local, CAP, model_width)
    col_count = model_width // exp_count
    col_first = exp_place * col_count
    outgoing_part = lax.dynamic_slice_in_dim(outgoing, col_first, col_count, 3)
    incoming = lax.all_gather(
        lax.all_to_all(outgoing_part, "seq", split_axis=0, concat_axis=0, tiled=True),
        "exp",
        axis=3,
        tiled=True,
    )
    expert_part = expert_parts(incoming, expert_in, expert_out)
    summed = lax.psum_scatter(
        expert_part.astype(jnp.float32).astype(jnp.bfloat16), "exp", scatter_dimension=3, tiled=True
    ).astype(jnp.float32)
    returned = lax.all_to_all(
        summed.astype(jnp.bfloat16), "seq", split_axis=0, concat_axis=0, tiled=True
    ).astype(summed.dtype)
    picked = returned.reshape(SLOTS * CAP, col_count)[slot_place].reshape(
        block_len, TOPK, col_count
    )
    moe_cols = jnp.sum(gate_weights[:, :, None] * picked, axis=1)
    moe_term = lax.dynamic_update_slice_in_dim(
        jnp.zeros((block_len, model_width), jnp.float32), moe_cols, col_first, 1
    )
    combined = shared_factor[:, None] * shared_term + moe_term
    moe_rows = lax.psum_scatter(
        combined.astype(jnp.bfloat16), "exp", scatter_dimension=0, tiled=True
    ).astype(jnp.float32)
    mixed_out = (after_rows + moe_rows).astype(jnp.bfloat16)
    return (mixed_out, attn_rows, key_cache)


def solution(mesh):
    return jax.shard_map(
        body,
        mesh=mesh,
        in_specs=(
            P(),
            P("seq", "exp"),
            P("seq", "exp"),
            P("seq", "exp"),
            P("exp", None),
            P("seq", None),
            P(),
            P(None, None, "exp"),
            P("exp", None),
            P(),
            P("seq", None, None, "exp"),
            P("seq", "exp", None),
            P("seq", None),
            P("seq", None),
        ),
        out_specs=(P(("seq", "exp"), None), P(("seq", "exp"), None), P("seq", "exp")),
        check_vma=False,
    )
```

```python
import math

import jax
import jax.numpy as jnp
from jax import lax
from jax.sharding import Mesh, PartitionSpec as P
from jax.experimental import pallas as pl
from jax.experimental.pallas import tpu as pltpu

HD = 128
HEADS = 16
TOPK = 4
SLOTS = 64
CAP = 32


rope_base = 1000000.0
neg_fill = -1e30
norm_eps = 1e-06


KEY_TILE = 512


def flash_kernel(bounds_ref, q_ref, k_ref, v_ref, qseg_ref, kseg_ref, o_ref, m_sc, l_sc, acc_sc):
    step = pl.program_id(0)
    first_chunk = bounds_ref[0]
    end_chunk = bounds_ref[1]
    query_first = bounds_ref[2]
    chunk = first_chunk + step
    rows = q_ref.shape[0]
    heads = q_ref.shape[1] // HD

    @pl.when(step == 0)
    def _():
        m_sc[...] = jnp.full(m_sc.shape, neg_fill, jnp.float32)
        l_sc[...] = jnp.zeros(l_sc.shape, jnp.float32)
        acc_sc[...] = jnp.zeros(acc_sc.shape, jnp.float32)

    @pl.when(chunk < end_chunk)
    def _():
        key_pos = chunk * KEY_TILE + lax.broadcasted_iota(jnp.int32, (1, KEY_TILE), 1)
        query_pos = query_first + lax.broadcasted_iota(jnp.int32, (rows, 1), 0)
        visible = (key_pos <= query_pos) & (kseg_ref[...] == qseg_ref[...])
        score_scale = 1.0 / math.sqrt(HD)
        for h in range(heads):
            cols = slice(h * HD, (h + 1) * HD)
            scores = (
                lax.dot_general(
                    q_ref[:, cols], k_ref[:, cols], (((1,), (1,)), ((), ())),
                    preferred_element_type=jnp.float32,
                )
                * score_scale
            )
            m_old = m_sc[h]
            m_new = jnp.maximum(
                m_old, jnp.max(jnp.where(visible, scores, neg_fill), axis=1, keepdims=True)
            )
            weights_f = jnp.where(visible, jnp.exp(scores - m_new), 0.0)
            rescale = jnp.exp(m_old - m_new)
            l_sc[h] = l_sc[h] * rescale + jnp.sum(weights_f, axis=1, keepdims=True)
            acc_sc[h] = acc_sc[h] * rescale + jnp.dot(
                weights_f.astype(jnp.bfloat16), v_ref[:, cols], preferred_element_type=jnp.float32
            )
            m_sc[h] = m_new

    @pl.when(step == pl.num_programs(0) - 1)
    def _():
        for h in range(heads):
            o_ref[:, h * HD:(h + 1) * HD] = (acc_sc[h] / l_sc[h]).astype(o_ref.dtype)


def flash_attention(rotated_q, key_all, value_all, query_seg, segment_ids, query_first, seg_first):
    rows, width = rotated_q.shape
    heads = width // HD
    key_count = key_all.shape[0]
    chunks = key_count // KEY_TILE
    first_chunk = seg_first // KEY_TILE
    end_chunk = (query_first + rows + KEY_TILE - 1) // KEY_TILE
    bounds = jnp.stack([first_chunk, end_chunk, query_first]).astype(jnp.int32)

    def kv_map(c, b):
        return (jnp.minimum(b[0] + c, b[1] - 1), 0)

    def kseg_map(c, b):
        return (0, jnp.minimum(b[0] + c, b[1] - 1))

    grid_spec = pltpu.PrefetchScalarGridSpec(
        num_scalar_prefetch=1,
        grid=(chunks,),
        in_specs=[
            pl.BlockSpec((rows, width), lambda c, b: (0, 0)),
            pl.BlockSpec((KEY_TILE, width), kv_map),
            pl.BlockSpec((KEY_TILE, width), kv_map),
            pl.BlockSpec((rows, 1), lambda c, b: (0, 0)),
            pl.BlockSpec((1, KEY_TILE), kseg_map),
        ],
        out_specs=pl.BlockSpec((rows, width), lambda c, b: (0, 0)),
        scratch_shapes=[
            pltpu.VMEM((heads, rows, 1), jnp.float32),
            pltpu.VMEM((heads, rows, 1), jnp.float32),
            pltpu.VMEM((heads, rows, HD), jnp.float32),
        ],
    )
    flops = 4 * rows * key_count * width
    return pl.pallas_call(
        flash_kernel,
        grid_spec=grid_spec,
        out_shape=jax.ShapeDtypeStruct((rows, width), jnp.bfloat16),
        compiler_params=pltpu.CompilerParams(
            dimension_semantics=("arbitrary",), vmem_limit_bytes=48 * 1024 * 1024
        ),
        cost_estimate=pl.CostEstimate(
            flops=flops,
            transcendentals=rows * key_count * heads,
            bytes_accessed=2 * key_count * width * 2 + 2 * rows * width * 2,
        ),
    )(
        bounds,
        rotated_q,
        key_all,
        value_all,
        query_seg.reshape(rows, 1).astype(jnp.int32),
        segment_ids.reshape(1, key_count).astype(jnp.int32),
    )


def token_positions(segment_ids):
    stream_len = segment_ids.shape[0]
    token_index = jnp.arange(stream_len, dtype=jnp.int32)
    boundary = jnp.concatenate([jnp.ones((1,), jnp.bool_), segment_ids[1:] != segment_ids[:-1]])
    seg_start = lax.cummax(jnp.where(boundary, token_index, 0), axis=0)
    return (token_index - seg_start, seg_start)


def rotate(values_in, positions, head_count):
    half_dim = HD // 2
    frequency = rope_base ** (-(2.0 * jnp.arange(half_dim, dtype=jnp.float32)) / HD)
    angle_all = positions.astype(jnp.float32)[:, None] * frequency[None, :]
    cosine = jnp.cos(angle_all)[:, None, :]
    sine_part = jnp.sin(angle_all)[:, None, :]
    shaped = values_in.astype(jnp.float32).reshape(values_in.shape[0], head_count, HD)
    first_half = shaped[..., :half_dim]
    second_half = shaped[..., half_dim:]
    turned = jnp.concatenate(
        [
            first_half * cosine - second_half * sine_part,
            second_half * cosine + first_half * sine_part,
        ],
        axis=-1,
    )
    return turned.reshape(values_in.shape[0], head_count * HD).astype(jnp.bfloat16)


def rms_norm(hidden_in, norm_gain):
    mean_square = jnp.mean(hidden_in * hidden_in, axis=-1, keepdims=True)
    return (hidden_in * lax.rsqrt(mean_square + norm_eps) * norm_gain.astype(jnp.float32)).astype(
        jnp.bfloat16
    )


def expert_parts(incoming, expert_in, expert_out):
    expert_pre = jnp.einsum(
        "nscd,sgde->nscge", incoming, expert_in, preferred_element_type=jnp.float32
    )
    expert_hidden = (jax.nn.silu(expert_pre[..., 0, :]) * expert_pre[..., 1, :]).astype(
        jnp.bfloat16
    )
    return jnp.einsum(
        "nsce,sed->nscd", expert_hidden, expert_out, preferred_element_type=jnp.float32
    ).astype(jnp.bfloat16)


def body(
    segment_ids,
    queries,
    keys,
    values,
    out_weight,
    residual,
    norm_gain,
    shared_in,
    shared_out,
    shared_gate,
    expert_in,
    expert_out,
    expert_ids,
    gate_weights,
):
    seq_count = lax.axis_size("sh") * lax.axis_size("sl")
    exp_count = lax.axis_size("exp")
    group_place = lax.axis_index("sh")
    sub_count = lax.axis_size("sl")
    seq_place = group_place * sub_count + lax.axis_index("sl")
    exp_place = lax.axis_index("exp")
    block_len = queries.shape[0]
    local_heads = queries.shape[1] // HD
    block_first = seq_place * block_len
    query_seg = lax.dynamic_slice_in_dim(segment_ids, block_first, block_len, 0)
    local_start = jnp.sum((segment_ids[None, :] < query_seg[:, None]).astype(jnp.int32), axis=1)
    local_pos = block_first + jnp.arange(block_len, dtype=jnp.int32) - local_start
    rotated_q = rotate(queries, local_pos, local_heads)
    key_cache = rotate(keys, local_pos, local_heads)
    stacked = jnp.stack([rotated_q, key_cache, values]).reshape(3, block_len, local_heads, HD)
    moved = lax.all_to_all(stacked, "sl", split_axis=2, concat_axis=1, tiled=True)
    span = block_len * sub_count
    head_q = moved[0].reshape(span, HD)
    head_kv = moved[1:].reshape(2, span, HD)
    gathered = lax.all_gather(head_kv, "sh", axis=1, tiled=True)
    span_first = group_place * span
    span_seg = lax.dynamic_slice_in_dim(segment_ids, span_first, span, 0)
    seg_first = jnp.sum((segment_ids < span_seg[0]).astype(jnp.int32))
    head_out = flash_attention(
        head_q, gathered[0], gathered[1], span_seg, segment_ids, span_first, seg_first
    )
    attended = lax.all_to_all(
        head_out.reshape(sub_count, block_len, 1, HD), "sl", split_axis=0, concat_axis=2, tiled=True
    ).reshape(block_len, local_heads * HD)
    attn_part = jnp.dot(attended, out_weight, preferred_element_type=jnp.float32)
    row_count = block_len // exp_count
    row_first = exp_place * row_count
    residual_f = residual.astype(jnp.float32)
    attn_sum = lax.psum(attn_part.astype(jnp.bfloat16), "exp").astype(jnp.float32)
    after_attn = residual_f + attn_sum
    normed = rms_norm(after_attn, norm_gain)
    attn_rows = lax.dynamic_slice_in_dim(attn_sum, row_first, row_count, 0).astype(jnp.bfloat16)
    after_rows = lax.dynamic_slice_in_dim(after_attn, row_first, row_count, 0)
    shared_pre = jnp.einsum("td,gde->tge", normed, shared_in, preferred_element_type=jnp.float32)
    shared_hidden = (jax.nn.silu(shared_pre[:, 0]) * shared_pre[:, 1]).astype(jnp.bfloat16)
    shared_term = jnp.dot(shared_hidden, shared_out, preferred_element_type=jnp.float32)
    shared_factor = jax.nn.sigmoid(jnp.dot(normed, shared_gate, preferred_element_type=jnp.float32))
    flat_ids = expert_ids.reshape(-1)
    one_hot = (flat_ids[:, None] == jnp.arange(SLOTS, dtype=jnp.int32)[None, :]).astype(jnp.int32)
    slot_rank = jnp.sum(jnp.cumsum(one_hot, axis=0) * one_hot, axis=1) - 1
    slot_place = flat_ids * CAP + slot_rank
    owner_row = jnp.arange(flat_ids.shape[0], dtype=jnp.int32) // TOPK
    source_row = jnp.full((SLOTS * CAP,), -1, jnp.int32).at[slot_place].set(owner_row)
    slot_local = SLOTS // seq_count
    model_width = normed.shape[1]
    outgoing = jnp.where(
        (source_row >= 0)[:, None], normed[jnp.maximum(source_row, 0)], jnp.zeros((), jnp.bfloat16)
    ).reshape(seq_count, slot_local, CAP, model_width)
    col_count = model_width // exp_count
    col_first = exp_place * col_count
    outgoing_part = lax.dynamic_slice_in_dim(outgoing, col_first, col_count, 3)
    incoming = lax.all_gather(
        lax.all_to_all(outgoing_part, SEQ, split_axis=0, concat_axis=0, tiled=True),
        "exp",
        axis=3,
        tiled=True,
    )
    expert_part = expert_parts(incoming, expert_in, expert_out)
    summed = lax.psum_scatter(
        expert_part.astype(jnp.float32).astype(jnp.bfloat16), "exp", scatter_dimension=3, tiled=True
    ).astype(jnp.float32)
    returned = lax.all_to_all(
        summed.astype(jnp.bfloat16), SEQ, split_axis=0, concat_axis=0, tiled=True
    ).astype(summed.dtype)
    picked = returned.reshape(SLOTS * CAP, col_count)[slot_place].reshape(
        block_len, TOPK, col_count
    )
    moe_cols = jnp.sum(gate_weights[:, :, None] * picked, axis=1)
    moe_term = lax.dynamic_update_slice_in_dim(
        jnp.zeros((block_len, model_width), jnp.float32), moe_cols, col_first, 1
    )
    combined = shared_factor[:, None] * shared_term + moe_term
    moe_rows = lax.psum_scatter(
        combined.astype(jnp.bfloat16), "exp", scatter_dimension=0, tiled=True
    ).astype(jnp.float32)
    mixed_out = (after_rows + moe_rows).astype(jnp.bfloat16)
    return (mixed_out, attn_rows, key_cache)


SEQ = ("sh", "sl")


def solution(mesh):
    exp_count = mesh.shape["exp"]
    seq_count = mesh.shape["seq"]
    sub_count = HEADS // exp_count
    grid = mesh.devices.reshape(seq_count // sub_count, sub_count, exp_count)
    split_mesh = Mesh(grid, ("sh", "sl", "exp"))
    return jax.shard_map(
        body,
        mesh=split_mesh,
        in_specs=(
            P(),
            P(SEQ, "exp"),
            P(SEQ, "exp"),
            P(SEQ, "exp"),
            P("exp", None),
            P(SEQ, None),
            P(),
            P(None, None, "exp"),
            P("exp", None),
            P(),
            P(SEQ, None, None, "exp"),
            P(SEQ, "exp", None),
            P(SEQ, None),
            P(SEQ, None),
        ),
        out_specs=(P(("sh", "sl", "exp"), None), P(("sh", "sl", "exp"), None), P(SEQ, "exp")),
        check_vma=False,
    )
```

```python
import math

import jax
import jax.numpy as jnp
from jax import lax
from jax.sharding import Mesh, PartitionSpec as P
from jax.experimental import pallas as pl
from jax.experimental.pallas import tpu as pltpu

HD = 128
HEADS = 16
TOPK = 4
SLOTS = 64
CAP = 32


rope_base = 1000000.0
neg_fill = -1e30
norm_eps = 1e-06


KEY_TILE = 512


def flash_kernel(bounds_ref, q_ref, k_ref, v_ref, qseg_ref, kseg_ref, o_ref, m_sc, l_sc, acc_sc):
    step = pl.program_id(0)
    first_chunk = bounds_ref[0]
    end_chunk = bounds_ref[1]
    query_first = bounds_ref[2]
    chunk = first_chunk + step
    rows = q_ref.shape[0]
    heads = q_ref.shape[1] // HD

    @pl.when(step == 0)
    def _():
        m_sc[...] = jnp.full(m_sc.shape, neg_fill, jnp.float32)
        l_sc[...] = jnp.zeros(l_sc.shape, jnp.float32)
        acc_sc[...] = jnp.zeros(acc_sc.shape, jnp.float32)

    @pl.when(chunk < end_chunk)
    def _():
        key_pos = chunk * KEY_TILE + lax.broadcasted_iota(jnp.int32, (1, KEY_TILE), 1)
        query_pos = query_first + lax.broadcasted_iota(jnp.int32, (rows, 1), 0)
        visible = (key_pos <= query_pos) & (kseg_ref[...] == qseg_ref[...])
        score_scale = 1.0 / math.sqrt(HD)
        for h in range(heads):
            cols = slice(h * HD, (h + 1) * HD)
            scores = (
                lax.dot_general(
                    q_ref[:, cols], k_ref[:, cols], (((1,), (1,)), ((), ())),
                    preferred_element_type=jnp.float32,
                )
                * score_scale
            )
            m_old = m_sc[h]
            m_new = jnp.maximum(
                m_old, jnp.max(jnp.where(visible, scores, neg_fill), axis=1, keepdims=True)
            )
            weights_f = jnp.where(visible, jnp.exp(scores - m_new), 0.0)
            rescale = jnp.exp(m_old - m_new)
            l_sc[h] = l_sc[h] * rescale + jnp.sum(weights_f, axis=1, keepdims=True)
            acc_sc[h] = acc_sc[h] * rescale + jnp.dot(
                weights_f.astype(jnp.bfloat16), v_ref[:, cols], preferred_element_type=jnp.float32
            )
            m_sc[h] = m_new

    @pl.when(step == pl.num_programs(0) - 1)
    def _():
        for h in range(heads):
            o_ref[:, h * HD:(h + 1) * HD] = (acc_sc[h] / l_sc[h]).astype(o_ref.dtype)


def flash_attention(rotated_q, key_all, value_all, query_seg, segment_ids, query_first, seg_first):
    rows, width = rotated_q.shape
    heads = width // HD
    key_count = key_all.shape[0]
    chunks = key_count // KEY_TILE
    first_chunk = seg_first // KEY_TILE
    end_chunk = (query_first + rows + KEY_TILE - 1) // KEY_TILE
    bounds = jnp.stack([first_chunk, end_chunk, query_first]).astype(jnp.int32)

    def kv_map(c, b):
        return (jnp.minimum(b[0] + c, b[1] - 1), 0)

    def kseg_map(c, b):
        return (0, jnp.minimum(b[0] + c, b[1] - 1))

    grid_spec = pltpu.PrefetchScalarGridSpec(
        num_scalar_prefetch=1,
        grid=(chunks,),
        in_specs=[
            pl.BlockSpec((rows, width), lambda c, b: (0, 0)),
            pl.BlockSpec((KEY_TILE, width), kv_map),
            pl.BlockSpec((KEY_TILE, width), kv_map),
            pl.BlockSpec((rows, 1), lambda c, b: (0, 0)),
            pl.BlockSpec((1, KEY_TILE), kseg_map),
        ],
        out_specs=pl.BlockSpec((rows, width), lambda c, b: (0, 0)),
        scratch_shapes=[
            pltpu.VMEM((heads, rows, 1), jnp.float32),
            pltpu.VMEM((heads, rows, 1), jnp.float32),
            pltpu.VMEM((heads, rows, HD), jnp.float32),
        ],
    )
    flops = 4 * rows * key_count * width
    return pl.pallas_call(
        flash_kernel,
        grid_spec=grid_spec,
        out_shape=jax.ShapeDtypeStruct((rows, width), jnp.bfloat16),
        compiler_params=pltpu.CompilerParams(
            dimension_semantics=("arbitrary",), vmem_limit_bytes=48 * 1024 * 1024
        ),
        cost_estimate=pl.CostEstimate(
            flops=flops,
            transcendentals=rows * key_count * heads,
            bytes_accessed=2 * key_count * width * 2 + 2 * rows * width * 2,
        ),
    )(
        bounds,
        rotated_q,
        key_all,
        value_all,
        query_seg.reshape(rows, 1).astype(jnp.int32),
        segment_ids.reshape(1, key_count).astype(jnp.int32),
    )


def token_positions(segment_ids):
    stream_len = segment_ids.shape[0]
    token_index = jnp.arange(stream_len, dtype=jnp.int32)
    boundary = jnp.concatenate([jnp.ones((1,), jnp.bool_), segment_ids[1:] != segment_ids[:-1]])
    seg_start = lax.cummax(jnp.where(boundary, token_index, 0), axis=0)
    return (token_index - seg_start, seg_start)


def rotate(values_in, positions, head_count):
    half_dim = HD // 2
    frequency = rope_base ** (-(2.0 * jnp.arange(half_dim, dtype=jnp.float32)) / HD)
    angle_all = positions.astype(jnp.float32)[:, None] * frequency[None, :]
    cosine = jnp.cos(angle_all)[:, None, :]
    sine_part = jnp.sin(angle_all)[:, None, :]
    shaped = values_in.astype(jnp.float32).reshape(values_in.shape[0], head_count, HD)
    first_half = shaped[..., :half_dim]
    second_half = shaped[..., half_dim:]
    turned = jnp.concatenate(
        [
            first_half * cosine - second_half * sine_part,
            second_half * cosine + first_half * sine_part,
        ],
        axis=-1,
    )
    return turned.reshape(values_in.shape[0], head_count * HD).astype(jnp.bfloat16)


def rms_norm(hidden_in, norm_gain):
    mean_square = jnp.mean(hidden_in * hidden_in, axis=-1, keepdims=True)
    return (hidden_in * lax.rsqrt(mean_square + norm_eps) * norm_gain.astype(jnp.float32)).astype(
        jnp.bfloat16
    )


def expert_parts(incoming, expert_in, expert_out):
    expert_pre = jnp.einsum(
        "nscd,sgde->nscge", incoming, expert_in, preferred_element_type=jnp.float32
    )
    expert_hidden = (jax.nn.silu(expert_pre[..., 0, :]) * expert_pre[..., 1, :]).astype(
        jnp.bfloat16
    )
    return jnp.einsum(
        "nsce,sed->nscd", expert_hidden, expert_out, preferred_element_type=jnp.float32
    ).astype(jnp.bfloat16)


def body(
    segment_ids,
    queries,
    keys,
    values,
    out_weight,
    residual,
    norm_gain,
    shared_in,
    shared_out,
    shared_gate,
    expert_in,
    expert_out,
    expert_ids,
    gate_weights,
):
    seq_count = lax.axis_size("sh") * lax.axis_size("sl")
    exp_count = lax.axis_size("zl") * lax.axis_size("co")
    group_place = lax.axis_index("sh")
    sub_count = lax.axis_size("sl")
    seq_place = group_place * sub_count + lax.axis_index("sl")
    exp_place = lax.axis_index("zl") * lax.axis_size("co") + lax.axis_index("co")
    quarter_place = lax.axis_index("co") * lax.axis_size("zl") + lax.axis_index("zl")
    block_len = queries.shape[0]
    local_heads = queries.shape[1] // HD
    block_first = seq_place * block_len
    query_seg = lax.dynamic_slice_in_dim(segment_ids, block_first, block_len, 0)
    local_start = jnp.sum((segment_ids[None, :] < query_seg[:, None]).astype(jnp.int32), axis=1)
    local_pos = block_first + jnp.arange(block_len, dtype=jnp.int32) - local_start
    rotated_q = rotate(queries, local_pos, local_heads)
    key_cache = rotate(keys, local_pos, local_heads)
    stacked = jnp.stack([rotated_q, key_cache, values]).reshape(3, block_len, local_heads, HD)
    moved = lax.all_to_all(stacked, "sl", split_axis=2, concat_axis=1, tiled=True)
    span = block_len * sub_count
    head_q = moved[0].reshape(span, HD)
    head_kv = moved[1:].reshape(2, span, HD)
    gathered = lax.all_gather(head_kv, "sh", axis=1, tiled=True)
    span_first = group_place * span
    span_seg = lax.dynamic_slice_in_dim(segment_ids, span_first, span, 0)
    seg_first = jnp.sum((segment_ids < span_seg[0]).astype(jnp.int32))
    head_out = flash_attention(
        head_q, gathered[0], gathered[1], span_seg, segment_ids, span_first, seg_first
    )
    attended = lax.all_to_all(
        head_out.reshape(sub_count, block_len, 1, HD), "sl", split_axis=0, concat_axis=2, tiled=True
    ).reshape(block_len, local_heads * HD)
    attn_part = jnp.dot(attended, out_weight, preferred_element_type=jnp.float32)
    row_count = block_len // exp_count
    row_first = exp_place * row_count
    residual_f = residual.astype(jnp.float32)
    attn_sum = lax.psum(lax.psum(attn_part.astype(jnp.bfloat16), "co"), "zl").astype(jnp.float32)
    after_attn = residual_f + attn_sum
    normed = rms_norm(after_attn, norm_gain)
    attn_rows = lax.dynamic_slice_in_dim(attn_sum, row_first, row_count, 0).astype(jnp.bfloat16)
    after_rows = lax.dynamic_slice_in_dim(after_attn, row_first, row_count, 0)
    shared_pre = jnp.einsum("td,gde->tge", normed, shared_in, preferred_element_type=jnp.float32)
    shared_hidden = (jax.nn.silu(shared_pre[:, 0]) * shared_pre[:, 1]).astype(jnp.bfloat16)
    shared_term = jnp.dot(shared_hidden, shared_out, preferred_element_type=jnp.float32)
    shared_factor = jax.nn.sigmoid(jnp.dot(normed, shared_gate, preferred_element_type=jnp.float32))
    flat_ids = expert_ids.reshape(-1)
    flat_index = jnp.arange(flat_ids.shape[0], dtype=jnp.int32)
    earlier_same = (flat_ids[None, :] == flat_ids[:, None]) & (flat_index[None, :] < flat_index[:, None])
    slot_rank = jnp.sum(earlier_same.astype(jnp.int32), axis=1)
    slot_place = flat_ids * CAP + slot_rank
    owner_row = jnp.arange(flat_ids.shape[0], dtype=jnp.int32) // TOPK
    source_row = jnp.full((SLOTS * CAP,), -1, jnp.int32).at[slot_place].set(owner_row)
    slot_local = SLOTS // seq_count
    model_width = normed.shape[1]
    outgoing = jnp.where(
        (source_row >= 0)[:, None], normed[jnp.maximum(source_row, 0)], jnp.zeros((), jnp.bfloat16)
    ).reshape(seq_count, slot_local, CAP, model_width)
    col_count = model_width // exp_count
    col_first = quarter_place * col_count
    outgoing_part = lax.dynamic_slice_in_dim(outgoing, col_first, col_count, 3)
    incoming = lax.all_gather(
        lax.all_gather(
            lax.all_to_all(outgoing_part, SEQ, split_axis=0, concat_axis=0, tiled=True),
            "zl",
            axis=3,
            tiled=True,
        ),
        "co",
        axis=3,
        tiled=True,
    )
    expert_part = expert_parts(incoming, expert_in, expert_out)
    summed = lax.psum_scatter(
        lax.psum_scatter(expert_part, "co", scatter_dimension=3, tiled=True),
        "zl",
        scatter_dimension=3,
        tiled=True,
    ).astype(jnp.float32)
    returned = lax.all_to_all(
        summed.astype(jnp.bfloat16), SEQ, split_axis=0, concat_axis=0, tiled=True
    ).astype(summed.dtype)
    picked = returned.reshape(SLOTS * CAP, col_count)[slot_place].reshape(
        block_len, TOPK, col_count
    )
    moe_cols = jnp.sum(gate_weights[:, :, None] * picked, axis=1)
    moe_term = lax.dynamic_update_slice_in_dim(
        jnp.zeros((block_len, model_width), jnp.float32), moe_cols, col_first, 1
    )
    combined = shared_factor[:, None] * shared_term + moe_term
    moe_rows = lax.psum_scatter(
        combined.astype(jnp.bfloat16), EXP, scatter_dimension=0, tiled=True
    ).astype(jnp.float32)
    mixed_out = (after_rows + moe_rows).astype(jnp.bfloat16)
    return (mixed_out, attn_rows, key_cache)


SEQ = ("sh", "sl")
EXP = ("zl", "co")


def solution(mesh):
    exp_count = mesh.shape["exp"]
    seq_count = mesh.shape["seq"]
    sub_count = HEADS // exp_count
    grid = mesh.devices.reshape(seq_count // sub_count, sub_count, exp_count // 2, 2)
    split_mesh = Mesh(grid, ("sh", "sl", "zl", "co"))
    return jax.shard_map(
        body,
        mesh=split_mesh,
        in_specs=(
            P(),
            P(SEQ, EXP),
            P(SEQ, EXP),
            P(SEQ, EXP),
            P(EXP, None),
            P(SEQ, None),
            P(),
            P(None, None, EXP),
            P(EXP, None),
            P(),
            P(SEQ, None, None, EXP),
            P(SEQ, EXP, None),
            P(SEQ, None),
            P(SEQ, None),
        ),
        out_specs=(P(("sh", "sl", "zl", "co"), None), P(("sh", "sl", "zl", "co"), None), P(SEQ, EXP)),
        check_vma=False,
    )
```

```python
import math

import jax
import jax.numpy as jnp
from jax import lax
from jax.sharding import Mesh, PartitionSpec as P
from jax.experimental import pallas as pl
from jax.experimental.pallas import tpu as pltpu

HD = 128
HEADS = 16
TOPK = 4
SLOTS = 64
CAP = 32


rope_base = 1000000.0
neg_fill = -1e30
norm_eps = 1e-06


KEY_TILE = 512


def flash_kernel(bounds_ref, q_ref, k_ref, v_ref, qseg_ref, kseg_ref, o_ref, m_sc, l_sc, acc_sc):
    step = pl.program_id(0)
    first_chunk = bounds_ref[0]
    end_chunk = bounds_ref[1]
    query_first = bounds_ref[2]
    chunk = first_chunk + step
    rows = q_ref.shape[0]
    heads = q_ref.shape[1] // HD

    @pl.when(step == 0)
    def _():
        m_sc[...] = jnp.full(m_sc.shape, neg_fill, jnp.float32)
        l_sc[...] = jnp.zeros(l_sc.shape, jnp.float32)
        acc_sc[...] = jnp.zeros(acc_sc.shape, jnp.float32)

    @pl.when(chunk < end_chunk)
    def _():
        key_pos = chunk * KEY_TILE + lax.broadcasted_iota(jnp.int32, (1, KEY_TILE), 1)
        query_pos = query_first + lax.broadcasted_iota(jnp.int32, (rows, 1), 0)
        visible = (key_pos <= query_pos) & (kseg_ref[...] == qseg_ref[...])
        score_scale = 1.0 / math.sqrt(HD)
        for h in range(heads):
            cols = slice(h * HD, (h + 1) * HD)
            scores = (
                lax.dot_general(
                    q_ref[:, cols], k_ref[:, cols], (((1,), (1,)), ((), ())),
                    preferred_element_type=jnp.float32,
                )
                * score_scale
            )
            m_old = m_sc[h]
            m_new = jnp.maximum(
                m_old, jnp.max(jnp.where(visible, scores, neg_fill), axis=1, keepdims=True)
            )
            weights_f = jnp.where(visible, jnp.exp(scores - m_new), 0.0)
            rescale = jnp.exp(m_old - m_new)
            l_sc[h] = l_sc[h] * rescale + jnp.sum(weights_f, axis=1, keepdims=True)
            acc_sc[h] = acc_sc[h] * rescale + jnp.dot(
                weights_f.astype(jnp.bfloat16), v_ref[:, cols], preferred_element_type=jnp.float32
            )
            m_sc[h] = m_new

    @pl.when(step == pl.num_programs(0) - 1)
    def _():
        for h in range(heads):
            o_ref[:, h * HD:(h + 1) * HD] = (acc_sc[h] / l_sc[h]).astype(o_ref.dtype)


def flash_attention(rotated_q, key_all, value_all, query_seg, segment_ids, query_first, seg_first):
    rows, width = rotated_q.shape
    heads = width // HD
    key_count = key_all.shape[0]
    chunks = key_count // KEY_TILE
    first_chunk = seg_first // KEY_TILE
    end_chunk = (query_first + rows + KEY_TILE - 1) // KEY_TILE
    bounds = jnp.stack([first_chunk, end_chunk, query_first]).astype(jnp.int32)

    def kv_map(c, b):
        return (jnp.minimum(b[0] + c, b[1] - 1), 0)

    def kseg_map(c, b):
        return (0, jnp.minimum(b[0] + c, b[1] - 1))

    grid_spec = pltpu.PrefetchScalarGridSpec(
        num_scalar_prefetch=1,
        grid=(chunks,),
        in_specs=[
            pl.BlockSpec((rows, width), lambda c, b: (0, 0)),
            pl.BlockSpec((KEY_TILE, width), kv_map),
            pl.BlockSpec((KEY_TILE, width), kv_map),
            pl.BlockSpec((rows, 1), lambda c, b: (0, 0)),
            pl.BlockSpec((1, KEY_TILE), kseg_map),
        ],
        out_specs=pl.BlockSpec((rows, width), lambda c, b: (0, 0)),
        scratch_shapes=[
            pltpu.VMEM((heads, rows, 1), jnp.float32),
            pltpu.VMEM((heads, rows, 1), jnp.float32),
            pltpu.VMEM((heads, rows, HD), jnp.float32),
        ],
    )
    flops = 4 * rows * key_count * width
    return pl.pallas_call(
        flash_kernel,
        grid_spec=grid_spec,
        out_shape=jax.ShapeDtypeStruct((rows, width), jnp.bfloat16),
        compiler_params=pltpu.CompilerParams(
            dimension_semantics=("arbitrary",), vmem_limit_bytes=48 * 1024 * 1024
        ),
        cost_estimate=pl.CostEstimate(
            flops=flops,
            transcendentals=rows * key_count * heads,
            bytes_accessed=2 * key_count * width * 2 + 2 * rows * width * 2,
        ),
    )(
        bounds,
        rotated_q,
        key_all,
        value_all,
        query_seg.reshape(rows, 1).astype(jnp.int32),
        segment_ids.reshape(1, key_count).astype(jnp.int32),
    )


def shifted_copies(x, axis_name, count):
    moved = [x]
    for shift in range(1, count):
        pairs = [(i, (i + shift) % count) for i in range(count)]
        moved.append(lax.ppermute(x, axis_name, pairs))
    return moved


def sum_by_permutes(x, axis_name, count):
    total = x.astype(jnp.float32)
    for part in shifted_copies(x, axis_name, count)[1:]:
        total = total + part.astype(jnp.float32)
    return total


def gather_by_permutes(x, axis_name, count, place):
    moved = shifted_copies(x, axis_name, count)
    reverse = jnp.stack([moved[0]] + moved[1:][::-1])
    return jnp.roll(reverse, place, axis=0)


def token_positions(segment_ids):
    stream_len = segment_ids.shape[0]
    token_index = jnp.arange(stream_len, dtype=jnp.int32)
    boundary = jnp.concatenate([jnp.ones((1,), jnp.bool_), segment_ids[1:] != segment_ids[:-1]])
    seg_start = lax.cummax(jnp.where(boundary, token_index, 0), axis=0)
    return (token_index - seg_start, seg_start)


def rotate(values_in, positions, head_count):
    half_dim = HD // 2
    frequency = rope_base ** (-(2.0 * jnp.arange(half_dim, dtype=jnp.float32)) / HD)
    angle_all = positions.astype(jnp.float32)[:, None] * frequency[None, :]
    cosine = jnp.cos(angle_all)[:, None, :]
    sine_part = jnp.sin(angle_all)[:, None, :]
    shaped = values_in.astype(jnp.float32).reshape(values_in.shape[0], head_count, HD)
    first_half = shaped[..., :half_dim]
    second_half = shaped[..., half_dim:]
    turned = jnp.concatenate(
        [
            first_half * cosine - second_half * sine_part,
            second_half * cosine + first_half * sine_part,
        ],
        axis=-1,
    )
    return turned.reshape(values_in.shape[0], head_count * HD).astype(jnp.bfloat16)


def rms_norm(hidden_in, norm_gain):
    mean_square = jnp.mean(hidden_in * hidden_in, axis=-1, keepdims=True)
    return (hidden_in * lax.rsqrt(mean_square + norm_eps) * norm_gain.astype(jnp.float32)).astype(
        jnp.bfloat16
    )


def expert_parts(incoming, expert_in, expert_out):
    expert_pre = jnp.einsum(
        "nscd,sgde->nscge", incoming, expert_in, preferred_element_type=jnp.float32
    )
    expert_hidden = (jax.nn.silu(expert_pre[..., 0, :]) * expert_pre[..., 1, :]).astype(
        jnp.bfloat16
    )
    return jnp.einsum(
        "nsce,sed->nscd", expert_hidden, expert_out, preferred_element_type=jnp.float32
    ).astype(jnp.bfloat16)


def body(
    segment_ids,
    queries,
    keys,
    values,
    out_weight,
    residual,
    norm_gain,
    shared_in,
    shared_out,
    shared_gate,
    expert_in,
    expert_out,
    expert_ids,
    gate_weights,
):
    seq_count = lax.axis_size("sh") * lax.axis_size("sl")
    exp_count = lax.axis_size("zl") * lax.axis_size("co")
    group_place = lax.axis_index("sh")
    sub_count = lax.axis_size("sl")
    seq_place = group_place * sub_count + lax.axis_index("sl")
    exp_place = lax.axis_index("zl") * lax.axis_size("co") + lax.axis_index("co")
    block_len = queries.shape[0]
    local_heads = queries.shape[1] // HD
    block_first = seq_place * block_len
    query_seg = lax.dynamic_slice_in_dim(segment_ids, block_first, block_len, 0)
    local_start = jnp.sum((segment_ids[None, :] < query_seg[:, None]).astype(jnp.int32), axis=1)
    local_pos = block_first + jnp.arange(block_len, dtype=jnp.int32) - local_start
    rotated_q = rotate(queries, local_pos, local_heads)
    key_cache = rotate(keys, local_pos, local_heads)
    stacked = jnp.stack([rotated_q, key_cache, values]).reshape(3, block_len, local_heads, HD)
    moved = lax.all_to_all(stacked, "sl", split_axis=2, concat_axis=1, tiled=True)
    span = block_len * sub_count
    head_q = moved[0].reshape(span, HD)
    head_kv = moved[1:].reshape(2, span, HD)
    group_count = lax.axis_size("sh")
    gathered = gather_by_permutes(head_kv, "sh", group_count, group_place)
    gathered = jnp.moveaxis(gathered, 0, 1).reshape(2, group_count * span, HD)
    span_first = group_place * span
    span_seg = lax.dynamic_slice_in_dim(segment_ids, span_first, span, 0)
    seg_first = jnp.sum((segment_ids < span_seg[0]).astype(jnp.int32))
    head_out = flash_attention(
        head_q, gathered[0], gathered[1], span_seg, segment_ids, span_first, seg_first
    )
    attended = lax.all_to_all(
        head_out.reshape(sub_count, block_len, 1, HD), "sl", split_axis=0, concat_axis=2, tiled=True
    ).reshape(block_len, local_heads * HD)
    attn_part = jnp.dot(attended, out_weight, preferred_element_type=jnp.float32)
    row_count = block_len // exp_count
    row_first = exp_place * row_count
    residual_f = residual.astype(jnp.float32)
    attn_sum = sum_by_permutes(attn_part.astype(jnp.bfloat16), EXP, exp_count)
    after_attn = residual_f + attn_sum
    normed = rms_norm(after_attn, norm_gain)
    attn_rows = lax.dynamic_slice_in_dim(attn_sum, row_first, row_count, 0).astype(jnp.bfloat16)
    after_rows = lax.dynamic_slice_in_dim(after_attn, row_first, row_count, 0)
    shared_pre = jnp.einsum("td,gde->tge", normed, shared_in, preferred_element_type=jnp.float32)
    shared_hidden = (jax.nn.silu(shared_pre[:, 0]) * shared_pre[:, 1]).astype(jnp.bfloat16)
    shared_term = jnp.dot(shared_hidden, shared_out, preferred_element_type=jnp.float32)
    shared_factor = jax.nn.sigmoid(jnp.dot(normed, shared_gate, preferred_element_type=jnp.float32))
    flat_ids = expert_ids.reshape(-1)
    flat_index = jnp.arange(flat_ids.shape[0], dtype=jnp.int32)
    earlier_same = (flat_ids[None, :] == flat_ids[:, None]) & (flat_index[None, :] < flat_index[:, None])
    slot_rank = jnp.sum(earlier_same.astype(jnp.int32), axis=1)
    slot_place = flat_ids * CAP + slot_rank
    owner_row = jnp.arange(flat_ids.shape[0], dtype=jnp.int32) // TOPK
    source_row = jnp.full((SLOTS * CAP,), -1, jnp.int32).at[slot_place].set(owner_row)
    slot_local = SLOTS // seq_count
    model_width = normed.shape[1]
    outgoing = jnp.where(
        (source_row >= 0)[:, None], normed[jnp.maximum(source_row, 0)], jnp.zeros((), jnp.bfloat16)
    ).reshape(seq_count, slot_local, CAP, model_width)
    col_count = model_width // exp_count
    col_first = exp_place * col_count
    outgoing_part = lax.dynamic_slice_in_dim(outgoing, col_first, col_count, 3)
    incoming = lax.all_gather(
        lax.all_to_all(outgoing_part, SEQ, split_axis=0, concat_axis=0, tiled=True),
        EXP,
        axis=3,
        tiled=True,
    )
    expert_part = expert_parts(incoming, expert_in, expert_out)
    summed = lax.psum_scatter(expert_part, EXP, scatter_dimension=3, tiled=True).astype(
        jnp.float32
    )
    returned = lax.all_to_all(
        summed.astype(jnp.bfloat16), SEQ, split_axis=0, concat_axis=0, tiled=True
    ).astype(summed.dtype)
    picked = returned.reshape(SLOTS * CAP, col_count)[slot_place].reshape(
        block_len, TOPK, col_count
    )
    moe_cols = jnp.sum(gate_weights[:, :, None] * picked, axis=1)
    moe_term = lax.dynamic_update_slice_in_dim(
        jnp.zeros((block_len, model_width), jnp.float32), moe_cols, col_first, 1
    )
    combined = shared_factor[:, None] * shared_term + moe_term
    moe_rows = lax.psum_scatter(
        combined.astype(jnp.bfloat16), EXP, scatter_dimension=0, tiled=True
    ).astype(jnp.float32)
    mixed_out = (after_rows + moe_rows).astype(jnp.bfloat16)
    return (mixed_out, attn_rows, key_cache)


SEQ = ("sh", "sl")
EXP = ("zl", "co")


def solution(mesh):
    exp_count = mesh.shape["exp"]
    seq_count = mesh.shape["seq"]
    sub_count = HEADS // exp_count
    grid = mesh.devices.reshape(seq_count // sub_count, sub_count, exp_count // 2, 2)
    split_mesh = Mesh(grid, ("sh", "sl", "zl", "co"))
    return jax.shard_map(
        body,
        mesh=split_mesh,
        in_specs=(
            P(),
            P(SEQ, EXP),
            P(SEQ, EXP),
            P(SEQ, EXP),
            P(EXP, None),
            P(SEQ, None),
            P(),
            P(None, None, EXP),
            P(EXP, None),
            P(),
            P(SEQ, None, None, EXP),
            P(SEQ, EXP, None),
            P(SEQ, None),
            P(SEQ, None),
        ),
        out_specs=(P(("sh", "sl", "zl", "co"), None), P(("sh", "sl", "zl", "co"), None), P(SEQ, EXP)),
        check_vma=False,
    )
```

```python
import math

import jax
import jax.numpy as jnp
from jax import lax
from jax.sharding import Mesh, PartitionSpec as P
from jax.experimental import pallas as pl
from jax.experimental.pallas import tpu as pltpu

HD = 128
HEADS = 16
TOPK = 4
SLOTS = 64
CAP = 32


rope_base = 1000000.0
neg_fill = -1e30
norm_eps = 1e-06


KEY_TILE = 512


def flash_kernel(bounds_ref, q_ref, k_ref, v_ref, qseg_ref, kseg_ref, o_ref, m_sc, l_sc, acc_sc):
    step = pl.program_id(0)
    first_chunk = bounds_ref[0]
    end_chunk = bounds_ref[1]
    query_first = bounds_ref[2]
    chunk = first_chunk + step
    rows = q_ref.shape[0]
    heads = q_ref.shape[1] // HD

    @pl.when(step == 0)
    def _():
        m_sc[...] = jnp.full(m_sc.shape, neg_fill, jnp.float32)
        l_sc[...] = jnp.zeros(l_sc.shape, jnp.float32)
        acc_sc[...] = jnp.zeros(acc_sc.shape, jnp.float32)

    @pl.when(chunk < end_chunk)
    def _():
        key_pos = chunk * KEY_TILE + lax.broadcasted_iota(jnp.int32, (1, KEY_TILE), 1)
        query_pos = query_first + lax.broadcasted_iota(jnp.int32, (rows, 1), 0)
        visible = (key_pos <= query_pos) & (kseg_ref[...] == qseg_ref[...])
        score_scale = 1.0 / math.sqrt(HD)
        for h in range(heads):
            cols = slice(h * HD, (h + 1) * HD)
            scores = (
                lax.dot_general(
                    q_ref[:, cols], k_ref[:, cols], (((1,), (1,)), ((), ())),
                    preferred_element_type=jnp.float32,
                )
                * score_scale
            )
            m_old = m_sc[h]
            m_new = jnp.maximum(
                m_old, jnp.max(jnp.where(visible, scores, neg_fill), axis=1, keepdims=True)
            )
            weights_f = jnp.where(visible, jnp.exp(scores - m_new), 0.0)
            rescale = jnp.exp(m_old - m_new)
            l_sc[h] = l_sc[h] * rescale + jnp.sum(weights_f, axis=1, keepdims=True)
            acc_sc[h] = acc_sc[h] * rescale + jnp.dot(
                weights_f.astype(jnp.bfloat16), v_ref[:, cols], preferred_element_type=jnp.float32
            )
            m_sc[h] = m_new

    @pl.when(step == pl.num_programs(0) - 1)
    def _():
        for h in range(heads):
            o_ref[:, h * HD:(h + 1) * HD] = (acc_sc[h] / l_sc[h]).astype(o_ref.dtype)


def flash_attention(rotated_q, key_all, value_all, query_seg, segment_ids, query_first, seg_first):
    rows, width = rotated_q.shape
    heads = width // HD
    key_count = key_all.shape[0]
    chunks = key_count // KEY_TILE
    first_chunk = seg_first // KEY_TILE
    end_chunk = (query_first + rows + KEY_TILE - 1) // KEY_TILE
    bounds = jnp.stack([first_chunk, end_chunk, query_first]).astype(jnp.int32)

    def kv_map(c, b):
        return (jnp.minimum(b[0] + c, b[1] - 1), 0)

    def kseg_map(c, b):
        return (0, jnp.minimum(b[0] + c, b[1] - 1))

    grid_spec = pltpu.PrefetchScalarGridSpec(
        num_scalar_prefetch=1,
        grid=(chunks,),
        in_specs=[
            pl.BlockSpec((rows, width), lambda c, b: (0, 0)),
            pl.BlockSpec((KEY_TILE, width), kv_map),
            pl.BlockSpec((KEY_TILE, width), kv_map),
            pl.BlockSpec((rows, 1), lambda c, b: (0, 0)),
            pl.BlockSpec((1, KEY_TILE), kseg_map),
        ],
        out_specs=pl.BlockSpec((rows, width), lambda c, b: (0, 0)),
        scratch_shapes=[
            pltpu.VMEM((heads, rows, 1), jnp.float32),
            pltpu.VMEM((heads, rows, 1), jnp.float32),
            pltpu.VMEM((heads, rows, HD), jnp.float32),
        ],
    )
    flops = 4 * rows * key_count * width
    return pl.pallas_call(
        flash_kernel,
        grid_spec=grid_spec,
        out_shape=jax.ShapeDtypeStruct((rows, width), jnp.bfloat16),
        compiler_params=pltpu.CompilerParams(
            dimension_semantics=("arbitrary",), vmem_limit_bytes=48 * 1024 * 1024
        ),
        cost_estimate=pl.CostEstimate(
            flops=flops,
            transcendentals=rows * key_count * heads,
            bytes_accessed=2 * key_count * width * 2 + 2 * rows * width * 2,
        ),
    )(
        bounds,
        rotated_q,
        key_all,
        value_all,
        query_seg.reshape(rows, 1).astype(jnp.int32),
        segment_ids.reshape(1, key_count).astype(jnp.int32),
    )


def shifted_copies(x, axis_name, count):
    moved = [x]
    for shift in range(1, count):
        pairs = [(i, (i + shift) % count) for i in range(count)]
        moved.append(lax.ppermute(x, axis_name, pairs))
    return moved


def sum_by_permutes(x, axis_name, count):
    total = x.astype(jnp.float32)
    for part in shifted_copies(x, axis_name, count)[1:]:
        total = total + part.astype(jnp.float32)
    return total


def gather_by_permutes(x, axis_name, count, place):
    moved = shifted_copies(x, axis_name, count)
    reverse = jnp.stack([moved[0]] + moved[1:][::-1])
    return jnp.roll(reverse, place, axis=0)


def token_positions(segment_ids):
    stream_len = segment_ids.shape[0]
    token_index = jnp.arange(stream_len, dtype=jnp.int32)
    boundary = jnp.concatenate([jnp.ones((1,), jnp.bool_), segment_ids[1:] != segment_ids[:-1]])
    seg_start = lax.cummax(jnp.where(boundary, token_index, 0), axis=0)
    return (token_index - seg_start, seg_start)


def rotate(values_in, positions, head_count):
    half_dim = HD // 2
    frequency = rope_base ** (-(2.0 * jnp.arange(half_dim, dtype=jnp.float32)) / HD)
    angle_all = positions.astype(jnp.float32)[:, None] * frequency[None, :]
    cosine = jnp.cos(angle_all)[:, None, :]
    sine_part = jnp.sin(angle_all)[:, None, :]
    shaped = values_in.astype(jnp.float32).reshape(values_in.shape[0], head_count, HD)
    first_half = shaped[..., :half_dim]
    second_half = shaped[..., half_dim:]
    turned = jnp.concatenate(
        [
            first_half * cosine - second_half * sine_part,
            second_half * cosine + first_half * sine_part,
        ],
        axis=-1,
    )
    return turned.reshape(values_in.shape[0], head_count * HD).astype(jnp.bfloat16)


def rms_norm(hidden_in, norm_gain):
    mean_square = jnp.mean(hidden_in * hidden_in, axis=-1, keepdims=True)
    return (hidden_in * lax.rsqrt(mean_square + norm_eps) * norm_gain.astype(jnp.float32)).astype(
        jnp.bfloat16
    )


def expert_parts(incoming, expert_in, expert_out):
    expert_pre = jnp.einsum(
        "nscd,sgde->nscge", incoming, expert_in, preferred_element_type=jnp.float32
    )
    expert_hidden = (jax.nn.silu(expert_pre[..., 0, :]) * expert_pre[..., 1, :]).astype(
        jnp.bfloat16
    )
    return jnp.einsum(
        "nsce,sed->nscd", expert_hidden, expert_out, preferred_element_type=jnp.float32
    ).astype(jnp.bfloat16)


def body(
    segment_ids,
    queries,
    keys,
    values,
    out_weight,
    residual,
    norm_gain,
    shared_in,
    shared_out,
    shared_gate,
    expert_in,
    expert_out,
    expert_ids,
    gate_weights,
):
    seq_count = lax.axis_size("sh") * lax.axis_size("sl")
    exp_count = lax.axis_size("zl") * lax.axis_size("co")
    group_place = lax.axis_index("sh")
    sub_count = lax.axis_size("sl")
    seq_place = group_place * sub_count + lax.axis_index("sl")
    exp_place = lax.axis_index("zl") * lax.axis_size("co") + lax.axis_index("co")
    block_len = queries.shape[0]
    local_heads = queries.shape[1] // HD
    block_first = seq_place * block_len
    query_seg = lax.dynamic_slice_in_dim(segment_ids, block_first, block_len, 0)
    local_start = jnp.sum((segment_ids[None, :] < query_seg[:, None]).astype(jnp.int32), axis=1)
    local_pos = block_first + jnp.arange(block_len, dtype=jnp.int32) - local_start
    rotated_q = rotate(queries, local_pos, local_heads)
    key_cache = rotate(keys, local_pos, local_heads)
    stacked = jnp.stack([rotated_q, key_cache, values]).reshape(3, block_len, local_heads, HD)
    moved = lax.all_to_all(stacked, "sl", split_axis=2, concat_axis=1, tiled=True)
    span = block_len * sub_count
    head_q = moved[0].reshape(span, HD)
    head_kv = moved[1:].reshape(2, span, HD)
    group_count = lax.axis_size("sh")
    gathered = gather_by_permutes(head_kv, "sh", group_count, group_place)
    gathered = jnp.moveaxis(gathered, 0, 1).reshape(2, group_count * span, HD)
    span_first = group_place * span
    span_seg = lax.dynamic_slice_in_dim(segment_ids, span_first, span, 0)
    seg_first = jnp.sum((segment_ids < span_seg[0]).astype(jnp.int32))
    head_out = flash_attention(
        head_q, gathered[0], gathered[1], span_seg, segment_ids, span_first, seg_first
    )
    attended = lax.all_to_all(
        head_out.reshape(sub_count, block_len, 1, HD), "sl", split_axis=0, concat_axis=2, tiled=True
    ).reshape(block_len, local_heads * HD)
    attn_part = jnp.dot(attended, out_weight, preferred_element_type=jnp.float32)
    row_count = block_len // exp_count
    row_first = exp_place * row_count
    residual_f = residual.astype(jnp.float32)
    attn_sum = sum_by_permutes(attn_part.astype(jnp.bfloat16), EXP, exp_count)
    after_attn = residual_f + attn_sum
    normed = rms_norm(after_attn, norm_gain)
    attn_rows = lax.dynamic_slice_in_dim(attn_sum, row_first, row_count, 0).astype(jnp.bfloat16)
    after_rows = lax.dynamic_slice_in_dim(after_attn, row_first, row_count, 0)
    shared_pre = jnp.einsum("td,gde->tge", normed, shared_in, preferred_element_type=jnp.float32)
    shared_hidden = (jax.nn.silu(shared_pre[:, 0]) * shared_pre[:, 1]).astype(jnp.bfloat16)
    shared_term = jnp.dot(shared_hidden, shared_out, preferred_element_type=jnp.float32)
    shared_factor = jax.nn.sigmoid(jnp.dot(normed, shared_gate, preferred_element_type=jnp.float32))
    flat_ids = expert_ids.reshape(-1)
    flat_index = jnp.arange(flat_ids.shape[0], dtype=jnp.int32)
    earlier_same = (flat_ids[None, :] == flat_ids[:, None]) & (flat_index[None, :] < flat_index[:, None])
    slot_rank = jnp.sum(earlier_same.astype(jnp.int32), axis=1)
    slot_place = flat_ids * CAP + slot_rank
    slot_local = SLOTS // seq_count
    model_width = normed.shape[1]
    col_count = model_width // exp_count
    col_first = exp_place * col_count
    slot_rows = jnp.arange(SLOTS * CAP, dtype=jnp.int32)
    place_hit = (slot_place[None, :] == slot_rows[:, None]).reshape(SLOTS * CAP, block_len, TOPK)
    dispatch = jnp.any(place_hit, axis=2).astype(jnp.bfloat16)
    normed_part = lax.dynamic_slice_in_dim(normed, col_first, col_count, 1)
    outgoing_part = (
        jnp.dot(dispatch, normed_part, preferred_element_type=jnp.float32)
        .astype(jnp.bfloat16)
        .reshape(seq_count, slot_local, CAP, col_count)
    )
    incoming = lax.all_gather(
        lax.all_to_all(outgoing_part, SEQ, split_axis=0, concat_axis=0, tiled=True),
        EXP,
        axis=3,
        tiled=True,
    )
    expert_part = expert_parts(incoming, expert_in, expert_out)
    summed = lax.psum_scatter(expert_part, EXP, scatter_dimension=3, tiled=True).astype(
        jnp.float32
    )
    returned = lax.all_to_all(
        summed.astype(jnp.bfloat16), SEQ, split_axis=0, concat_axis=0, tiled=True
    ).astype(summed.dtype)
    select_rows = (slot_place[:, None] == slot_rows[None, :]).astype(jnp.bfloat16)
    picked = jnp.dot(
        select_rows,
        returned.reshape(SLOTS * CAP, col_count).astype(jnp.bfloat16),
        preferred_element_type=jnp.float32,
    ).reshape(block_len, TOPK, col_count)
    moe_cols = jnp.sum(gate_weights[:, :, None] * picked, axis=1)
    moe_term = lax.dynamic_update_slice_in_dim(
        jnp.zeros((block_len, model_width), jnp.float32), moe_cols, col_first, 1
    )
    combined = shared_factor[:, None] * shared_term + moe_term
    moe_rows = lax.psum_scatter(
        combined.astype(jnp.bfloat16), EXP, scatter_dimension=0, tiled=True
    ).astype(jnp.float32)
    mixed_out = (after_rows + moe_rows).astype(jnp.bfloat16)
    return (mixed_out, attn_rows, key_cache)


SEQ = ("sh", "sl")
EXP = ("zl", "co")


def solution(mesh):
    exp_count = mesh.shape["exp"]
    seq_count = mesh.shape["seq"]
    sub_count = HEADS // exp_count
    grid = mesh.devices.reshape(seq_count // sub_count, sub_count, exp_count // 2, 2)
    split_mesh = Mesh(grid, ("sh", "sl", "zl", "co"))
    return jax.shard_map(
        body,
        mesh=split_mesh,
        in_specs=(
            P(),
            P(SEQ, EXP),
            P(SEQ, EXP),
            P(SEQ, EXP),
            P(EXP, None),
            P(SEQ, None),
            P(),
            P(None, None, EXP),
            P(EXP, None),
            P(),
            P(SEQ, None, None, EXP),
            P(SEQ, EXP, None),
            P(SEQ, None),
            P(SEQ, None),
        ),
        out_specs=(P(("sh", "sl", "zl", "co"), None), P(("sh", "sl", "zl", "co"), None), P(SEQ, EXP)),
        check_vma=False,
    )
```

```python
import math

import jax
import jax.numpy as jnp
from jax import lax
from jax.sharding import Mesh, PartitionSpec as P
from jax.experimental import pallas as pl
from jax.experimental.pallas import tpu as pltpu

HD = 128
HEADS = 16
TOPK = 4
SLOTS = 64
CAP = 32


rope_base = 1000000.0
neg_fill = -1e30
norm_eps = 1e-06


KEY_TILE = 512


def flash_kernel(bounds_ref, q_ref, k_ref, v_ref, qseg_ref, kseg_ref, o_ref, m_sc, l_sc, acc_sc):
    step = pl.program_id(0)
    first_chunk = bounds_ref[0]
    end_chunk = bounds_ref[1]
    query_first = bounds_ref[2]
    chunk = first_chunk + step
    rows = q_ref.shape[0]
    heads = q_ref.shape[1] // HD

    @pl.when(step == 0)
    def _():
        m_sc[...] = jnp.full(m_sc.shape, neg_fill, jnp.float32)
        l_sc[...] = jnp.zeros(l_sc.shape, jnp.float32)
        acc_sc[...] = jnp.zeros(acc_sc.shape, jnp.float32)

    @pl.when(chunk < end_chunk)
    def _():
        key_pos = chunk * KEY_TILE + lax.broadcasted_iota(jnp.int32, (1, KEY_TILE), 1)
        query_pos = query_first + lax.broadcasted_iota(jnp.int32, (rows, 1), 0)
        visible = (key_pos <= query_pos) & (kseg_ref[...] == qseg_ref[...])
        score_scale = 1.0 / math.sqrt(HD)
        for h in range(heads):
            cols = slice(h * HD, (h + 1) * HD)
            scores = (
                lax.dot_general(
                    q_ref[:, cols], k_ref[:, cols], (((1,), (1,)), ((), ())),
                    preferred_element_type=jnp.float32,
                )
                * score_scale
            )
            m_old = m_sc[h]
            m_new = jnp.maximum(
                m_old, jnp.max(jnp.where(visible, scores, neg_fill), axis=1, keepdims=True)
            )
            weights_f = jnp.where(visible, jnp.exp(scores - m_new), 0.0)
            rescale = jnp.exp(m_old - m_new)
            l_sc[h] = l_sc[h] * rescale + jnp.sum(weights_f, axis=1, keepdims=True)
            acc_sc[h] = acc_sc[h] * rescale + jnp.dot(
                weights_f.astype(jnp.bfloat16), v_ref[:, cols], preferred_element_type=jnp.float32
            )
            m_sc[h] = m_new

    @pl.when(step == pl.num_programs(0) - 1)
    def _():
        for h in range(heads):
            o_ref[:, h * HD:(h + 1) * HD] = (acc_sc[h] / l_sc[h]).astype(o_ref.dtype)


def flash_attention(rotated_q, key_all, value_all, query_seg, segment_ids, query_first, seg_first):
    rows, width = rotated_q.shape
    heads = width // HD
    key_count = key_all.shape[0]
    chunks = key_count // KEY_TILE
    first_chunk = seg_first // KEY_TILE
    end_chunk = (query_first + rows + KEY_TILE - 1) // KEY_TILE
    bounds = jnp.stack([first_chunk, end_chunk, query_first]).astype(jnp.int32)

    def kv_map(c, b):
        return (jnp.minimum(b[0] + c, b[1] - 1), 0)

    def kseg_map(c, b):
        return (0, jnp.minimum(b[0] + c, b[1] - 1))

    grid_spec = pltpu.PrefetchScalarGridSpec(
        num_scalar_prefetch=1,
        grid=(chunks,),
        in_specs=[
            pl.BlockSpec((rows, width), lambda c, b: (0, 0)),
            pl.BlockSpec((KEY_TILE, width), kv_map),
            pl.BlockSpec((KEY_TILE, width), kv_map),
            pl.BlockSpec((rows, 1), lambda c, b: (0, 0)),
            pl.BlockSpec((1, KEY_TILE), kseg_map),
        ],
        out_specs=pl.BlockSpec((rows, width), lambda c, b: (0, 0)),
        scratch_shapes=[
            pltpu.VMEM((heads, rows, 1), jnp.float32),
            pltpu.VMEM((heads, rows, 1), jnp.float32),
            pltpu.VMEM((heads, rows, HD), jnp.float32),
        ],
    )
    flops = 4 * rows * key_count * width
    return pl.pallas_call(
        flash_kernel,
        grid_spec=grid_spec,
        out_shape=jax.ShapeDtypeStruct((rows, width), jnp.bfloat16),
        compiler_params=pltpu.CompilerParams(
            dimension_semantics=("arbitrary",), vmem_limit_bytes=48 * 1024 * 1024
        ),
        cost_estimate=pl.CostEstimate(
            flops=flops,
            transcendentals=rows * key_count * heads,
            bytes_accessed=2 * key_count * width * 2 + 2 * rows * width * 2,
        ),
    )(
        bounds,
        rotated_q,
        key_all,
        value_all,
        query_seg.reshape(rows, 1).astype(jnp.int32),
        segment_ids.reshape(1, key_count).astype(jnp.int32),
    )


def shifted_copies(x, axis_name, count):
    moved = [x]
    for shift in range(1, count):
        pairs = [(i, (i + shift) % count) for i in range(count)]
        moved.append(lax.ppermute(x, axis_name, pairs))
    return moved


def sum_by_permutes(x, axis_name, count):
    total = x.astype(jnp.float32)
    for part in shifted_copies(x, axis_name, count)[1:]:
        total = total + part.astype(jnp.float32)
    return total


def gather_by_permutes(x, axis_name, count, place):
    moved = shifted_copies(x, axis_name, count)
    reverse = jnp.stack([moved[0]] + moved[1:][::-1])
    return jnp.roll(reverse, place, axis=0)


def token_positions(segment_ids):
    stream_len = segment_ids.shape[0]
    token_index = jnp.arange(stream_len, dtype=jnp.int32)
    boundary = jnp.concatenate([jnp.ones((1,), jnp.bool_), segment_ids[1:] != segment_ids[:-1]])
    seg_start = lax.cummax(jnp.where(boundary, token_index, 0), axis=0)
    return (token_index - seg_start, seg_start)


def rotate(values_in, positions, head_count):
    half_dim = HD // 2
    frequency = rope_base ** (-(2.0 * jnp.arange(half_dim, dtype=jnp.float32)) / HD)
    angle_all = positions.astype(jnp.float32)[:, None] * frequency[None, :]
    cosine = jnp.cos(angle_all)[:, None, :]
    sine_part = jnp.sin(angle_all)[:, None, :]
    shaped = values_in.astype(jnp.float32).reshape(values_in.shape[0], head_count, HD)
    first_half = shaped[..., :half_dim]
    second_half = shaped[..., half_dim:]
    turned = jnp.concatenate(
        [
            first_half * cosine - second_half * sine_part,
            second_half * cosine + first_half * sine_part,
        ],
        axis=-1,
    )
    return turned.reshape(values_in.shape[0], head_count * HD).astype(jnp.bfloat16)


def rms_norm(hidden_in, norm_gain):
    mean_square = jnp.mean(hidden_in * hidden_in, axis=-1, keepdims=True)
    return (hidden_in * lax.rsqrt(mean_square + norm_eps) * norm_gain.astype(jnp.float32)).astype(
        jnp.bfloat16
    )


def expert_parts(incoming, expert_in, expert_out):
    expert_pre = jnp.einsum(
        "nscd,sgde->nscge", incoming, expert_in, preferred_element_type=jnp.float32
    )
    expert_hidden = (jax.nn.silu(expert_pre[..., 0, :]) * expert_pre[..., 1, :]).astype(
        jnp.bfloat16
    )
    return jnp.einsum(
        "nsce,sed->nscd", expert_hidden, expert_out, preferred_element_type=jnp.float32
    ).astype(jnp.bfloat16)


def body(
    segment_ids,
    queries,
    keys,
    values,
    out_weight,
    residual,
    norm_gain,
    shared_in,
    shared_out,
    shared_gate,
    expert_in,
    expert_out,
    expert_ids,
    gate_weights,
):
    seq_count = lax.axis_size("sh") * lax.axis_size("sl")
    exp_count = lax.axis_size("zl") * lax.axis_size("co")
    group_place = lax.axis_index("sh")
    sub_count = lax.axis_size("sl")
    seq_place = group_place * sub_count + lax.axis_index("sl")
    exp_place = lax.axis_index("zl") * lax.axis_size("co") + lax.axis_index("co")
    block_len = queries.shape[0]
    local_heads = queries.shape[1] // HD
    block_first = seq_place * block_len
    query_seg = lax.dynamic_slice_in_dim(segment_ids, block_first, block_len, 0)
    local_start = jnp.sum((segment_ids[None, :] < query_seg[:, None]).astype(jnp.int32), axis=1)
    local_pos = block_first + jnp.arange(block_len, dtype=jnp.int32) - local_start
    rotated_q = rotate(queries, local_pos, local_heads)
    key_cache = rotate(keys, local_pos, local_heads)
    stacked = jnp.stack([rotated_q, key_cache, values]).reshape(3, block_len, local_heads, HD)
    moved = lax.all_to_all(stacked, "sl", split_axis=2, concat_axis=1, tiled=True)
    span = block_len * sub_count
    head_q = moved[0].reshape(span, HD)
    head_kv = moved[1:].reshape(2, span, HD)
    group_count = lax.axis_size("sh")
    gathered = gather_by_permutes(head_kv, "sh", group_count, group_place)
    gathered = jnp.moveaxis(gathered, 0, 1).reshape(2, group_count * span, HD)
    span_first = group_place * span
    span_seg = lax.dynamic_slice_in_dim(segment_ids, span_first, span, 0)
    seg_first = jnp.sum((segment_ids < span_seg[0]).astype(jnp.int32))
    head_out = flash_attention(
        head_q, gathered[0], gathered[1], span_seg, segment_ids, span_first, seg_first
    )
    attended = lax.all_to_all(
        head_out.reshape(sub_count, block_len, 1, HD), "sl", split_axis=0, concat_axis=2, tiled=True
    ).reshape(block_len, local_heads * HD)
    attn_part = jnp.dot(attended, out_weight, preferred_element_type=jnp.float32)
    row_count = block_len // exp_count
    row_first = exp_place * row_count
    residual_f = residual.astype(jnp.float32)
    attn_sum = sum_by_permutes(attn_part.astype(jnp.bfloat16), EXP, exp_count)
    after_attn = residual_f + attn_sum
    normed = rms_norm(after_attn, norm_gain)
    attn_rows = lax.dynamic_slice_in_dim(attn_sum, row_first, row_count, 0).astype(jnp.bfloat16)
    after_rows = lax.dynamic_slice_in_dim(after_attn, row_first, row_count, 0)
    shared_pre = jnp.einsum("td,gde->tge", normed, shared_in, preferred_element_type=jnp.float32)
    shared_hidden = (jax.nn.silu(shared_pre[:, 0]) * shared_pre[:, 1]).astype(jnp.bfloat16)
    shared_term = jnp.dot(shared_hidden, shared_out, preferred_element_type=jnp.float32)
    shared_factor = jax.nn.sigmoid(jnp.dot(normed, shared_gate, preferred_element_type=jnp.float32))
    flat_ids = expert_ids.reshape(-1)
    flat_index = jnp.arange(flat_ids.shape[0], dtype=jnp.int32)
    earlier_same = (flat_ids[None, :] == flat_ids[:, None]) & (flat_index[None, :] < flat_index[:, None])
    slot_rank = jnp.sum(earlier_same.astype(jnp.int32), axis=1)
    slot_place = flat_ids * CAP + slot_rank
    slot_local = SLOTS // seq_count
    model_width = normed.shape[1]
    col_count = model_width // exp_count
    col_first = exp_place * col_count
    slot_rows = jnp.arange(SLOTS * CAP, dtype=jnp.int32)
    place_hit = (slot_place[None, :] == slot_rows[:, None]).reshape(SLOTS * CAP, block_len, TOPK)
    dispatch = jnp.any(place_hit, axis=2).astype(jnp.bfloat16)
    normed_part = lax.dynamic_slice_in_dim(normed, col_first, col_count, 1)
    outgoing_part = (
        jnp.dot(dispatch, normed_part, preferred_element_type=jnp.float32)
        .astype(jnp.bfloat16)
        .reshape(seq_count, slot_local, CAP, col_count)
    )
    returned_parts = []
    for slot_id in range(slot_local):
        incoming = lax.all_gather(
            lax.all_to_all(
                outgoing_part[:, slot_id:slot_id + 1], SEQ, split_axis=0, concat_axis=0, tiled=True
            ),
            EXP,
            axis=3,
            tiled=True,
        )
        expert_part = expert_parts(
            incoming, expert_in[slot_id:slot_id + 1], expert_out[slot_id:slot_id + 1]
        )
        summed = lax.psum_scatter(expert_part, EXP, scatter_dimension=3, tiled=True)
        returned_parts.append(
            lax.all_to_all(summed, SEQ, split_axis=0, concat_axis=0, tiled=True)
        )
    returned = jnp.concatenate(returned_parts, axis=1)
    select_rows = (slot_place[:, None] == slot_rows[None, :]).astype(jnp.bfloat16)
    picked = jnp.dot(
        select_rows,
        returned.reshape(SLOTS * CAP, col_count).astype(jnp.bfloat16),
        preferred_element_type=jnp.float32,
    ).reshape(block_len, TOPK, col_count)
    moe_cols = jnp.sum(gate_weights[:, :, None] * picked, axis=1)
    moe_term = lax.dynamic_update_slice_in_dim(
        jnp.zeros((block_len, model_width), jnp.float32), moe_cols, col_first, 1
    )
    combined = shared_factor[:, None] * shared_term + moe_term
    moe_rows = lax.psum_scatter(
        combined.astype(jnp.bfloat16), EXP, scatter_dimension=0, tiled=True
    ).astype(jnp.float32)
    mixed_out = (after_rows + moe_rows).astype(jnp.bfloat16)
    return (mixed_out, attn_rows, key_cache)


SEQ = ("sh", "sl")
EXP = ("zl", "co")


def solution(mesh):
    exp_count = mesh.shape["exp"]
    seq_count = mesh.shape["seq"]
    sub_count = HEADS // exp_count
    grid = mesh.devices.reshape(seq_count // sub_count, sub_count, exp_count // 2, 2)
    split_mesh = Mesh(grid, ("sh", "sl", "zl", "co"))
    return jax.shard_map(
        body,
        mesh=split_mesh,
        in_specs=(
            P(),
            P(SEQ, EXP),
            P(SEQ, EXP),
            P(SEQ, EXP),
            P(EXP, None),
            P(SEQ, None),
            P(),
            P(None, None, EXP),
            P(EXP, None),
            P(),
            P(SEQ, None, None, EXP),
            P(SEQ, EXP, None),
            P(SEQ, None),
            P(SEQ, None),
        ),
        out_specs=(P(("sh", "sl", "zl", "co"), None), P(("sh", "sl", "zl", "co"), None), P(SEQ, EXP)),
        check_vma=False,
    )
```

```python
import math

import jax
import jax.numpy as jnp
from jax import lax
from jax.sharding import Mesh, PartitionSpec as P
from jax.experimental import pallas as pl
from jax.experimental.pallas import tpu as pltpu

HD = 128
HEADS = 16
TOPK = 4
SLOTS = 64
CAP = 32


rope_base = 1000000.0
neg_fill = -1e30
norm_eps = 1e-06


KEY_TILE = 512


def flash_kernel(bounds_ref, q_ref, k_ref, v_ref, qseg_ref, kseg_ref, o_ref, m_sc, l_sc, acc_sc):
    step = pl.program_id(0)
    first_chunk = bounds_ref[0]
    end_chunk = bounds_ref[1]
    query_first = bounds_ref[2]
    chunk = first_chunk + step
    rows = q_ref.shape[0]
    heads = q_ref.shape[1] // HD

    @pl.when(step == 0)
    def _():
        m_sc[...] = jnp.full(m_sc.shape, neg_fill, jnp.float32)
        l_sc[...] = jnp.zeros(l_sc.shape, jnp.float32)
        acc_sc[...] = jnp.zeros(acc_sc.shape, jnp.float32)

    @pl.when(chunk < end_chunk)
    def _():
        key_pos = chunk * KEY_TILE + lax.broadcasted_iota(jnp.int32, (1, KEY_TILE), 1)
        query_pos = query_first + lax.broadcasted_iota(jnp.int32, (rows, 1), 0)
        visible = (key_pos <= query_pos) & (kseg_ref[...] == qseg_ref[...])
        score_scale = 1.0 / math.sqrt(HD)
        for h in range(heads):
            cols = slice(h * HD, (h + 1) * HD)
            scores = (
                lax.dot_general(
                    q_ref[:, cols], k_ref[:, cols], (((1,), (1,)), ((), ())),
                    preferred_element_type=jnp.float32,
                )
                * score_scale
            )
            m_old = m_sc[h]
            m_new = jnp.maximum(
                m_old, jnp.max(jnp.where(visible, scores, neg_fill), axis=1, keepdims=True)
            )
            weights_f = jnp.where(visible, jnp.exp(scores - m_new), 0.0)
            rescale = jnp.exp(m_old - m_new)
            l_sc[h] = l_sc[h] * rescale + jnp.sum(weights_f, axis=1, keepdims=True)
            acc_sc[h] = acc_sc[h] * rescale + jnp.dot(
                weights_f.astype(jnp.bfloat16), v_ref[:, cols], preferred_element_type=jnp.float32
            )
            m_sc[h] = m_new

    @pl.when(step == pl.num_programs(0) - 1)
    def _():
        for h in range(heads):
            o_ref[:, h * HD:(h + 1) * HD] = (acc_sc[h] / l_sc[h]).astype(o_ref.dtype)


def flash_attention(rotated_q, key_all, value_all, query_seg, segment_ids, query_first, seg_first):
    rows, width = rotated_q.shape
    heads = width // HD
    key_count = key_all.shape[0]
    chunks = key_count // KEY_TILE
    first_chunk = seg_first // KEY_TILE
    end_chunk = (query_first + rows + KEY_TILE - 1) // KEY_TILE
    bounds = jnp.stack([first_chunk, end_chunk, query_first]).astype(jnp.int32)

    def kv_map(c, b):
        return (jnp.minimum(b[0] + c, b[1] - 1), 0)

    def kseg_map(c, b):
        return (0, jnp.minimum(b[0] + c, b[1] - 1))

    grid_spec = pltpu.PrefetchScalarGridSpec(
        num_scalar_prefetch=1,
        grid=(chunks,),
        in_specs=[
            pl.BlockSpec((rows, width), lambda c, b: (0, 0)),
            pl.BlockSpec((KEY_TILE, width), kv_map),
            pl.BlockSpec((KEY_TILE, width), kv_map),
            pl.BlockSpec((rows, 1), lambda c, b: (0, 0)),
            pl.BlockSpec((1, KEY_TILE), kseg_map),
        ],
        out_specs=pl.BlockSpec((rows, width), lambda c, b: (0, 0)),
        scratch_shapes=[
            pltpu.VMEM((heads, rows, 1), jnp.float32),
            pltpu.VMEM((heads, rows, 1), jnp.float32),
            pltpu.VMEM((heads, rows, HD), jnp.float32),
        ],
    )
    flops = 4 * rows * key_count * width
    return pl.pallas_call(
        flash_kernel,
        grid_spec=grid_spec,
        out_shape=jax.ShapeDtypeStruct((rows, width), jnp.bfloat16),
        compiler_params=pltpu.CompilerParams(
            dimension_semantics=("arbitrary",), vmem_limit_bytes=48 * 1024 * 1024
        ),
        cost_estimate=pl.CostEstimate(
            flops=flops,
            transcendentals=rows * key_count * heads,
            bytes_accessed=2 * key_count * width * 2 + 2 * rows * width * 2,
        ),
    )(
        bounds,
        rotated_q,
        key_all,
        value_all,
        query_seg.reshape(rows, 1).astype(jnp.int32),
        segment_ids.reshape(1, key_count).astype(jnp.int32),
    )


def shifted_copies(x, axis_name, count):
    moved = [x]
    for shift in range(1, count):
        pairs = [(i, (i + shift) % count) for i in range(count)]
        moved.append(lax.ppermute(x, axis_name, pairs))
    return moved


def sum_by_permutes(x, axis_name, count):
    total = x.astype(jnp.float32)
    for part in shifted_copies(x, axis_name, count)[1:]:
        total = total + part.astype(jnp.float32)
    return total


def gather_by_permutes(x, axis_name, count, place):
    moved = shifted_copies(x, axis_name, count)
    reverse = jnp.stack([moved[0]] + moved[1:][::-1])
    return jnp.roll(reverse, place, axis=0)


def token_positions(segment_ids):
    stream_len = segment_ids.shape[0]
    token_index = jnp.arange(stream_len, dtype=jnp.int32)
    boundary = jnp.concatenate([jnp.ones((1,), jnp.bool_), segment_ids[1:] != segment_ids[:-1]])
    seg_start = lax.cummax(jnp.where(boundary, token_index, 0), axis=0)
    return (token_index - seg_start, seg_start)


def rotate(values_in, positions, head_count):
    half_dim = HD // 2
    frequency = rope_base ** (-(2.0 * jnp.arange(half_dim, dtype=jnp.float32)) / HD)
    angle_all = positions.astype(jnp.float32)[:, None] * frequency[None, :]
    cosine = jnp.cos(angle_all)[:, None, :]
    sine_part = jnp.sin(angle_all)[:, None, :]
    shaped = values_in.astype(jnp.float32).reshape(values_in.shape[0], head_count, HD)
    first_half = shaped[..., :half_dim]
    second_half = shaped[..., half_dim:]
    turned = jnp.concatenate(
        [
            first_half * cosine - second_half * sine_part,
            second_half * cosine + first_half * sine_part,
        ],
        axis=-1,
    )
    return turned.reshape(values_in.shape[0], head_count * HD).astype(jnp.bfloat16)


def rms_norm(hidden_in, norm_gain):
    mean_square = jnp.mean(hidden_in * hidden_in, axis=-1, keepdims=True)
    return (hidden_in * lax.rsqrt(mean_square + norm_eps) * norm_gain.astype(jnp.float32)).astype(
        jnp.bfloat16
    )


def expert_parts(incoming, expert_in, expert_out):
    expert_pre = jnp.einsum(
        "nscd,sgde->nscge", incoming, expert_in, preferred_element_type=jnp.float32
    )
    expert_hidden = (jax.nn.silu(expert_pre[..., 0, :]) * expert_pre[..., 1, :]).astype(
        jnp.bfloat16
    )
    return jnp.einsum(
        "nsce,sed->nscd", expert_hidden, expert_out, preferred_element_type=jnp.float32
    ).astype(jnp.bfloat16)


def body(
    segment_ids,
    queries,
    keys,
    values,
    out_weight,
    residual,
    norm_gain,
    shared_in,
    shared_out,
    shared_gate,
    expert_in,
    expert_out,
    expert_ids,
    gate_weights,
):
    seq_count = lax.axis_size("sh") * lax.axis_size("sl")
    exp_count = lax.axis_size("zl") * lax.axis_size("co")
    group_place = lax.axis_index("sh")
    sub_count = lax.axis_size("sl")
    seq_place = group_place * sub_count + lax.axis_index("sl")
    exp_place = lax.axis_index("zl") * lax.axis_size("co") + lax.axis_index("co")
    block_len = queries.shape[0]
    local_heads = queries.shape[1] // HD
    block_first = seq_place * block_len
    query_seg = lax.dynamic_slice_in_dim(segment_ids, block_first, block_len, 0)
    local_start = jnp.sum((segment_ids[None, :] < query_seg[:, None]).astype(jnp.int32), axis=1)
    local_pos = block_first + jnp.arange(block_len, dtype=jnp.int32) - local_start
    rotated_q = rotate(queries, local_pos, local_heads)
    key_cache = rotate(keys, local_pos, local_heads)
    stacked = jnp.stack([rotated_q, key_cache, values]).reshape(3, block_len, local_heads, HD)
    moved = lax.all_to_all(stacked, "sl", split_axis=2, concat_axis=1, tiled=True)
    span = block_len * sub_count
    head_q = moved[0].reshape(span, HD)
    head_kv = moved[1:].reshape(2, span, HD)
    group_count = lax.axis_size("sh")
    gathered = gather_by_permutes(head_kv, "sh", group_count, group_place)
    gathered = jnp.moveaxis(gathered, 0, 1).reshape(2, group_count * span, HD)
    span_first = group_place * span
    span_seg = lax.dynamic_slice_in_dim(segment_ids, span_first, span, 0)
    seg_first = jnp.sum((segment_ids < span_seg[0]).astype(jnp.int32))
    head_out = flash_attention(
        head_q, gathered[0], gathered[1], span_seg, segment_ids, span_first, seg_first
    )
    attended = lax.all_to_all(
        head_out.reshape(sub_count, block_len, 1, HD), "sl", split_axis=0, concat_axis=2, tiled=True
    ).reshape(block_len, local_heads * HD)
    attn_part = jnp.dot(attended, out_weight, preferred_element_type=jnp.float32)
    row_count = block_len // exp_count
    row_first = exp_place * row_count
    residual_f = residual.astype(jnp.float32)
    attn_sum = sum_by_permutes(attn_part.astype(jnp.bfloat16), EXP, exp_count)
    after_attn = residual_f + attn_sum
    normed = rms_norm(after_attn, norm_gain)
    attn_rows = lax.dynamic_slice_in_dim(attn_sum, row_first, row_count, 0).astype(jnp.bfloat16)
    after_rows = lax.dynamic_slice_in_dim(after_attn, row_first, row_count, 0)
    shared_pre = jnp.einsum("td,gde->tge", normed, shared_in, preferred_element_type=jnp.float32)
    shared_hidden = (jax.nn.silu(shared_pre[:, 0]) * shared_pre[:, 1]).astype(jnp.bfloat16)
    shared_term = jnp.dot(shared_hidden, shared_out, preferred_element_type=jnp.float32)
    shared_factor = jax.nn.sigmoid(jnp.dot(normed, shared_gate, preferred_element_type=jnp.float32))
    flat_ids = expert_ids.reshape(-1)
    flat_index = jnp.arange(flat_ids.shape[0], dtype=jnp.int32)
    earlier_same = (flat_ids[None, :] == flat_ids[:, None]) & (flat_index[None, :] < flat_index[:, None])
    slot_rank = jnp.sum(earlier_same.astype(jnp.int32), axis=1)
    slot_place = flat_ids * CAP + slot_rank
    slot_local = SLOTS // seq_count
    model_width = normed.shape[1]
    core_count = lax.axis_size("co")
    col_count = model_width // core_count
    col_first = lax.axis_index("co") * col_count
    slot_rows = jnp.arange(SLOTS * CAP, dtype=jnp.int32)
    place_hit = (slot_place[None, :] == slot_rows[:, None]).reshape(SLOTS * CAP, block_len, TOPK)
    dispatch = jnp.any(place_hit, axis=2).astype(jnp.bfloat16)
    normed_part = lax.dynamic_slice_in_dim(normed, col_first, col_count, 1)
    outgoing_part = (
        jnp.dot(dispatch, normed_part, preferred_element_type=jnp.float32)
        .astype(jnp.bfloat16)
        .reshape(seq_count, slot_local, CAP, col_count)
    )
    incoming = lax.all_gather(
        lax.all_to_all(outgoing_part, SEQ, split_axis=0, concat_axis=0, tiled=True),
        "co",
        axis=3,
        tiled=True,
    )
    expert_part = expert_parts(incoming, expert_in, expert_out)
    summed = lax.psum_scatter(expert_part, "co", scatter_dimension=3, tiled=True).astype(
        jnp.float32
    )
    returned = lax.all_to_all(
        summed.astype(jnp.bfloat16), SEQ, split_axis=0, concat_axis=0, tiled=True
    ).astype(summed.dtype)
    select_rows = (slot_place[:, None] == slot_rows[None, :]).astype(jnp.bfloat16)
    picked = jnp.dot(
        select_rows,
        returned.reshape(SLOTS * CAP, col_count).astype(jnp.bfloat16),
        preferred_element_type=jnp.float32,
    ).reshape(block_len, TOPK, col_count)
    moe_cols = jnp.sum(gate_weights[:, :, None] * picked, axis=1)
    moe_term = lax.dynamic_update_slice_in_dim(
        jnp.zeros((block_len, model_width), jnp.float32), moe_cols, col_first, 1
    )
    combined = shared_factor[:, None] * shared_term + moe_term
    moe_rows = lax.psum_scatter(
        combined.astype(jnp.bfloat16), EXP, scatter_dimension=0, tiled=True
    ).astype(jnp.float32)
    mixed_out = (after_rows + moe_rows).astype(jnp.bfloat16)
    return (mixed_out, attn_rows, key_cache)


SEQ = ("sh", "sl")
EXP = ("zl", "co")


def solution(mesh):
    exp_count = mesh.shape["exp"]
    seq_count = mesh.shape["seq"]
    sub_count = HEADS // exp_count
    grid = mesh.devices.reshape(seq_count // sub_count, sub_count, exp_count // 2, 2)
    split_mesh = Mesh(grid, ("sh", "sl", "zl", "co"))
    return jax.shard_map(
        body,
        mesh=split_mesh,
        in_specs=(
            P(),
            P(SEQ, EXP),
            P(SEQ, EXP),
            P(SEQ, EXP),
            P(EXP, None),
            P(SEQ, None),
            P(),
            P(None, None, EXP),
            P(EXP, None),
            P(),
            P(SEQ, None, None, EXP),
            P(SEQ, EXP, None),
            P(SEQ, None),
            P(SEQ, None),
        ),
        out_specs=(P(("sh", "sl", "zl", "co"), None), P(("sh", "sl", "zl", "co"), None), P(SEQ, EXP)),
        check_vma=False,
    )
```

```python
import math

import jax
import jax.numpy as jnp
from jax import lax
from jax.sharding import Mesh, PartitionSpec as P
from jax.experimental import pallas as pl
from jax.experimental.pallas import tpu as pltpu

HD = 128
HEADS = 16
MOST = 6144
TOPK = 4
SLOTS = 64
CAP = 32


rope_base = 1000000.0
neg_fill = -1e30
norm_eps = 1e-06


KEY_TILE = 512


def flash_kernel(bounds_ref, q_ref, k_ref, v_ref, qseg_ref, kseg_ref, o_ref, m_sc, l_sc, acc_sc):
    step = pl.program_id(0)
    first_chunk = bounds_ref[0]
    end_chunk = bounds_ref[1]
    query_first = bounds_ref[2]
    chunk = first_chunk + step
    rows = q_ref.shape[0]
    heads = q_ref.shape[1] // HD

    @pl.when(step == 0)
    def _():
        m_sc[...] = jnp.full(m_sc.shape, neg_fill, jnp.float32)
        l_sc[...] = jnp.zeros(l_sc.shape, jnp.float32)
        acc_sc[...] = jnp.zeros(acc_sc.shape, jnp.float32)

    @pl.when(chunk < end_chunk)
    def _():
        key_pos = chunk * KEY_TILE + lax.broadcasted_iota(jnp.int32, (1, KEY_TILE), 1)
        query_pos = query_first + lax.broadcasted_iota(jnp.int32, (rows, 1), 0)
        visible = (key_pos <= query_pos) & (kseg_ref[...] == qseg_ref[...])
        score_scale = 1.0 / math.sqrt(HD)
        for h in range(heads):
            cols = slice(h * HD, (h + 1) * HD)
            scores = (
                lax.dot_general(
                    q_ref[:, cols], k_ref[:, cols], (((1,), (1,)), ((), ())),
                    preferred_element_type=jnp.float32,
                )
                * score_scale
            )
            m_old = m_sc[h]
            m_new = jnp.maximum(
                m_old, jnp.max(jnp.where(visible, scores, neg_fill), axis=1, keepdims=True)
            )
            weights_f = jnp.where(visible, jnp.exp(scores - m_new), 0.0)
            rescale = jnp.exp(m_old - m_new)
            l_sc[h] = l_sc[h] * rescale + jnp.sum(weights_f, axis=1, keepdims=True)
            acc_sc[h] = acc_sc[h] * rescale + jnp.dot(
                weights_f.astype(jnp.bfloat16), v_ref[:, cols], preferred_element_type=jnp.float32
            )
            m_sc[h] = m_new

    @pl.when(step == pl.num_programs(0) - 1)
    def _():
        for h in range(heads):
            o_ref[:, h * HD:(h + 1) * HD] = (acc_sc[h] / l_sc[h]).astype(o_ref.dtype)


def flash_attention(rotated_q, key_all, value_all, query_seg, segment_ids, query_first, seg_first):
    rows, width = rotated_q.shape
    heads = width // HD
    key_count = key_all.shape[0]
    chunks = key_count // KEY_TILE
    first_chunk = seg_first // KEY_TILE
    end_chunk = (query_first + rows + KEY_TILE - 1) // KEY_TILE
    bounds = jnp.stack([first_chunk, end_chunk, query_first]).astype(jnp.int32)

    def kv_map(c, b):
        return (jnp.minimum(b[0] + c, b[1] - 1), 0)

    def kseg_map(c, b):
        return (0, jnp.minimum(b[0] + c, b[1] - 1))

    grid_spec = pltpu.PrefetchScalarGridSpec(
        num_scalar_prefetch=1,
        grid=(chunks,),
        in_specs=[
            pl.BlockSpec((rows, width), lambda c, b: (0, 0)),
            pl.BlockSpec((KEY_TILE, width), kv_map),
            pl.BlockSpec((KEY_TILE, width), kv_map),
            pl.BlockSpec((rows, 1), lambda c, b: (0, 0)),
            pl.BlockSpec((1, KEY_TILE), kseg_map),
        ],
        out_specs=pl.BlockSpec((rows, width), lambda c, b: (0, 0)),
        scratch_shapes=[
            pltpu.VMEM((heads, rows, 1), jnp.float32),
            pltpu.VMEM((heads, rows, 1), jnp.float32),
            pltpu.VMEM((heads, rows, HD), jnp.float32),
        ],
    )
    flops = 4 * rows * key_count * width
    return pl.pallas_call(
        flash_kernel,
        grid_spec=grid_spec,
        out_shape=jax.ShapeDtypeStruct((rows, width), jnp.bfloat16),
        compiler_params=pltpu.CompilerParams(
            dimension_semantics=("arbitrary",), vmem_limit_bytes=48 * 1024 * 1024
        ),
        cost_estimate=pl.CostEstimate(
            flops=flops,
            transcendentals=rows * key_count * heads,
            bytes_accessed=2 * key_count * width * 2 + 2 * rows * width * 2,
        ),
    )(
        bounds,
        rotated_q,
        key_all,
        value_all,
        query_seg.reshape(rows, 1).astype(jnp.int32),
        segment_ids.reshape(1, key_count).astype(jnp.int32),
    )


def shifted_copies(x, axis_name, count):
    moved = [x]
    for shift in range(1, count):
        pairs = [(i, (i + shift) % count) for i in range(count)]
        moved.append(lax.ppermute(x, axis_name, pairs))
    return moved


def sum_by_permutes(x, axis_name, count):
    total = x.astype(jnp.float32)
    for part in shifted_copies(x, axis_name, count)[1:]:
        total = total + part.astype(jnp.float32)
    return total


def causal_copies(x, axis_name, count, reach):
    moved = [x]
    for shift in range(1, count):
        pairs = [(i, i + shift) for i in range(count - shift)] if shift <= reach else []
        moved.append(lax.ppermute(x, axis_name, pairs) if pairs else jnp.zeros_like(x))
    return moved


def sum_over_chip_pairs(x):
    half = x.shape[1] // 2
    core = lax.axis_index("co")
    swap = [(0, 1), (1, 0)]
    pair = x.astype(jnp.float32) + lax.ppermute(x, "co", swap).astype(jnp.float32)
    mine = lax.dynamic_slice_in_dim(pair, core * half, half, 1).astype(jnp.bfloat16)
    done = (mine.astype(jnp.float32) + lax.ppermute(mine, "zl", swap).astype(jnp.float32)).astype(
        jnp.bfloat16
    )
    other = lax.ppermute(done, "co", swap)
    whole = jnp.where(
        core == 0, jnp.concatenate([done, other], axis=1), jnp.concatenate([other, done], axis=1)
    )
    return whole.astype(jnp.float32)


def gather_by_permutes(x, axis_name, count, place, reach):
    moved = causal_copies(x, axis_name, count, reach)
    reverse = jnp.stack([moved[0]] + moved[1:][::-1])
    return jnp.roll(reverse, place, axis=0)


def token_positions(segment_ids):
    stream_len = segment_ids.shape[0]
    token_index = jnp.arange(stream_len, dtype=jnp.int32)
    boundary = jnp.concatenate([jnp.ones((1,), jnp.bool_), segment_ids[1:] != segment_ids[:-1]])
    seg_start = lax.cummax(jnp.where(boundary, token_index, 0), axis=0)
    return (token_index - seg_start, seg_start)


def rotate(values_in, positions, head_count):
    half_dim = HD // 2
    frequency = rope_base ** (-(2.0 * jnp.arange(half_dim, dtype=jnp.float32)) / HD)
    angle_all = positions.astype(jnp.float32)[:, None] * frequency[None, :]
    cosine = jnp.cos(angle_all)[:, None, :]
    sine_part = jnp.sin(angle_all)[:, None, :]
    shaped = values_in.astype(jnp.float32).reshape(values_in.shape[0], head_count, HD)
    first_half = shaped[..., :half_dim]
    second_half = shaped[..., half_dim:]
    turned = jnp.concatenate(
        [
            first_half * cosine - second_half * sine_part,
            second_half * cosine + first_half * sine_part,
        ],
        axis=-1,
    )
    return turned.reshape(values_in.shape[0], head_count * HD).astype(jnp.bfloat16)


def rms_norm(hidden_in, norm_gain):
    mean_square = jnp.mean(hidden_in * hidden_in, axis=-1, keepdims=True)
    return (hidden_in * lax.rsqrt(mean_square + norm_eps) * norm_gain.astype(jnp.float32)).astype(
        jnp.bfloat16
    )


def expert_parts(incoming, expert_in, expert_out):
    expert_pre = jnp.einsum(
        "nscd,sgde->nscge", incoming, expert_in, preferred_element_type=jnp.float32
    )
    expert_hidden = (jax.nn.silu(expert_pre[..., 0, :]) * expert_pre[..., 1, :]).astype(
        jnp.bfloat16
    )
    return jnp.einsum(
        "nsce,sed->nscd", expert_hidden, expert_out, preferred_element_type=jnp.float32
    ).astype(jnp.bfloat16)


def body(
    segment_ids,
    queries,
    keys,
    values,
    out_weight,
    residual,
    norm_gain,
    shared_in,
    shared_out,
    shared_gate,
    expert_in,
    expert_out,
    expert_ids,
    gate_weights,
):
    seq_count = lax.axis_size("sh") * lax.axis_size("sl")
    exp_count = lax.axis_size("zl") * lax.axis_size("co")
    group_place = lax.axis_index("sh")
    sub_count = lax.axis_size("sl")
    seq_place = group_place * sub_count + lax.axis_index("sl")
    exp_place = lax.axis_index("zl") * lax.axis_size("co") + lax.axis_index("co")
    block_len = queries.shape[0]
    local_heads = queries.shape[1] // HD
    block_first = seq_place * block_len
    query_seg = lax.dynamic_slice_in_dim(segment_ids, block_first, block_len, 0)
    local_start = jnp.sum((segment_ids[None, :] < query_seg[:, None]).astype(jnp.int32), axis=1)
    local_pos = block_first + jnp.arange(block_len, dtype=jnp.int32) - local_start
    rotated_q = rotate(queries, local_pos, local_heads)
    key_cache = rotate(keys, local_pos, local_heads)
    stacked = jnp.stack([rotated_q, key_cache, values]).reshape(3, block_len, local_heads, HD)
    moved = lax.all_to_all(stacked, "sl", split_axis=2, concat_axis=1, tiled=True)
    span = block_len * sub_count
    head_q = moved[0].reshape(span, HD)
    head_kv = moved[1:].reshape(2, span, HD)
    group_count = lax.axis_size("sh")
    reach = -(-(MOST + span - 1) // span) - 1
    gathered = gather_by_permutes(head_kv, "sh", group_count, group_place, reach)
    gathered = jnp.moveaxis(gathered, 0, 1).reshape(2, group_count * span, HD)
    span_first = group_place * span
    span_seg = lax.dynamic_slice_in_dim(segment_ids, span_first, span, 0)
    seg_first = jnp.sum((segment_ids < span_seg[0]).astype(jnp.int32))
    head_out = flash_attention(
        head_q, gathered[0], gathered[1], span_seg, segment_ids, span_first, seg_first
    )
    attended = lax.all_to_all(
        head_out.reshape(sub_count, block_len, 1, HD), "sl", split_axis=0, concat_axis=2, tiled=True
    ).reshape(block_len, local_heads * HD)
    attn_part = jnp.dot(attended, out_weight, preferred_element_type=jnp.float32)
    row_count = block_len // exp_count
    row_first = exp_place * row_count
    residual_f = residual.astype(jnp.float32)
    attn_sum = sum_over_chip_pairs(attn_part.astype(jnp.bfloat16))
    after_attn = residual_f + attn_sum
    normed = rms_norm(after_attn, norm_gain)
    attn_rows = lax.dynamic_slice_in_dim(attn_sum, row_first, row_count, 0).astype(jnp.bfloat16)
    after_rows = lax.dynamic_slice_in_dim(after_attn, row_first, row_count, 0)
    shared_pre = jnp.einsum("td,gde->tge", normed, shared_in, preferred_element_type=jnp.float32)
    shared_hidden = (jax.nn.silu(shared_pre[:, 0]) * shared_pre[:, 1]).astype(jnp.bfloat16)
    shared_term = jnp.dot(shared_hidden, shared_out, preferred_element_type=jnp.float32)
    shared_factor = jax.nn.sigmoid(jnp.dot(normed, shared_gate, preferred_element_type=jnp.float32))
    flat_ids = expert_ids.reshape(-1)
    flat_index = jnp.arange(flat_ids.shape[0], dtype=jnp.int32)
    earlier_same = (flat_ids[None, :] == flat_ids[:, None]) & (flat_index[None, :] < flat_index[:, None])
    slot_rank = jnp.sum(earlier_same.astype(jnp.int32), axis=1)
    slot_place = flat_ids * CAP + slot_rank
    slot_local = SLOTS // seq_count
    model_width = normed.shape[1]
    core_count = lax.axis_size("co")
    col_count = model_width // core_count
    col_first = lax.axis_index("co") * col_count
    slot_rows = jnp.arange(SLOTS * CAP, dtype=jnp.int32)
    place_hit = (slot_place[None, :] == slot_rows[:, None]).reshape(SLOTS * CAP, block_len, TOPK)
    dispatch = jnp.any(place_hit, axis=2).astype(jnp.bfloat16)
    normed_part = lax.dynamic_slice_in_dim(normed, col_first, col_count, 1)
    outgoing_part = (
        jnp.dot(dispatch, normed_part, preferred_element_type=jnp.float32)
        .astype(jnp.bfloat16)
        .reshape(seq_count, slot_local, CAP, col_count)
    )
    incoming = lax.all_gather(
        lax.all_to_all(outgoing_part, SEQ, split_axis=0, concat_axis=0, tiled=True),
        "co",
        axis=3,
        tiled=True,
    )
    expert_part = expert_parts(incoming, expert_in, expert_out)
    summed = lax.psum_scatter(expert_part, "co", scatter_dimension=3, tiled=True).astype(
        jnp.float32
    )
    returned = lax.all_to_all(
        summed.astype(jnp.bfloat16), SEQ, split_axis=0, concat_axis=0, tiled=True
    ).astype(summed.dtype)
    select_rows = (slot_place[:, None] == slot_rows[None, :]).astype(jnp.bfloat16)
    picked = jnp.dot(
        select_rows,
        returned.reshape(SLOTS * CAP, col_count).astype(jnp.bfloat16),
        preferred_element_type=jnp.float32,
    ).reshape(block_len, TOPK, col_count)
    moe_cols = jnp.sum(gate_weights[:, :, None] * picked, axis=1)
    moe_term = lax.dynamic_update_slice_in_dim(
        jnp.zeros((block_len, model_width), jnp.float32), moe_cols, col_first, 1
    )
    combined = shared_factor[:, None] * shared_term + moe_term
    moe_rows = lax.psum_scatter(
        combined.astype(jnp.bfloat16), EXP, scatter_dimension=0, tiled=True
    ).astype(jnp.float32)
    mixed_out = (after_rows + moe_rows).astype(jnp.bfloat16)
    return (mixed_out, attn_rows, key_cache)


SEQ = ("sh", "sl")
EXP = ("zl", "co")


def solution(mesh):
    exp_count = mesh.shape["exp"]
    seq_count = mesh.shape["seq"]
    sub_count = HEADS // exp_count
    grid = mesh.devices.reshape(seq_count // sub_count, sub_count, exp_count // 2, 2)
    split_mesh = Mesh(grid, ("sh", "sl", "zl", "co"))
    return jax.shard_map(
        body,
        mesh=split_mesh,
        in_specs=(
            P(),
            P(SEQ, EXP),
            P(SEQ, EXP),
            P(SEQ, EXP),
            P(EXP, None),
            P(SEQ, None),
            P(),
            P(None, None, EXP),
            P(EXP, None),
            P(),
            P(SEQ, None, None, EXP),
            P(SEQ, EXP, None),
            P(SEQ, None),
            P(SEQ, None),
        ),
        out_specs=(P(("sh", "sl", "zl", "co"), None), P(("sh", "sl", "zl", "co"), None), P(SEQ, EXP)),
        check_vma=False,
    )
```

```python
import math

import jax
import jax.numpy as jnp
from jax import lax
from jax.sharding import Mesh, PartitionSpec as P
from jax.experimental import pallas as pl
from jax.experimental.pallas import tpu as pltpu

HD = 128
HEADS = 16
MOST = 6144
TOPK = 4
SLOTS = 64
CAP = 32


rope_base = 1000000.0
neg_fill = -1e30
norm_eps = 1e-06


KEY_TILE = 512


def flash_kernel(bounds_ref, q_ref, k_ref, v_ref, qseg_ref, kseg_ref, o_ref, m_sc, l_sc, acc_sc):
    step = pl.program_id(0)
    first_chunk = bounds_ref[0]
    end_chunk = bounds_ref[1]
    query_first = bounds_ref[2]
    chunk = first_chunk + step
    rows = q_ref.shape[0]
    heads = q_ref.shape[1] // HD

    @pl.when(step == 0)
    def _():
        m_sc[...] = jnp.full(m_sc.shape, neg_fill, jnp.float32)
        l_sc[...] = jnp.zeros(l_sc.shape, jnp.float32)
        acc_sc[...] = jnp.zeros(acc_sc.shape, jnp.float32)

    def accumulate(visible):
        score_scale = 1.0 / math.sqrt(HD)
        for h in range(heads):
            cols = slice(h * HD, (h + 1) * HD)
            scores = (
                lax.dot_general(
                    q_ref[:, cols], k_ref[:, cols], (((1,), (1,)), ((), ())),
                    preferred_element_type=jnp.float32,
                )
                * score_scale
            )
            m_old = m_sc[h]
            if visible is None:
                m_new = jnp.maximum(m_old, jnp.max(scores, axis=1, keepdims=True))
                weights_f = jnp.exp(scores - m_new)
            else:
                m_new = jnp.maximum(
                    m_old, jnp.max(jnp.where(visible, scores, neg_fill), axis=1, keepdims=True)
                )
                weights_f = jnp.where(visible, jnp.exp(scores - m_new), 0.0)
            rescale = jnp.exp(m_old - m_new)
            l_sc[h] = l_sc[h] * rescale + jnp.sum(weights_f, axis=1, keepdims=True)
            acc_sc[h] = acc_sc[h] * rescale + jnp.dot(
                weights_f.astype(jnp.bfloat16), v_ref[:, cols], preferred_element_type=jnp.float32
            )
            m_sc[h] = m_new

    whole = (chunk >= bounds_ref[3]) & (chunk < bounds_ref[4])

    @pl.when((chunk < end_chunk) & whole)
    def _():
        accumulate(None)

    @pl.when((chunk < end_chunk) & jnp.logical_not(whole))
    def _():
        key_pos = chunk * KEY_TILE + lax.broadcasted_iota(jnp.int32, (1, KEY_TILE), 1)
        query_pos = query_first + lax.broadcasted_iota(jnp.int32, (rows, 1), 0)
        accumulate((key_pos <= query_pos) & (kseg_ref[...] == qseg_ref[...]))

    @pl.when(step == pl.num_programs(0) - 1)
    def _():
        for h in range(heads):
            o_ref[:, h * HD:(h + 1) * HD] = (acc_sc[h] / l_sc[h]).astype(o_ref.dtype)


def flash_attention(rotated_q, key_all, value_all, query_seg, segment_ids, query_first, seg_first):
    rows, width = rotated_q.shape
    heads = width // HD
    key_count = key_all.shape[0]
    chunks = key_count // KEY_TILE
    first_chunk = seg_first // KEY_TILE
    end_chunk = (query_first + rows + KEY_TILE - 1) // KEY_TILE
    last_start = jnp.sum((segment_ids < query_seg[rows - 1]).astype(jnp.int32))
    whole_first = (last_start + KEY_TILE - 1) // KEY_TILE
    whole_end = (query_first + 1) // KEY_TILE
    bounds = jnp.stack([first_chunk, end_chunk, query_first, whole_first, whole_end]).astype(
        jnp.int32
    )

    def kv_map(c, b):
        return (jnp.minimum(b[0] + c, b[1] - 1), 0)

    def kseg_map(c, b):
        return (0, jnp.minimum(b[0] + c, b[1] - 1))

    grid_spec = pltpu.PrefetchScalarGridSpec(
        num_scalar_prefetch=1,
        grid=(chunks,),
        in_specs=[
            pl.BlockSpec((rows, width), lambda c, b: (0, 0)),
            pl.BlockSpec((KEY_TILE, width), kv_map),
            pl.BlockSpec((KEY_TILE, width), kv_map),
            pl.BlockSpec((rows, 1), lambda c, b: (0, 0)),
            pl.BlockSpec((1, KEY_TILE), kseg_map),
        ],
        out_specs=pl.BlockSpec((rows, width), lambda c, b: (0, 0)),
        scratch_shapes=[
            pltpu.VMEM((heads, rows, 1), jnp.float32),
            pltpu.VMEM((heads, rows, 1), jnp.float32),
            pltpu.VMEM((heads, rows, HD), jnp.float32),
        ],
    )
    flops = 4 * rows * key_count * width
    return pl.pallas_call(
        flash_kernel,
        grid_spec=grid_spec,
        out_shape=jax.ShapeDtypeStruct((rows, width), jnp.bfloat16),
        compiler_params=pltpu.CompilerParams(
            dimension_semantics=("arbitrary",), vmem_limit_bytes=48 * 1024 * 1024
        ),
        cost_estimate=pl.CostEstimate(
            flops=flops,
            transcendentals=rows * key_count * heads,
            bytes_accessed=2 * key_count * width * 2 + 2 * rows * width * 2,
        ),
    )(
        bounds,
        rotated_q,
        key_all,
        value_all,
        query_seg.reshape(rows, 1).astype(jnp.int32),
        segment_ids.reshape(1, key_count).astype(jnp.int32),
    )


def shifted_copies(x, axis_name, count):
    moved = [x]
    for shift in range(1, count):
        pairs = [(i, (i + shift) % count) for i in range(count)]
        moved.append(lax.ppermute(x, axis_name, pairs))
    return moved


def sum_by_permutes(x, axis_name, count):
    total = x.astype(jnp.float32)
    for part in shifted_copies(x, axis_name, count)[1:]:
        total = total + part.astype(jnp.float32)
    return total


def causal_copies(x, axis_name, count, reach):
    moved = [x]
    for shift in range(1, count):
        pairs = [(i, i + shift) for i in range(count - shift)] if shift <= reach else []
        moved.append(lax.ppermute(x, axis_name, pairs) if pairs else jnp.zeros_like(x))
    return moved


def sum_over_chip_pairs(x):
    half = x.shape[1] // 2
    core = lax.axis_index("co")
    swap = [(0, 1), (1, 0)]
    pair = x.astype(jnp.float32) + lax.ppermute(x, "co", swap).astype(jnp.float32)
    mine = lax.dynamic_slice_in_dim(pair, core * half, half, 1).astype(jnp.bfloat16)
    done = (mine.astype(jnp.float32) + lax.ppermute(mine, "zl", swap).astype(jnp.float32)).astype(
        jnp.bfloat16
    )
    other = lax.ppermute(done, "co", swap)
    whole = jnp.where(
        core == 0, jnp.concatenate([done, other], axis=1), jnp.concatenate([other, done], axis=1)
    )
    return whole.astype(jnp.float32)


def gather_by_permutes(x, axis_name, count, place, reach):
    moved = causal_copies(x, axis_name, count, reach)
    reverse = jnp.stack([moved[0]] + moved[1:][::-1])
    return jnp.roll(reverse, place, axis=0)


def token_positions(segment_ids):
    stream_len = segment_ids.shape[0]
    token_index = jnp.arange(stream_len, dtype=jnp.int32)
    boundary = jnp.concatenate([jnp.ones((1,), jnp.bool_), segment_ids[1:] != segment_ids[:-1]])
    seg_start = lax.cummax(jnp.where(boundary, token_index, 0), axis=0)
    return (token_index - seg_start, seg_start)


def rotate(values_in, positions, head_count):
    half_dim = HD // 2
    frequency = rope_base ** (-(2.0 * jnp.arange(half_dim, dtype=jnp.float32)) / HD)
    angle_all = positions.astype(jnp.float32)[:, None] * frequency[None, :]
    cosine = jnp.cos(angle_all)[:, None, :]
    sine_part = jnp.sin(angle_all)[:, None, :]
    shaped = values_in.astype(jnp.float32).reshape(values_in.shape[0], head_count, HD)
    first_half = shaped[..., :half_dim]
    second_half = shaped[..., half_dim:]
    turned = jnp.concatenate(
        [
            first_half * cosine - second_half * sine_part,
            second_half * cosine + first_half * sine_part,
        ],
        axis=-1,
    )
    return turned.reshape(values_in.shape[0], head_count * HD).astype(jnp.bfloat16)


def rms_norm(hidden_in, norm_gain):
    mean_square = jnp.mean(hidden_in * hidden_in, axis=-1, keepdims=True)
    return (hidden_in * lax.rsqrt(mean_square + norm_eps) * norm_gain.astype(jnp.float32)).astype(
        jnp.bfloat16
    )


def expert_parts(incoming, expert_in, expert_out):
    expert_pre = jnp.einsum(
        "nscd,sgde->nscge", incoming, expert_in, preferred_element_type=jnp.float32
    )
    expert_hidden = (jax.nn.silu(expert_pre[..., 0, :]) * expert_pre[..., 1, :]).astype(
        jnp.bfloat16
    )
    return jnp.einsum(
        "nsce,sed->nscd", expert_hidden, expert_out, preferred_element_type=jnp.float32
    ).astype(jnp.bfloat16)


def body(
    segment_ids,
    queries,
    keys,
    values,
    out_weight,
    residual,
    norm_gain,
    shared_in,
    shared_out,
    shared_gate,
    expert_in,
    expert_out,
    expert_ids,
    gate_weights,
):
    seq_count = lax.axis_size("sh") * lax.axis_size("sl")
    exp_count = lax.axis_size("zl") * lax.axis_size("co")
    group_place = lax.axis_index("sh")
    sub_count = lax.axis_size("sl")
    seq_place = group_place * sub_count + lax.axis_index("sl")
    exp_place = lax.axis_index("zl") * lax.axis_size("co") + lax.axis_index("co")
    block_len = queries.shape[0]
    local_heads = queries.shape[1] // HD
    block_first = seq_place * block_len
    query_seg = lax.dynamic_slice_in_dim(segment_ids, block_first, block_len, 0)
    local_start = jnp.sum((segment_ids[None, :] < query_seg[:, None]).astype(jnp.int32), axis=1)
    local_pos = block_first + jnp.arange(block_len, dtype=jnp.int32) - local_start
    rotated_q = rotate(queries, local_pos, local_heads)
    key_cache = rotate(keys, local_pos, local_heads)
    stacked = jnp.stack([rotated_q, key_cache, values]).reshape(3, block_len, local_heads, HD)
    moved = lax.all_to_all(stacked, "sl", split_axis=2, concat_axis=1, tiled=True)
    span = block_len * sub_count
    head_q = moved[0].reshape(span, HD)
    head_kv = moved[1:].reshape(2, span, HD)
    group_count = lax.axis_size("sh")
    reach = -(-(MOST + span - 1) // span) - 1
    gathered = gather_by_permutes(head_kv, "sh", group_count, group_place, reach)
    gathered = jnp.moveaxis(gathered, 0, 1).reshape(2, group_count * span, HD)
    span_first = group_place * span
    span_seg = lax.dynamic_slice_in_dim(segment_ids, span_first, span, 0)
    seg_first = jnp.sum((segment_ids < span_seg[0]).astype(jnp.int32))
    head_out = flash_attention(
        head_q, gathered[0], gathered[1], span_seg, segment_ids, span_first, seg_first
    )
    attended = lax.all_to_all(
        head_out.reshape(sub_count, block_len, 1, HD), "sl", split_axis=0, concat_axis=2, tiled=True
    ).reshape(block_len, local_heads * HD)
    attn_part = jnp.dot(attended, out_weight, preferred_element_type=jnp.float32)
    row_count = block_len // exp_count
    row_first = exp_place * row_count
    residual_f = residual.astype(jnp.float32)
    attn_sum = sum_over_chip_pairs(attn_part.astype(jnp.bfloat16))
    after_attn = residual_f + attn_sum
    normed = rms_norm(after_attn, norm_gain)
    attn_rows = lax.dynamic_slice_in_dim(attn_sum, row_first, row_count, 0).astype(jnp.bfloat16)
    after_rows = lax.dynamic_slice_in_dim(after_attn, row_first, row_count, 0)
    shared_pre = jnp.einsum("td,gde->tge", normed, shared_in, preferred_element_type=jnp.float32)
    shared_hidden = (jax.nn.silu(shared_pre[:, 0]) * shared_pre[:, 1]).astype(jnp.bfloat16)
    shared_term = jnp.dot(shared_hidden, shared_out, preferred_element_type=jnp.float32)
    shared_factor = jax.nn.sigmoid(jnp.dot(normed, shared_gate, preferred_element_type=jnp.float32))
    flat_ids = expert_ids.reshape(-1)
    flat_index = jnp.arange(flat_ids.shape[0], dtype=jnp.int32)
    earlier_same = (flat_ids[None, :] == flat_ids[:, None]) & (flat_index[None, :] < flat_index[:, None])
    slot_rank = jnp.sum(earlier_same.astype(jnp.int32), axis=1)
    slot_place = flat_ids * CAP + slot_rank
    slot_local = SLOTS // seq_count
    model_width = normed.shape[1]
    core_count = lax.axis_size("co")
    col_count = model_width // core_count
    col_first = lax.axis_index("co") * col_count
    slot_rows = jnp.arange(SLOTS * CAP, dtype=jnp.int32)
    place_hit = (slot_place[None, :] == slot_rows[:, None]).reshape(SLOTS * CAP, block_len, TOPK)
    dispatch = jnp.any(place_hit, axis=2).astype(jnp.bfloat16)
    normed_part = lax.dynamic_slice_in_dim(normed, col_first, col_count, 1)
    outgoing_part = (
        jnp.dot(dispatch, normed_part, preferred_element_type=jnp.float32)
        .astype(jnp.bfloat16)
        .reshape(seq_count, slot_local, CAP, col_count)
    )
    incoming = lax.all_gather(
        lax.all_to_all(outgoing_part, SEQ, split_axis=0, concat_axis=0, tiled=True),
        "co",
        axis=3,
        tiled=True,
    )
    expert_part = expert_parts(incoming, expert_in, expert_out)
    summed = lax.psum_scatter(expert_part, "co", scatter_dimension=3, tiled=True).astype(
        jnp.float32
    )
    returned = lax.all_to_all(
        summed.astype(jnp.bfloat16), SEQ, split_axis=0, concat_axis=0, tiled=True
    ).astype(summed.dtype)
    select_rows = (slot_place[:, None] == slot_rows[None, :]).astype(jnp.bfloat16)
    picked = jnp.dot(
        select_rows,
        returned.reshape(SLOTS * CAP, col_count).astype(jnp.bfloat16),
        preferred_element_type=jnp.float32,
    ).reshape(block_len, TOPK, col_count)
    moe_cols = jnp.sum(gate_weights[:, :, None] * picked, axis=1)
    moe_term = lax.dynamic_update_slice_in_dim(
        jnp.zeros((block_len, model_width), jnp.float32), moe_cols, col_first, 1
    )
    combined = shared_factor[:, None] * shared_term + moe_term
    moe_rows = lax.psum_scatter(
        combined.astype(jnp.bfloat16), EXP, scatter_dimension=0, tiled=True
    ).astype(jnp.float32)
    mixed_out = (after_rows + moe_rows).astype(jnp.bfloat16)
    return (mixed_out, attn_rows, key_cache)


SEQ = ("sh", "sl")
EXP = ("zl", "co")


def solution(mesh):
    exp_count = mesh.shape["exp"]
    seq_count = mesh.shape["seq"]
    sub_count = HEADS // exp_count
    grid = mesh.devices.reshape(seq_count // sub_count, sub_count, exp_count // 2, 2)
    split_mesh = Mesh(grid, ("sh", "sl", "zl", "co"))
    return jax.shard_map(
        body,
        mesh=split_mesh,
        in_specs=(
            P(),
            P(SEQ, EXP),
            P(SEQ, EXP),
            P(SEQ, EXP),
            P(EXP, None),
            P(SEQ, None),
            P(),
            P(None, None, EXP),
            P(EXP, None),
            P(),
            P(SEQ, None, None, EXP),
            P(SEQ, EXP, None),
            P(SEQ, None),
            P(SEQ, None),
        ),
        out_specs=(P(("sh", "sl", "zl", "co"), None), P(("sh", "sl", "zl", "co"), None), P(SEQ, EXP)),
        check_vma=False,
    )
```

```python
import math

import jax
import jax.numpy as jnp
from jax import lax
from jax.sharding import Mesh, PartitionSpec as P
from jax.experimental import pallas as pl
from jax.experimental.pallas import tpu as pltpu

HD = 128
HEADS = 16
MOST = 6144
TOPK = 4
SLOTS = 64
CAP = 32


rope_base = 1000000.0
neg_fill = -1e30
norm_eps = 1e-06


KEY_TILE = 512


def flash_kernel(bounds_ref, q_ref, k_ref, v_ref, qseg_ref, kseg_ref, o_ref, m_sc, l_sc, acc_sc):
    step = pl.program_id(0)
    first_chunk = bounds_ref[0]
    end_chunk = bounds_ref[1]
    query_first = bounds_ref[2]
    chunk = first_chunk + step
    rows = q_ref.shape[0]
    heads = q_ref.shape[1] // HD

    @pl.when(step == 0)
    def _():
        m_sc[...] = jnp.full(m_sc.shape, neg_fill, jnp.float32)
        l_sc[...] = jnp.zeros(l_sc.shape, jnp.float32)
        acc_sc[...] = jnp.zeros(acc_sc.shape, jnp.float32)

    @pl.when(chunk < end_chunk)
    def _():
        key_pos = chunk * KEY_TILE + lax.broadcasted_iota(jnp.int32, (1, KEY_TILE), 1)
        query_pos = query_first + lax.broadcasted_iota(jnp.int32, (rows, 1), 0)
        visible = (key_pos <= query_pos) & (kseg_ref[...] == qseg_ref[...])
        score_scale = 1.0 / math.sqrt(HD)
        for h in range(heads):
            cols = slice(h * HD, (h + 1) * HD)
            scores = (
                lax.dot_general(
                    q_ref[:, cols], k_ref[:, cols], (((1,), (1,)), ((), ())),
                    preferred_element_type=jnp.float32,
                )
                * score_scale
            )
            m_old = m_sc[h]
            m_new = jnp.maximum(
                m_old, jnp.max(jnp.where(visible, scores, neg_fill), axis=1, keepdims=True)
            )
            weights_f = jnp.where(visible, jnp.exp(scores - m_new), 0.0)
            rescale = jnp.exp(m_old - m_new)
            l_sc[h] = l_sc[h] * rescale + jnp.sum(weights_f, axis=1, keepdims=True)
            acc_sc[h] = acc_sc[h] * rescale + jnp.dot(
                weights_f.astype(jnp.bfloat16), v_ref[:, cols], preferred_element_type=jnp.float32
            )
            m_sc[h] = m_new

    @pl.when(step == pl.num_programs(0) - 1)
    def _():
        for h in range(heads):
            o_ref[:, h * HD:(h + 1) * HD] = (acc_sc[h] / l_sc[h]).astype(o_ref.dtype)


def flash_attention(rotated_q, key_all, value_all, query_seg, segment_ids, query_first, seg_first):
    rows, width = rotated_q.shape
    heads = width // HD
    key_count = key_all.shape[0]
    chunks = key_count // KEY_TILE
    first_chunk = seg_first // KEY_TILE
    end_chunk = (query_first + rows + KEY_TILE - 1) // KEY_TILE
    bounds = jnp.stack([first_chunk, end_chunk, query_first]).astype(jnp.int32)

    def kv_map(c, b):
        return (jnp.minimum(b[0] + c, b[1] - 1), 0)

    def kseg_map(c, b):
        return (0, jnp.minimum(b[0] + c, b[1] - 1))

    grid_spec = pltpu.PrefetchScalarGridSpec(
        num_scalar_prefetch=1,
        grid=(chunks,),
        in_specs=[
            pl.BlockSpec((rows, width), lambda c, b: (0, 0)),
            pl.BlockSpec((KEY_TILE, width), kv_map),
            pl.BlockSpec((KEY_TILE, width), kv_map),
            pl.BlockSpec((rows, 1), lambda c, b: (0, 0)),
            pl.BlockSpec((1, KEY_TILE), kseg_map),
        ],
        out_specs=pl.BlockSpec((rows, width), lambda c, b: (0, 0)),
        scratch_shapes=[
            pltpu.VMEM((heads, rows, 1), jnp.float32),
            pltpu.VMEM((heads, rows, 1), jnp.float32),
            pltpu.VMEM((heads, rows, HD), jnp.float32),
        ],
    )
    flops = 4 * rows * key_count * width
    return pl.pallas_call(
        flash_kernel,
        grid_spec=grid_spec,
        out_shape=jax.ShapeDtypeStruct((rows, width), jnp.bfloat16),
        compiler_params=pltpu.CompilerParams(
            dimension_semantics=("arbitrary",), vmem_limit_bytes=48 * 1024 * 1024
        ),
        cost_estimate=pl.CostEstimate(
            flops=flops,
            transcendentals=rows * key_count * heads,
            bytes_accessed=2 * key_count * width * 2 + 2 * rows * width * 2,
        ),
    )(
        bounds,
        rotated_q,
        key_all,
        value_all,
        query_seg.reshape(rows, 1).astype(jnp.int32),
        segment_ids.reshape(1, key_count).astype(jnp.int32),
    )


def shifted_copies(x, axis_name, count):
    moved = [x]
    for shift in range(1, count):
        pairs = [(i, (i + shift) % count) for i in range(count)]
        moved.append(lax.ppermute(x, axis_name, pairs))
    return moved


def sum_by_permutes(x, axis_name, count):
    total = x.astype(jnp.float32)
    for part in shifted_copies(x, axis_name, count)[1:]:
        total = total + part.astype(jnp.float32)
    return total


def causal_copies(x, axis_name, count, reach):
    moved = [x]
    for shift in range(1, count):
        pairs = [(i, i + shift) for i in range(count - shift)] if shift <= reach else []
        moved.append(lax.ppermute(x, axis_name, pairs) if pairs else jnp.zeros_like(x))
    return moved


def sum_over_chip_pairs(x):
    half = x.shape[1] // 2
    core = lax.axis_index("co")
    swap = [(0, 1), (1, 0)]
    pair = x.astype(jnp.float32) + lax.ppermute(x, "co", swap).astype(jnp.float32)
    mine = lax.dynamic_slice_in_dim(pair, core * half, half, 1).astype(jnp.bfloat16)
    done = (mine.astype(jnp.float32) + lax.ppermute(mine, "zl", swap).astype(jnp.float32)).astype(
        jnp.bfloat16
    )
    other = lax.ppermute(done, "co", swap)
    whole = jnp.where(
        core == 0, jnp.concatenate([done, other], axis=1), jnp.concatenate([other, done], axis=1)
    )
    return whole.astype(jnp.float32)


def gather_by_permutes(x, axis_name, count, place, reach):
    moved = causal_copies(x, axis_name, count, reach)
    reverse = jnp.stack([moved[0]] + moved[1:][::-1])
    return jnp.roll(reverse, place, axis=0)


def token_positions(segment_ids):
    stream_len = segment_ids.shape[0]
    token_index = jnp.arange(stream_len, dtype=jnp.int32)
    boundary = jnp.concatenate([jnp.ones((1,), jnp.bool_), segment_ids[1:] != segment_ids[:-1]])
    seg_start = lax.cummax(jnp.where(boundary, token_index, 0), axis=0)
    return (token_index - seg_start, seg_start)


def rotate(values_in, positions, head_count):
    half_dim = HD // 2
    frequency = rope_base ** (-(2.0 * jnp.arange(half_dim, dtype=jnp.float32)) / HD)
    angle_all = positions.astype(jnp.float32)[:, None] * frequency[None, :]
    cosine = jnp.cos(angle_all)[:, None, :]
    sine_part = jnp.sin(angle_all)[:, None, :]
    shaped = values_in.astype(jnp.float32).reshape(values_in.shape[0], head_count, HD)
    first_half = shaped[..., :half_dim]
    second_half = shaped[..., half_dim:]
    turned = jnp.concatenate(
        [
            first_half * cosine - second_half * sine_part,
            second_half * cosine + first_half * sine_part,
        ],
        axis=-1,
    )
    return turned.reshape(values_in.shape[0], head_count * HD).astype(jnp.bfloat16)


def rms_norm(hidden_in, norm_gain):
    mean_square = jnp.mean(hidden_in * hidden_in, axis=-1, keepdims=True)
    return (hidden_in * lax.rsqrt(mean_square + norm_eps) * norm_gain.astype(jnp.float32)).astype(
        jnp.bfloat16
    )


def expert_parts(incoming, expert_in, expert_out):
    expert_pre = jnp.einsum(
        "nscd,sgde->nscge", incoming, expert_in, preferred_element_type=jnp.float32
    )
    expert_hidden = (jax.nn.silu(expert_pre[..., 0, :]) * expert_pre[..., 1, :]).astype(
        jnp.bfloat16
    )
    return jnp.einsum(
        "nsce,sed->nscd", expert_hidden, expert_out, preferred_element_type=jnp.float32
    ).astype(jnp.bfloat16)


def body(
    segment_ids,
    queries,
    keys,
    values,
    out_weight,
    residual,
    norm_gain,
    shared_in,
    shared_out,
    shared_gate,
    expert_in,
    expert_out,
    expert_ids,
    gate_weights,
):
    seq_count = lax.axis_size("sh") * lax.axis_size("sl")
    exp_count = lax.axis_size("zl") * lax.axis_size("co")
    group_place = lax.axis_index("sh")
    sub_count = lax.axis_size("sl")
    seq_place = group_place * sub_count + lax.axis_index("sl")
    exp_place = lax.axis_index("zl") * lax.axis_size("co") + lax.axis_index("co")
    block_len = queries.shape[0]
    local_heads = queries.shape[1] // HD
    block_first = seq_place * block_len
    query_seg = lax.dynamic_slice_in_dim(segment_ids, block_first, block_len, 0)
    local_start = jnp.sum((segment_ids[None, :] < query_seg[:, None]).astype(jnp.int32), axis=1)
    local_pos = block_first + jnp.arange(block_len, dtype=jnp.int32) - local_start
    rotated_q = rotate(queries, local_pos, local_heads)
    key_cache = rotate(keys, local_pos, local_heads)
    sub_heads = (block_len, local_heads, HD)
    span = block_len * sub_count
    group_count = lax.axis_size("sh")
    reach = -(-(MOST + span - 1) // span) - 1
    value_moved = lax.all_to_all(
        values.reshape(sub_heads), "sl", split_axis=1, concat_axis=0, tiled=True
    ).reshape(span, HD)
    value_all = gather_by_permutes(value_moved, "sh", group_count, group_place, reach)
    stacked = jnp.stack([rotated_q, key_cache]).reshape((2,) + sub_heads)
    moved = lax.all_to_all(stacked, "sl", split_axis=2, concat_axis=1, tiled=True)
    head_q = moved[0].reshape(span, HD)
    key_all = gather_by_permutes(moved[1].reshape(span, HD), "sh", group_count, group_place, reach)
    span_first = group_place * span
    span_seg = lax.dynamic_slice_in_dim(segment_ids, span_first, span, 0)
    seg_first = jnp.sum((segment_ids < span_seg[0]).astype(jnp.int32))
    head_out = flash_attention(
        head_q,
        key_all.reshape(group_count * span, HD),
        value_all.reshape(group_count * span, HD),
        span_seg,
        segment_ids,
        span_first,
        seg_first,
    )
    attended = lax.all_to_all(
        head_out.reshape(sub_count, block_len, 1, HD), "sl", split_axis=0, concat_axis=2, tiled=True
    ).reshape(block_len, local_heads * HD)
    attn_part = jnp.dot(attended, out_weight, preferred_element_type=jnp.float32)
    row_count = block_len // exp_count
    row_first = exp_place * row_count
    residual_f = residual.astype(jnp.float32)
    attn_sum = sum_over_chip_pairs(attn_part.astype(jnp.bfloat16))
    after_attn = residual_f + attn_sum
    normed = rms_norm(after_attn, norm_gain)
    attn_rows = lax.dynamic_slice_in_dim(attn_sum, row_first, row_count, 0).astype(jnp.bfloat16)
    after_rows = lax.dynamic_slice_in_dim(after_attn, row_first, row_count, 0)
    shared_pre = jnp.einsum("td,gde->tge", normed, shared_in, preferred_element_type=jnp.float32)
    shared_hidden = (jax.nn.silu(shared_pre[:, 0]) * shared_pre[:, 1]).astype(jnp.bfloat16)
    shared_term = jnp.dot(shared_hidden, shared_out, preferred_element_type=jnp.float32)
    shared_factor = jax.nn.sigmoid(jnp.dot(normed, shared_gate, preferred_element_type=jnp.float32))
    flat_ids = expert_ids.reshape(-1)
    flat_index = jnp.arange(flat_ids.shape[0], dtype=jnp.int32)
    earlier_same = (flat_ids[None, :] == flat_ids[:, None]) & (flat_index[None, :] < flat_index[:, None])
    slot_rank = jnp.sum(earlier_same.astype(jnp.int32), axis=1)
    slot_place = flat_ids * CAP + slot_rank
    slot_local = SLOTS // seq_count
    model_width = normed.shape[1]
    core_count = lax.axis_size("co")
    col_count = model_width // core_count
    col_first = lax.axis_index("co") * col_count
    slot_rows = jnp.arange(SLOTS * CAP, dtype=jnp.int32)
    place_hit = (slot_place[None, :] == slot_rows[:, None]).reshape(SLOTS * CAP, block_len, TOPK)
    dispatch = jnp.any(place_hit, axis=2).astype(jnp.bfloat16)
    normed_part = lax.dynamic_slice_in_dim(normed, col_first, col_count, 1)
    outgoing_part = (
        jnp.dot(dispatch, normed_part, preferred_element_type=jnp.float32)
        .astype(jnp.bfloat16)
        .reshape(seq_count, slot_local, CAP, col_count)
    )
    incoming = lax.all_gather(
        lax.all_to_all(outgoing_part, SEQ, split_axis=0, concat_axis=0, tiled=True),
        "co",
        axis=3,
        tiled=True,
    )
    expert_part = expert_parts(incoming, expert_in, expert_out)
    summed = lax.psum_scatter(expert_part, "co", scatter_dimension=3, tiled=True).astype(
        jnp.float32
    )
    returned = lax.all_to_all(
        summed.astype(jnp.bfloat16), SEQ, split_axis=0, concat_axis=0, tiled=True
    ).astype(summed.dtype)
    select_rows = (slot_place[:, None] == slot_rows[None, :]).astype(jnp.bfloat16)
    picked = jnp.dot(
        select_rows,
        returned.reshape(SLOTS * CAP, col_count).astype(jnp.bfloat16),
        preferred_element_type=jnp.float32,
    ).reshape(block_len, TOPK, col_count)
    moe_cols = jnp.sum(gate_weights[:, :, None] * picked, axis=1)
    moe_term = lax.dynamic_update_slice_in_dim(
        jnp.zeros((block_len, model_width), jnp.float32), moe_cols, col_first, 1
    )
    combined = shared_factor[:, None] * shared_term + moe_term
    moe_rows = lax.psum_scatter(
        combined.astype(jnp.bfloat16), EXP, scatter_dimension=0, tiled=True
    ).astype(jnp.float32)
    mixed_out = (after_rows + moe_rows).astype(jnp.bfloat16)
    return (mixed_out, attn_rows, key_cache)


SEQ = ("sh", "sl")
EXP = ("zl", "co")


def solution(mesh):
    exp_count = mesh.shape["exp"]
    seq_count = mesh.shape["seq"]
    sub_count = HEADS // exp_count
    grid = mesh.devices.reshape(seq_count // sub_count, sub_count, exp_count // 2, 2)
    split_mesh = Mesh(grid, ("sh", "sl", "zl", "co"))
    return jax.shard_map(
        body,
        mesh=split_mesh,
        in_specs=(
            P(),
            P(SEQ, EXP),
            P(SEQ, EXP),
            P(SEQ, EXP),
            P(EXP, None),
            P(SEQ, None),
            P(),
            P(None, None, EXP),
            P(EXP, None),
            P(),
            P(SEQ, None, None, EXP),
            P(SEQ, EXP, None),
            P(SEQ, None),
            P(SEQ, None),
        ),
        out_specs=(P(("sh", "sl", "zl", "co"), None), P(("sh", "sl", "zl", "co"), None), P(SEQ, EXP)),
        check_vma=False,
    )
```

```python
import math

import jax
import jax.numpy as jnp
from jax import lax
from jax.sharding import Mesh, PartitionSpec as P
from jax.experimental import pallas as pl
from jax.experimental.pallas import tpu as pltpu

HD = 128
HEADS = 16
MOST = 6144
TOPK = 4
SLOTS = 64
CAP = 32


rope_base = 1000000.0
neg_fill = -1e30
norm_eps = 1e-06


KEY_TILE = 512


def flash_kernel(bounds_ref, q_ref, k_ref, v_ref, qseg_ref, kseg_ref, o_ref, m_sc, l_sc, acc_sc):
    step = pl.program_id(0)
    first_chunk = bounds_ref[0]
    end_chunk = bounds_ref[1]
    query_first = bounds_ref[2]
    chunk = first_chunk + step
    rows = q_ref.shape[0]
    heads = q_ref.shape[1] // HD

    @pl.when(step == 0)
    def _():
        m_sc[...] = jnp.full(m_sc.shape, neg_fill, jnp.float32)
        l_sc[...] = jnp.zeros(l_sc.shape, jnp.float32)
        acc_sc[...] = jnp.zeros(acc_sc.shape, jnp.float32)

    @pl.when(chunk < end_chunk)
    def _():
        key_pos = chunk * KEY_TILE + lax.broadcasted_iota(jnp.int32, (1, KEY_TILE), 1)
        query_pos = query_first + lax.broadcasted_iota(jnp.int32, (rows, 1), 0)
        visible = (key_pos <= query_pos) & (kseg_ref[...] == qseg_ref[...])
        score_scale = 1.0 / math.sqrt(HD)
        for h in range(heads):
            cols = slice(h * HD, (h + 1) * HD)
            scores = (
                lax.dot_general(
                    q_ref[:, cols], k_ref[:, cols], (((1,), (1,)), ((), ())),
                    preferred_element_type=jnp.float32,
                )
                * score_scale
            )
            m_old = m_sc[h]
            m_new = jnp.maximum(
                m_old, jnp.max(jnp.where(visible, scores, neg_fill), axis=1, keepdims=True)
            )
            weights_f = jnp.where(visible, jnp.exp(scores - m_new), 0.0)
            rescale = jnp.exp(m_old - m_new)
            l_sc[h] = l_sc[h] * rescale + jnp.sum(weights_f, axis=1, keepdims=True)
            acc_sc[h] = acc_sc[h] * rescale + jnp.dot(
                weights_f.astype(jnp.bfloat16), v_ref[:, cols], preferred_element_type=jnp.float32
            )
            m_sc[h] = m_new

    @pl.when(step == pl.num_programs(0) - 1)
    def _():
        for h in range(heads):
            o_ref[:, h * HD:(h + 1) * HD] = (acc_sc[h] / l_sc[h]).astype(o_ref.dtype)


def flash_attention(
    rotated_q, key_all, value_all, query_seg, segment_ids, query_first, seg_first, place, groups
):
    rows, width = rotated_q.shape
    heads = width // HD
    key_count = key_all.shape[0]
    chunks = key_count // KEY_TILE
    first_chunk = seg_first // KEY_TILE
    end_chunk = (query_first + rows + KEY_TILE - 1) // KEY_TILE
    bounds = jnp.stack([first_chunk, end_chunk, query_first, place]).astype(jnp.int32)
    per_group = chunks // groups

    def kv_map(c, b):
        chunk = jnp.minimum(b[0] + c, b[1] - 1)
        turned = (chunk // per_group - b[3] + groups) % groups
        return (turned * per_group + chunk % per_group, 0)

    def kseg_map(c, b):
        return (0, jnp.minimum(b[0] + c, b[1] - 1))

    grid_spec = pltpu.PrefetchScalarGridSpec(
        num_scalar_prefetch=1,
        grid=(chunks,),
        in_specs=[
            pl.BlockSpec((rows, width), lambda c, b: (0, 0)),
            pl.BlockSpec((KEY_TILE, width), kv_map),
            pl.BlockSpec((KEY_TILE, width), kv_map),
            pl.BlockSpec((rows, 1), lambda c, b: (0, 0)),
            pl.BlockSpec((1, KEY_TILE), kseg_map),
        ],
        out_specs=pl.BlockSpec((rows, width), lambda c, b: (0, 0)),
        scratch_shapes=[
            pltpu.VMEM((heads, rows, 1), jnp.float32),
            pltpu.VMEM((heads, rows, 1), jnp.float32),
            pltpu.VMEM((heads, rows, HD), jnp.float32),
        ],
    )
    flops = 4 * rows * key_count * width
    return pl.pallas_call(
        flash_kernel,
        grid_spec=grid_spec,
        out_shape=jax.ShapeDtypeStruct((rows, width), jnp.bfloat16),
        compiler_params=pltpu.CompilerParams(
            dimension_semantics=("arbitrary",), vmem_limit_bytes=48 * 1024 * 1024
        ),
        cost_estimate=pl.CostEstimate(
            flops=flops,
            transcendentals=rows * key_count * heads,
            bytes_accessed=2 * key_count * width * 2 + 2 * rows * width * 2,
        ),
    )(
        bounds,
        rotated_q,
        key_all,
        value_all,
        query_seg.reshape(rows, 1).astype(jnp.int32),
        segment_ids.reshape(1, key_count).astype(jnp.int32),
    )


def shifted_copies(x, axis_name, count):
    moved = [x]
    for shift in range(1, count):
        pairs = [(i, (i + shift) % count) for i in range(count)]
        moved.append(lax.ppermute(x, axis_name, pairs))
    return moved


def sum_by_permutes(x, axis_name, count):
    total = x.astype(jnp.float32)
    for part in shifted_copies(x, axis_name, count)[1:]:
        total = total + part.astype(jnp.float32)
    return total


def causal_copies(x, axis_name, count, reach):
    moved = [x]
    for shift in range(1, count):
        pairs = [(i, i + shift) for i in range(count - shift)] if shift <= reach else []
        moved.append(lax.ppermute(x, axis_name, pairs) if pairs else jnp.zeros_like(x))
    return moved


def sum_over_chip_pairs(x):
    half = x.shape[1] // 2
    core = lax.axis_index("co")
    swap = [(0, 1), (1, 0)]
    pair = x.astype(jnp.float32) + lax.ppermute(x, "co", swap).astype(jnp.float32)
    mine = lax.dynamic_slice_in_dim(pair, core * half, half, 1).astype(jnp.bfloat16)
    done = (mine.astype(jnp.float32) + lax.ppermute(mine, "zl", swap).astype(jnp.float32)).astype(
        jnp.bfloat16
    )
    other = lax.ppermute(done, "co", swap)
    whole = jnp.where(
        core == 0, jnp.concatenate([done, other], axis=1), jnp.concatenate([other, done], axis=1)
    )
    return whole.astype(jnp.float32)


def gather_by_permutes(x, axis_name, count, place, reach):
    moved = causal_copies(x, axis_name, count, reach)
    return jnp.stack([moved[0]] + moved[1:][::-1])


def token_positions(segment_ids):
    stream_len = segment_ids.shape[0]
    token_index = jnp.arange(stream_len, dtype=jnp.int32)
    boundary = jnp.concatenate([jnp.ones((1,), jnp.bool_), segment_ids[1:] != segment_ids[:-1]])
    seg_start = lax.cummax(jnp.where(boundary, token_index, 0), axis=0)
    return (token_index - seg_start, seg_start)


def rotate(values_in, positions, head_count):
    half_dim = HD // 2
    frequency = rope_base ** (-(2.0 * jnp.arange(half_dim, dtype=jnp.float32)) / HD)
    angle_all = positions.astype(jnp.float32)[:, None] * frequency[None, :]
    cosine = jnp.cos(angle_all)[:, None, :]
    sine_part = jnp.sin(angle_all)[:, None, :]
    shaped = values_in.astype(jnp.float32).reshape(values_in.shape[0], head_count, HD)
    first_half = shaped[..., :half_dim]
    second_half = shaped[..., half_dim:]
    turned = jnp.concatenate(
        [
            first_half * cosine - second_half * sine_part,
            second_half * cosine + first_half * sine_part,
        ],
        axis=-1,
    )
    return turned.reshape(values_in.shape[0], head_count * HD).astype(jnp.bfloat16)


def rms_norm(hidden_in, norm_gain):
    mean_square = jnp.mean(hidden_in * hidden_in, axis=-1, keepdims=True)
    return (hidden_in * lax.rsqrt(mean_square + norm_eps) * norm_gain.astype(jnp.float32)).astype(
        jnp.bfloat16
    )


def expert_parts(incoming, expert_in, expert_out):
    expert_pre = jnp.einsum(
        "nscd,sgde->nscge", incoming, expert_in, preferred_element_type=jnp.float32
    )
    expert_hidden = (jax.nn.silu(expert_pre[..., 0, :]) * expert_pre[..., 1, :]).astype(
        jnp.bfloat16
    )
    return jnp.einsum(
        "nsce,sed->nscd", expert_hidden, expert_out, preferred_element_type=jnp.float32
    ).astype(jnp.bfloat16)


def body(
    segment_ids,
    queries,
    keys,
    values,
    out_weight,
    residual,
    norm_gain,
    shared_in,
    shared_out,
    shared_gate,
    expert_in,
    expert_out,
    expert_ids,
    gate_weights,
):
    seq_count = lax.axis_size("sh") * lax.axis_size("sl")
    exp_count = lax.axis_size("zl") * lax.axis_size("co")
    group_place = lax.axis_index("sh")
    sub_count = lax.axis_size("sl")
    seq_place = group_place * sub_count + lax.axis_index("sl")
    exp_place = lax.axis_index("zl") * lax.axis_size("co") + lax.axis_index("co")
    block_len = queries.shape[0]
    local_heads = queries.shape[1] // HD
    block_first = seq_place * block_len
    query_seg = lax.dynamic_slice_in_dim(segment_ids, block_first, block_len, 0)
    local_start = jnp.sum((segment_ids[None, :] < query_seg[:, None]).astype(jnp.int32), axis=1)
    local_pos = block_first + jnp.arange(block_len, dtype=jnp.int32) - local_start
    rotated_q = rotate(queries, local_pos, local_heads)
    key_cache = rotate(keys, local_pos, local_heads)
    sub_heads = (block_len, local_heads, HD)
    span = block_len * sub_count
    group_count = lax.axis_size("sh")
    reach = -(-(MOST + span - 1) // span) - 1
    value_moved = lax.all_to_all(
        values.reshape(sub_heads), "sl", split_axis=1, concat_axis=0, tiled=True
    ).reshape(span, HD)
    value_all = gather_by_permutes(value_moved, "sh", group_count, group_place, reach)
    stacked = jnp.stack([rotated_q, key_cache]).reshape((2,) + sub_heads)
    moved = lax.all_to_all(stacked, "sl", split_axis=2, concat_axis=1, tiled=True)
    head_q = moved[0].reshape(span, HD)
    key_all = gather_by_permutes(moved[1].reshape(span, HD), "sh", group_count, group_place, reach)
    span_first = group_place * span
    span_seg = lax.dynamic_slice_in_dim(segment_ids, span_first, span, 0)
    seg_first = jnp.sum((segment_ids < span_seg[0]).astype(jnp.int32))
    head_out = flash_attention(
        head_q,
        key_all.reshape(group_count * span, HD),
        value_all.reshape(group_count * span, HD),
        span_seg,
        segment_ids,
        span_first,
        seg_first,
        group_place,
        group_count,
    )
    attended = lax.all_to_all(
        head_out.reshape(sub_count, block_len, 1, HD), "sl", split_axis=0, concat_axis=2, tiled=True
    ).reshape(block_len, local_heads * HD)
    attn_part = jnp.dot(attended, out_weight, preferred_element_type=jnp.float32)
    row_count = block_len // exp_count
    row_first = exp_place * row_count
    residual_f = residual.astype(jnp.float32)
    attn_sum = sum_over_chip_pairs(attn_part.astype(jnp.bfloat16))
    after_attn = residual_f + attn_sum
    normed = rms_norm(after_attn, norm_gain)
    attn_rows = lax.dynamic_slice_in_dim(attn_sum, row_first, row_count, 0).astype(jnp.bfloat16)
    after_rows = lax.dynamic_slice_in_dim(after_attn, row_first, row_count, 0)
    shared_pre = jnp.einsum("td,gde->tge", normed, shared_in, preferred_element_type=jnp.float32)
    shared_hidden = (jax.nn.silu(shared_pre[:, 0]) * shared_pre[:, 1]).astype(jnp.bfloat16)
    shared_term = jnp.dot(shared_hidden, shared_out, preferred_element_type=jnp.float32)
    shared_factor = jax.nn.sigmoid(jnp.dot(normed, shared_gate, preferred_element_type=jnp.float32))
    flat_ids = expert_ids.reshape(-1)
    flat_index = jnp.arange(flat_ids.shape[0], dtype=jnp.int32)
    earlier_same = (flat_ids[None, :] == flat_ids[:, None]) & (flat_index[None, :] < flat_index[:, None])
    slot_rank = jnp.sum(earlier_same.astype(jnp.int32), axis=1)
    slot_place = flat_ids * CAP + slot_rank
    slot_local = SLOTS // seq_count
    model_width = normed.shape[1]
    core_count = lax.axis_size("co")
    col_count = model_width // core_count
    col_first = lax.axis_index("co") * col_count
    slot_rows = jnp.arange(SLOTS * CAP, dtype=jnp.int32)
    place_hit = (slot_place[None, :] == slot_rows[:, None]).reshape(SLOTS * CAP, block_len, TOPK)
    dispatch = jnp.any(place_hit, axis=2).astype(jnp.bfloat16)
    normed_part = lax.dynamic_slice_in_dim(normed, col_first, col_count, 1)
    outgoing_part = (
        jnp.dot(dispatch, normed_part, preferred_element_type=jnp.float32)
        .astype(jnp.bfloat16)
        .reshape(seq_count, slot_local, CAP, col_count)
    )
    incoming = lax.all_gather(
        lax.all_to_all(outgoing_part, SEQ, split_axis=0, concat_axis=0, tiled=True),
        "co",
        axis=3,
        tiled=True,
    )
    expert_part = expert_parts(incoming, expert_in, expert_out)
    summed = lax.psum_scatter(expert_part, "co", scatter_dimension=3, tiled=True).astype(
        jnp.float32
    )
    returned = lax.all_to_all(
        summed.astype(jnp.bfloat16), SEQ, split_axis=0, concat_axis=0, tiled=True
    ).astype(summed.dtype)
    select_rows = (slot_place[:, None] == slot_rows[None, :]).astype(jnp.bfloat16)
    picked = jnp.dot(
        select_rows,
        returned.reshape(SLOTS * CAP, col_count).astype(jnp.bfloat16),
        preferred_element_type=jnp.float32,
    ).reshape(block_len, TOPK, col_count)
    moe_cols = jnp.sum(gate_weights[:, :, None] * picked, axis=1)
    moe_term = lax.dynamic_update_slice_in_dim(
        jnp.zeros((block_len, model_width), jnp.float32), moe_cols, col_first, 1
    )
    combined = shared_factor[:, None] * shared_term + moe_term
    moe_rows = lax.psum_scatter(
        combined.astype(jnp.bfloat16), EXP, scatter_dimension=0, tiled=True
    ).astype(jnp.float32)
    mixed_out = (after_rows + moe_rows).astype(jnp.bfloat16)
    return (mixed_out, attn_rows, key_cache)


SEQ = ("sh", "sl")
EXP = ("zl", "co")


def solution(mesh):
    exp_count = mesh.shape["exp"]
    seq_count = mesh.shape["seq"]
    sub_count = HEADS // exp_count
    grid = mesh.devices.reshape(seq_count // sub_count, sub_count, exp_count // 2, 2)
    split_mesh = Mesh(grid, ("sh", "sl", "zl", "co"))
    return jax.shard_map(
        body,
        mesh=split_mesh,
        in_specs=(
            P(),
            P(SEQ, EXP),
            P(SEQ, EXP),
            P(SEQ, EXP),
            P(EXP, None),
            P(SEQ, None),
            P(),
            P(None, None, EXP),
            P(EXP, None),
            P(),
            P(SEQ, None, None, EXP),
            P(SEQ, EXP, None),
            P(SEQ, None),
            P(SEQ, None),
        ),
        out_specs=(P(("sh", "sl", "zl", "co"), None), P(("sh", "sl", "zl", "co"), None), P(SEQ, EXP)),
        check_vma=False,
    )
```

```python
import math

import jax
import jax.numpy as jnp
from jax import lax
from jax.sharding import Mesh, PartitionSpec as P
from jax.experimental import pallas as pl
from jax.experimental.pallas import tpu as pltpu

HD = 128
HEADS = 16
MOST = 6144
TOPK = 4
SLOTS = 64
CAP = 32


rope_base = 1000000.0
neg_fill = -1e30
norm_eps = 1e-06


KEY_TILE = 1024


def flash_kernel(bounds_ref, q_ref, k_ref, v_ref, qseg_ref, kseg_ref, o_ref, m_sc, l_sc, acc_sc):
    step = pl.program_id(0)
    first_chunk = bounds_ref[0]
    end_chunk = bounds_ref[1]
    query_first = bounds_ref[2]
    chunk = first_chunk + step
    rows = q_ref.shape[0]
    heads = q_ref.shape[1] // HD

    @pl.when(step == 0)
    def _():
        m_sc[...] = jnp.full(m_sc.shape, neg_fill, jnp.float32)
        l_sc[...] = jnp.zeros(l_sc.shape, jnp.float32)
        acc_sc[...] = jnp.zeros(acc_sc.shape, jnp.float32)

    @pl.when(chunk < end_chunk)
    def _():
        key_pos = chunk * KEY_TILE + lax.broadcasted_iota(jnp.int32, (1, KEY_TILE), 1)
        query_pos = query_first + lax.broadcasted_iota(jnp.int32, (rows, 1), 0)
        visible = (key_pos <= query_pos) & (kseg_ref[...] == qseg_ref[...])
        score_scale = 1.0 / math.sqrt(HD)
        for h in range(heads):
            cols = slice(h * HD, (h + 1) * HD)
            scores = (
                lax.dot_general(
                    q_ref[:, cols], k_ref[:, cols], (((1,), (1,)), ((), ())),
                    preferred_element_type=jnp.float32,
                )
                * score_scale
            )
            m_old = m_sc[h]
            m_new = jnp.maximum(
                m_old, jnp.max(jnp.where(visible, scores, neg_fill), axis=1, keepdims=True)
            )
            weights_f = jnp.where(visible, jnp.exp(scores - m_new), 0.0)
            rescale = jnp.exp(m_old - m_new)
            l_sc[h] = l_sc[h] * rescale + jnp.sum(weights_f, axis=1, keepdims=True)
            acc_sc[h] = acc_sc[h] * rescale + jnp.dot(
                weights_f.astype(jnp.bfloat16), v_ref[:, cols], preferred_element_type=jnp.float32
            )
            m_sc[h] = m_new

    @pl.when(step == pl.num_programs(0) - 1)
    def _():
        for h in range(heads):
            o_ref[:, h * HD:(h + 1) * HD] = (acc_sc[h] / l_sc[h]).astype(o_ref.dtype)


def flash_attention(
    rotated_q, key_all, value_all, query_seg, segment_ids, query_first, seg_first, place, groups
):
    rows, width = rotated_q.shape
    heads = width // HD
    key_count = key_all.shape[0]
    chunks = key_count // KEY_TILE
    first_chunk = seg_first // KEY_TILE
    end_chunk = (query_first + rows + KEY_TILE - 1) // KEY_TILE
    bounds = jnp.stack([first_chunk, end_chunk, query_first, place]).astype(jnp.int32)
    per_group = chunks // groups

    def kv_map(c, b):
        chunk = jnp.minimum(b[0] + c, b[1] - 1)
        turned = (chunk // per_group - b[3] + groups) % groups
        return (turned * per_group + chunk % per_group, 0)

    def kseg_map(c, b):
        return (0, jnp.minimum(b[0] + c, b[1] - 1))

    grid_spec = pltpu.PrefetchScalarGridSpec(
        num_scalar_prefetch=1,
        grid=(chunks,),
        in_specs=[
            pl.BlockSpec((rows, width), lambda c, b: (0, 0)),
            pl.BlockSpec((KEY_TILE, width), kv_map),
            pl.BlockSpec((KEY_TILE, width), kv_map),
            pl.BlockSpec((rows, 1), lambda c, b: (0, 0)),
            pl.BlockSpec((1, KEY_TILE), kseg_map),
        ],
        out_specs=pl.BlockSpec((rows, width), lambda c, b: (0, 0)),
        scratch_shapes=[
            pltpu.VMEM((heads, rows, 1), jnp.float32),
            pltpu.VMEM((heads, rows, 1), jnp.float32),
            pltpu.VMEM((heads, rows, HD), jnp.float32),
        ],
    )
    flops = 4 * rows * key_count * width
    return pl.pallas_call(
        flash_kernel,
        grid_spec=grid_spec,
        out_shape=jax.ShapeDtypeStruct((rows, width), jnp.bfloat16),
        compiler_params=pltpu.CompilerParams(
            dimension_semantics=("arbitrary",), vmem_limit_bytes=48 * 1024 * 1024
        ),
        cost_estimate=pl.CostEstimate(
            flops=flops,
            transcendentals=rows * key_count * heads,
            bytes_accessed=2 * key_count * width * 2 + 2 * rows * width * 2,
        ),
    )(
        bounds,
        rotated_q,
        key_all,
        value_all,
        query_seg.reshape(rows, 1).astype(jnp.int32),
        segment_ids.reshape(1, key_count).astype(jnp.int32),
    )


def shifted_copies(x, axis_name, count):
    moved = [x]
    for shift in range(1, count):
        pairs = [(i, (i + shift) % count) for i in range(count)]
        moved.append(lax.ppermute(x, axis_name, pairs))
    return moved


def sum_by_permutes(x, axis_name, count):
    total = x.astype(jnp.float32)
    for part in shifted_copies(x, axis_name, count)[1:]:
        total = total + part.astype(jnp.float32)
    return total


def causal_copies(x, axis_name, count, reach):
    moved = [x]
    for shift in range(1, count):
        pairs = [(i, i + shift) for i in range(count - shift)] if shift <= reach else []
        moved.append(lax.ppermute(x, axis_name, pairs) if pairs else jnp.zeros_like(x))
    return moved


def sum_over_chip_pairs(x):
    half = x.shape[1] // 2
    core = lax.axis_index("co")
    swap = [(0, 1), (1, 0)]
    pair = x.astype(jnp.float32) + lax.ppermute(x, "co", swap).astype(jnp.float32)
    mine = lax.dynamic_slice_in_dim(pair, core * half, half, 1).astype(jnp.bfloat16)
    done = (mine.astype(jnp.float32) + lax.ppermute(mine, "zl", swap).astype(jnp.float32)).astype(
        jnp.bfloat16
    )
    other = lax.ppermute(done, "co", swap)
    whole = jnp.where(
        core == 0, jnp.concatenate([done, other], axis=1), jnp.concatenate([other, done], axis=1)
    )
    return whole.astype(jnp.float32)


def gather_by_permutes(x, axis_name, count, place, reach):
    moved = causal_copies(x, axis_name, count, reach)
    return jnp.stack([moved[0]] + moved[1:][::-1])


def token_positions(segment_ids):
    stream_len = segment_ids.shape[0]
    token_index = jnp.arange(stream_len, dtype=jnp.int32)
    boundary = jnp.concatenate([jnp.ones((1,), jnp.bool_), segment_ids[1:] != segment_ids[:-1]])
    seg_start = lax.cummax(jnp.where(boundary, token_index, 0), axis=0)
    return (token_index - seg_start, seg_start)


def rotate(values_in, positions, head_count):
    half_dim = HD // 2
    frequency = rope_base ** (-(2.0 * jnp.arange(half_dim, dtype=jnp.float32)) / HD)
    angle_all = positions.astype(jnp.float32)[:, None] * frequency[None, :]
    cosine = jnp.cos(angle_all)[:, None, :]
    sine_part = jnp.sin(angle_all)[:, None, :]
    shaped = values_in.astype(jnp.float32).reshape(values_in.shape[0], head_count, HD)
    first_half = shaped[..., :half_dim]
    second_half = shaped[..., half_dim:]
    turned = jnp.concatenate(
        [
            first_half * cosine - second_half * sine_part,
            second_half * cosine + first_half * sine_part,
        ],
        axis=-1,
    )
    return turned.reshape(values_in.shape[0], head_count * HD).astype(jnp.bfloat16)


def rms_norm(hidden_in, norm_gain):
    mean_square = jnp.mean(hidden_in * hidden_in, axis=-1, keepdims=True)
    return (hidden_in * lax.rsqrt(mean_square + norm_eps) * norm_gain.astype(jnp.float32)).astype(
        jnp.bfloat16
    )


def expert_parts(incoming, expert_in, expert_out):
    expert_pre = jnp.einsum(
        "nscd,sgde->nscge", incoming, expert_in, preferred_element_type=jnp.float32
    )
    expert_hidden = (jax.nn.silu(expert_pre[..., 0, :]) * expert_pre[..., 1, :]).astype(
        jnp.bfloat16
    )
    return jnp.einsum(
        "nsce,sed->nscd", expert_hidden, expert_out, preferred_element_type=jnp.float32
    ).astype(jnp.bfloat16)


def body(
    segment_ids,
    queries,
    keys,
    values,
    out_weight,
    residual,
    norm_gain,
    shared_in,
    shared_out,
    shared_gate,
    expert_in,
    expert_out,
    expert_ids,
    gate_weights,
):
    seq_count = lax.axis_size("sh") * lax.axis_size("sl")
    exp_count = lax.axis_size("zl") * lax.axis_size("co")
    group_place = lax.axis_index("sh")
    sub_count = lax.axis_size("sl")
    seq_place = group_place * sub_count + lax.axis_index("sl")
    exp_place = lax.axis_index("zl") * lax.axis_size("co") + lax.axis_index("co")
    block_len = queries.shape[0]
    local_heads = queries.shape[1] // HD
    block_first = seq_place * block_len
    query_seg = lax.dynamic_slice_in_dim(segment_ids, block_first, block_len, 0)
    local_start = jnp.sum((segment_ids[None, :] < query_seg[:, None]).astype(jnp.int32), axis=1)
    local_pos = block_first + jnp.arange(block_len, dtype=jnp.int32) - local_start
    rotated_q = rotate(queries, local_pos, local_heads)
    key_cache = rotate(keys, local_pos, local_heads)
    sub_heads = (block_len, local_heads, HD)
    span = block_len * sub_count
    group_count = lax.axis_size("sh")
    reach = -(-(MOST + span - 1) // span) - 1
    value_moved = lax.all_to_all(
        values.reshape(sub_heads), "sl", split_axis=1, concat_axis=0, tiled=True
    ).reshape(span, HD)
    value_all = gather_by_permutes(value_moved, "sh", group_count, group_place, reach)
    stacked = jnp.stack([rotated_q, key_cache]).reshape((2,) + sub_heads)
    moved = lax.all_to_all(stacked, "sl", split_axis=2, concat_axis=1, tiled=True)
    head_q = moved[0].reshape(span, HD)
    key_all = gather_by_permutes(moved[1].reshape(span, HD), "sh", group_count, group_place, reach)
    span_first = group_place * span
    span_seg = lax.dynamic_slice_in_dim(segment_ids, span_first, span, 0)
    seg_first = jnp.sum((segment_ids < span_seg[0]).astype(jnp.int32))
    head_out = flash_attention(
        head_q,
        key_all.reshape(group_count * span, HD),
        value_all.reshape(group_count * span, HD),
        span_seg,
        segment_ids,
        span_first,
        seg_first,
        group_place,
        group_count,
    )
    attended = lax.all_to_all(
        head_out.reshape(sub_count, block_len, 1, HD), "sl", split_axis=0, concat_axis=2, tiled=True
    ).reshape(block_len, local_heads * HD)
    attn_part = jnp.dot(attended, out_weight, preferred_element_type=jnp.float32)
    row_count = block_len // exp_count
    row_first = exp_place * row_count
    residual_f = residual.astype(jnp.float32)
    attn_sum = sum_over_chip_pairs(attn_part.astype(jnp.bfloat16))
    after_attn = residual_f + attn_sum
    normed = rms_norm(after_attn, norm_gain)
    attn_rows = lax.dynamic_slice_in_dim(attn_sum, row_first, row_count, 0).astype(jnp.bfloat16)
    after_rows = lax.dynamic_slice_in_dim(after_attn, row_first, row_count, 0)
    shared_pre = jnp.einsum("td,gde->tge", normed, shared_in, preferred_element_type=jnp.float32)
    shared_hidden = (jax.nn.silu(shared_pre[:, 0]) * shared_pre[:, 1]).astype(jnp.bfloat16)
    shared_term = jnp.dot(shared_hidden, shared_out, preferred_element_type=jnp.float32)
    shared_factor = jax.nn.sigmoid(jnp.dot(normed, shared_gate, preferred_element_type=jnp.float32))
    flat_ids = expert_ids.reshape(-1)
    flat_index = jnp.arange(flat_ids.shape[0], dtype=jnp.int32)
    earlier_same = (flat_ids[None, :] == flat_ids[:, None]) & (flat_index[None, :] < flat_index[:, None])
    slot_rank = jnp.sum(earlier_same.astype(jnp.int32), axis=1)
    slot_place = flat_ids * CAP + slot_rank
    slot_local = SLOTS // seq_count
    model_width = normed.shape[1]
    core_count = lax.axis_size("co")
    col_count = model_width // core_count
    col_first = lax.axis_index("co") * col_count
    slot_rows = jnp.arange(SLOTS * CAP, dtype=jnp.int32)
    place_hit = (slot_place[None, :] == slot_rows[:, None]).reshape(SLOTS * CAP, block_len, TOPK)
    dispatch = jnp.any(place_hit, axis=2).astype(jnp.bfloat16)
    normed_part = lax.dynamic_slice_in_dim(normed, col_first, col_count, 1)
    outgoing_part = (
        jnp.dot(dispatch, normed_part, preferred_element_type=jnp.float32)
        .astype(jnp.bfloat16)
        .reshape(seq_count, slot_local, CAP, col_count)
    )
    incoming = lax.all_gather(
        lax.all_to_all(outgoing_part, SEQ, split_axis=0, concat_axis=0, tiled=True),
        "co",
        axis=3,
        tiled=True,
    )
    expert_part = expert_parts(incoming, expert_in, expert_out)
    summed = lax.psum_scatter(expert_part, "co", scatter_dimension=3, tiled=True).astype(
        jnp.float32
    )
    returned = lax.all_to_all(
        summed.astype(jnp.bfloat16), SEQ, split_axis=0, concat_axis=0, tiled=True
    ).astype(summed.dtype)
    select_rows = (slot_place[:, None] == slot_rows[None, :]).astype(jnp.bfloat16)
    picked = jnp.dot(
        select_rows,
        returned.reshape(SLOTS * CAP, col_count).astype(jnp.bfloat16),
        preferred_element_type=jnp.float32,
    ).reshape(block_len, TOPK, col_count)
    moe_cols = jnp.sum(gate_weights[:, :, None] * picked, axis=1)
    moe_term = lax.dynamic_update_slice_in_dim(
        jnp.zeros((block_len, model_width), jnp.float32), moe_cols, col_first, 1
    )
    combined = shared_factor[:, None] * shared_term + moe_term
    moe_rows = lax.psum_scatter(
        combined.astype(jnp.bfloat16), EXP, scatter_dimension=0, tiled=True
    ).astype(jnp.float32)
    mixed_out = (after_rows + moe_rows).astype(jnp.bfloat16)
    return (mixed_out, attn_rows, key_cache)


SEQ = ("sh", "sl")
EXP = ("zl", "co")


def solution(mesh):
    exp_count = mesh.shape["exp"]
    seq_count = mesh.shape["seq"]
    sub_count = HEADS // exp_count
    grid = mesh.devices.reshape(seq_count // sub_count, sub_count, exp_count // 2, 2)
    split_mesh = Mesh(grid, ("sh", "sl", "zl", "co"))
    return jax.shard_map(
        body,
        mesh=split_mesh,
        in_specs=(
            P(),
            P(SEQ, EXP),
            P(SEQ, EXP),
            P(SEQ, EXP),
            P(EXP, None),
            P(SEQ, None),
            P(),
            P(None, None, EXP),
            P(EXP, None),
            P(),
            P(SEQ, None, None, EXP),
            P(SEQ, EXP, None),
            P(SEQ, None),
            P(SEQ, None),
        ),
        out_specs=(P(("sh", "sl", "zl", "co"), None), P(("sh", "sl", "zl", "co"), None), P(SEQ, EXP)),
        check_vma=False,
    )
```

```python
import math

import jax
import jax.numpy as jnp
from jax import lax
from jax.sharding import Mesh, PartitionSpec as P
from jax.experimental import pallas as pl
from jax.experimental.pallas import tpu as pltpu

HD = 128
HEADS = 16
MOST = 6144
TOPK = 4
SLOTS = 64
CAP = 32


rope_base = 1000000.0
neg_fill = -1e30
norm_eps = 1e-06


KEY_TILE = 1024


def flash_kernel(bounds_ref, q_ref, k_ref, v_ref, qseg_ref, kseg_ref, o_ref, m_sc, l_sc, acc_sc):
    step = pl.program_id(0)
    first_chunk = bounds_ref[0]
    end_chunk = bounds_ref[1]
    query_first = bounds_ref[2]
    chunk = first_chunk + step
    rows = q_ref.shape[0]
    heads = q_ref.shape[1] // HD

    @pl.when(step == 0)
    def _():
        m_sc[...] = jnp.full(m_sc.shape, neg_fill, jnp.float32)
        l_sc[...] = jnp.zeros(l_sc.shape, jnp.float32)
        acc_sc[...] = jnp.zeros(acc_sc.shape, jnp.float32)

    @pl.when(chunk < end_chunk)
    def _():
        key_pos = chunk * KEY_TILE + lax.broadcasted_iota(jnp.int32, (1, KEY_TILE), 1)
        query_pos = query_first + lax.broadcasted_iota(jnp.int32, (rows, 1), 0)
        visible = (key_pos <= query_pos) & (kseg_ref[...] == qseg_ref[...])
        score_scale = 1.0 / math.sqrt(HD)
        for h in range(heads):
            cols = slice(h * HD, (h + 1) * HD)
            scores = (
                lax.dot_general(
                    q_ref[:, cols], k_ref[:, cols], (((1,), (1,)), ((), ())),
                    preferred_element_type=jnp.float32,
                )
                * score_scale
            )
            m_old = m_sc[h]
            m_new = jnp.maximum(
                m_old, jnp.max(jnp.where(visible, scores, neg_fill), axis=1, keepdims=True)
            )
            weights_f = jnp.where(visible, jnp.exp(scores - m_new), 0.0)
            rescale = jnp.exp(m_old - m_new)
            l_sc[h] = l_sc[h] * rescale + jnp.sum(weights_f, axis=1, keepdims=True)
            acc_sc[h] = acc_sc[h] * rescale + jnp.dot(
                weights_f.astype(jnp.bfloat16), v_ref[:, cols], preferred_element_type=jnp.float32
            )
            m_sc[h] = m_new

    @pl.when(step == pl.num_programs(0) - 1)
    def _():
        for h in range(heads):
            o_ref[:, h * HD:(h + 1) * HD] = (acc_sc[h] / l_sc[h]).astype(o_ref.dtype)


def flash_attention(
    rotated_q, key_all, value_all, query_seg, segment_ids, query_first, seg_first, place, groups
):
    rows, width = rotated_q.shape
    heads = width // HD
    key_count = key_all.shape[0]
    chunks = key_count // KEY_TILE
    first_chunk = seg_first // KEY_TILE
    end_chunk = (query_first + rows + KEY_TILE - 1) // KEY_TILE
    bounds = jnp.stack([first_chunk, end_chunk, query_first, place]).astype(jnp.int32)
    per_group = chunks // groups

    def kv_map(c, b):
        chunk = jnp.minimum(b[0] + c, b[1] - 1)
        turned = (chunk // per_group - b[3] + groups) % groups
        return (turned * per_group + chunk % per_group, 0)

    def kseg_map(c, b):
        return (0, jnp.minimum(b[0] + c, b[1] - 1))

    grid_spec = pltpu.PrefetchScalarGridSpec(
        num_scalar_prefetch=1,
        grid=(chunks,),
        in_specs=[
            pl.BlockSpec((rows, width), lambda c, b: (0, 0)),
            pl.BlockSpec((KEY_TILE, width), kv_map),
            pl.BlockSpec((KEY_TILE, width), kv_map),
            pl.BlockSpec((rows, 1), lambda c, b: (0, 0)),
            pl.BlockSpec((1, KEY_TILE), kseg_map),
        ],
        out_specs=pl.BlockSpec((rows, width), lambda c, b: (0, 0)),
        scratch_shapes=[
            pltpu.VMEM((heads, rows, 1), jnp.float32),
            pltpu.VMEM((heads, rows, 1), jnp.float32),
            pltpu.VMEM((heads, rows, HD), jnp.float32),
        ],
    )
    flops = 4 * rows * key_count * width
    return pl.pallas_call(
        flash_kernel,
        grid_spec=grid_spec,
        out_shape=jax.ShapeDtypeStruct((rows, width), jnp.bfloat16),
        compiler_params=pltpu.CompilerParams(
            dimension_semantics=("arbitrary",), vmem_limit_bytes=48 * 1024 * 1024
        ),
        cost_estimate=pl.CostEstimate(
            flops=flops,
            transcendentals=rows * key_count * heads,
            bytes_accessed=2 * key_count * width * 2 + 2 * rows * width * 2,
        ),
    )(
        bounds,
        rotated_q,
        key_all,
        value_all,
        query_seg.reshape(rows, 1).astype(jnp.int32),
        segment_ids.reshape(1, key_count).astype(jnp.int32),
    )


def shifted_copies(x, axis_name, count):
    moved = [x]
    for shift in range(1, count):
        pairs = [(i, (i + shift) % count) for i in range(count)]
        moved.append(lax.ppermute(x, axis_name, pairs))
    return moved


def sum_by_permutes(x, axis_name, count):
    total = x.astype(jnp.float32)
    for part in shifted_copies(x, axis_name, count)[1:]:
        total = total + part.astype(jnp.float32)
    return total


def causal_copies(x, axis_name, count, reach):
    moved = [x]
    for shift in range(1, count):
        pairs = [(i, i + shift) for i in range(count - shift)] if shift <= reach else []
        moved.append(lax.ppermute(x, axis_name, pairs) if pairs else jnp.zeros_like(x))
    return moved


def sum_over_chip_pairs(x):
    half = x.shape[1] // 2
    core = lax.axis_index("co")
    swap = [(0, 1), (1, 0)]
    pair = x.astype(jnp.float32) + lax.ppermute(x, "co", swap).astype(jnp.float32)
    mine = lax.dynamic_slice_in_dim(pair, core * half, half, 1).astype(jnp.bfloat16)
    done = (mine.astype(jnp.float32) + lax.ppermute(mine, "zl", swap).astype(jnp.float32)).astype(
        jnp.bfloat16
    )
    other = lax.ppermute(done, "co", swap)
    whole = jnp.where(
        core == 0, jnp.concatenate([done, other], axis=1), jnp.concatenate([other, done], axis=1)
    )
    return whole.astype(jnp.float32)


def rows_over_chip_pairs(x):
    swap = [(0, 1), (1, 0)]
    chip_rows = x.shape[0] // 2
    chip = lax.axis_index("zl")
    keep = lax.dynamic_slice_in_dim(x, chip * chip_rows, chip_rows, 0)
    give = lax.dynamic_slice_in_dim(x, (1 - chip) * chip_rows, chip_rows, 0)
    chip_sum = keep.astype(jnp.float32) + lax.ppermute(give, "zl", swap).astype(jnp.float32)
    core_rows = chip_rows // 2
    core = lax.axis_index("co")
    keep_c = lax.dynamic_slice_in_dim(chip_sum, core * core_rows, core_rows, 0)
    give_c = lax.dynamic_slice_in_dim(chip_sum, (1 - core) * core_rows, core_rows, 0)
    return keep_c + lax.ppermute(give_c.astype(jnp.bfloat16), "co", swap).astype(jnp.float32)


def gather_by_permutes(x, axis_name, count, place, reach):
    moved = causal_copies(x, axis_name, count, reach)
    return jnp.stack([moved[0]] + moved[1:][::-1])


def token_positions(segment_ids):
    stream_len = segment_ids.shape[0]
    token_index = jnp.arange(stream_len, dtype=jnp.int32)
    boundary = jnp.concatenate([jnp.ones((1,), jnp.bool_), segment_ids[1:] != segment_ids[:-1]])
    seg_start = lax.cummax(jnp.where(boundary, token_index, 0), axis=0)
    return (token_index - seg_start, seg_start)


def rotate(values_in, positions, head_count):
    half_dim = HD // 2
    frequency = rope_base ** (-(2.0 * jnp.arange(half_dim, dtype=jnp.float32)) / HD)
    angle_all = positions.astype(jnp.float32)[:, None] * frequency[None, :]
    cosine = jnp.cos(angle_all)[:, None, :]
    sine_part = jnp.sin(angle_all)[:, None, :]
    shaped = values_in.astype(jnp.float32).reshape(values_in.shape[0], head_count, HD)
    first_half = shaped[..., :half_dim]
    second_half = shaped[..., half_dim:]
    turned = jnp.concatenate(
        [
            first_half * cosine - second_half * sine_part,
            second_half * cosine + first_half * sine_part,
        ],
        axis=-1,
    )
    return turned.reshape(values_in.shape[0], head_count * HD).astype(jnp.bfloat16)


def rms_norm(hidden_in, norm_gain):
    mean_square = jnp.mean(hidden_in * hidden_in, axis=-1, keepdims=True)
    return (hidden_in * lax.rsqrt(mean_square + norm_eps) * norm_gain.astype(jnp.float32)).astype(
        jnp.bfloat16
    )


def expert_parts(incoming, expert_in, expert_out):
    expert_pre = jnp.einsum(
        "nscd,sgde->nscge", incoming, expert_in, preferred_element_type=jnp.float32
    )
    expert_hidden = (jax.nn.silu(expert_pre[..., 0, :]) * expert_pre[..., 1, :]).astype(
        jnp.bfloat16
    )
    return jnp.einsum(
        "nsce,sed->nscd", expert_hidden, expert_out, preferred_element_type=jnp.float32
    ).astype(jnp.bfloat16)


def body(
    segment_ids,
    queries,
    keys,
    values,
    out_weight,
    residual,
    norm_gain,
    shared_in,
    shared_out,
    shared_gate,
    expert_in,
    expert_out,
    expert_ids,
    gate_weights,
):
    seq_count = lax.axis_size("sh") * lax.axis_size("sl")
    exp_count = lax.axis_size("zl") * lax.axis_size("co")
    group_place = lax.axis_index("sh")
    sub_count = lax.axis_size("sl")
    seq_place = group_place * sub_count + lax.axis_index("sl")
    exp_place = lax.axis_index("zl") * lax.axis_size("co") + lax.axis_index("co")
    block_len = queries.shape[0]
    local_heads = queries.shape[1] // HD
    block_first = seq_place * block_len
    query_seg = lax.dynamic_slice_in_dim(segment_ids, block_first, block_len, 0)
    local_start = jnp.sum((segment_ids[None, :] < query_seg[:, None]).astype(jnp.int32), axis=1)
    local_pos = block_first + jnp.arange(block_len, dtype=jnp.int32) - local_start
    rotated_q = rotate(queries, local_pos, local_heads)
    key_cache = rotate(keys, local_pos, local_heads)
    sub_heads = (block_len, local_heads, HD)
    span = block_len * sub_count
    group_count = lax.axis_size("sh")
    reach = -(-(MOST + span - 1) // span) - 1
    value_moved = lax.all_to_all(
        values.reshape(sub_heads), "sl", split_axis=1, concat_axis=0, tiled=True
    ).reshape(span, HD)
    value_all = gather_by_permutes(value_moved, "sh", group_count, group_place, reach)
    stacked = jnp.stack([rotated_q, key_cache]).reshape((2,) + sub_heads)
    moved = lax.all_to_all(stacked, "sl", split_axis=2, concat_axis=1, tiled=True)
    head_q = moved[0].reshape(span, HD)
    key_all = gather_by_permutes(moved[1].reshape(span, HD), "sh", group_count, group_place, reach)
    span_first = group_place * span
    span_seg = lax.dynamic_slice_in_dim(segment_ids, span_first, span, 0)
    seg_first = jnp.sum((segment_ids < span_seg[0]).astype(jnp.int32))
    head_out = flash_attention(
        head_q,
        key_all.reshape(group_count * span, HD),
        value_all.reshape(group_count * span, HD),
        span_seg,
        segment_ids,
        span_first,
        seg_first,
        group_place,
        group_count,
    )
    attended = lax.all_to_all(
        head_out.reshape(sub_count, block_len, 1, HD), "sl", split_axis=0, concat_axis=2, tiled=True
    ).reshape(block_len, local_heads * HD)
    attn_part = jnp.dot(attended, out_weight, preferred_element_type=jnp.float32)
    row_count = block_len // exp_count
    row_first = exp_place * row_count
    residual_f = residual.astype(jnp.float32)
    attn_sum = sum_over_chip_pairs(attn_part.astype(jnp.bfloat16))
    after_attn = residual_f + attn_sum
    normed = rms_norm(after_attn, norm_gain)
    attn_rows = lax.dynamic_slice_in_dim(attn_sum, row_first, row_count, 0).astype(jnp.bfloat16)
    after_rows = lax.dynamic_slice_in_dim(after_attn, row_first, row_count, 0)
    shared_pre = jnp.einsum("td,gde->tge", normed, shared_in, preferred_element_type=jnp.float32)
    shared_hidden = (jax.nn.silu(shared_pre[:, 0]) * shared_pre[:, 1]).astype(jnp.bfloat16)
    shared_term = jnp.dot(shared_hidden, shared_out, preferred_element_type=jnp.float32)
    shared_factor = jax.nn.sigmoid(jnp.dot(normed, shared_gate, preferred_element_type=jnp.float32))
    flat_ids = expert_ids.reshape(-1)
    flat_index = jnp.arange(flat_ids.shape[0], dtype=jnp.int32)
    earlier_same = (flat_ids[None, :] == flat_ids[:, None]) & (flat_index[None, :] < flat_index[:, None])
    slot_rank = jnp.sum(earlier_same.astype(jnp.int32), axis=1)
    slot_place = flat_ids * CAP + slot_rank
    slot_local = SLOTS // seq_count
    model_width = normed.shape[1]
    core_count = lax.axis_size("co")
    col_count = model_width // core_count
    col_first = lax.axis_index("co") * col_count
    slot_rows = jnp.arange(SLOTS * CAP, dtype=jnp.int32)
    place_hit = (slot_place[None, :] == slot_rows[:, None]).reshape(SLOTS * CAP, block_len, TOPK)
    dispatch = jnp.any(place_hit, axis=2).astype(jnp.bfloat16)
    normed_part = lax.dynamic_slice_in_dim(normed, col_first, col_count, 1)
    outgoing_part = (
        jnp.dot(dispatch, normed_part, preferred_element_type=jnp.float32)
        .astype(jnp.bfloat16)
        .reshape(seq_count, slot_local, CAP, col_count)
    )
    incoming = lax.all_gather(
        lax.all_to_all(outgoing_part, SEQ, split_axis=0, concat_axis=0, tiled=True),
        "co",
        axis=3,
        tiled=True,
    )
    expert_part = expert_parts(incoming, expert_in, expert_out)
    summed = lax.psum_scatter(expert_part, "co", scatter_dimension=3, tiled=True).astype(
        jnp.float32
    )
    returned = lax.all_to_all(
        summed.astype(jnp.bfloat16), SEQ, split_axis=0, concat_axis=0, tiled=True
    ).astype(summed.dtype)
    select_rows = (slot_place[:, None] == slot_rows[None, :]).astype(jnp.bfloat16)
    picked = jnp.dot(
        select_rows,
        returned.reshape(SLOTS * CAP, col_count).astype(jnp.bfloat16),
        preferred_element_type=jnp.float32,
    ).reshape(block_len, TOPK, col_count)
    moe_cols = jnp.sum(gate_weights[:, :, None] * picked, axis=1)
    moe_term = lax.dynamic_update_slice_in_dim(
        jnp.zeros((block_len, model_width), jnp.float32), moe_cols, col_first, 1
    )
    combined = shared_factor[:, None] * shared_term + moe_term
    moe_rows = rows_over_chip_pairs(combined.astype(jnp.bfloat16))
    mixed_out = (after_rows + moe_rows).astype(jnp.bfloat16)
    return (mixed_out, attn_rows, key_cache)


SEQ = ("sh", "sl")
EXP = ("zl", "co")


def solution(mesh):
    exp_count = mesh.shape["exp"]
    seq_count = mesh.shape["seq"]
    sub_count = HEADS // exp_count
    grid = mesh.devices.reshape(seq_count // sub_count, sub_count, exp_count // 2, 2)
    split_mesh = Mesh(grid, ("sh", "sl", "zl", "co"))
    return jax.shard_map(
        body,
        mesh=split_mesh,
        in_specs=(
            P(),
            P(SEQ, EXP),
            P(SEQ, EXP),
            P(SEQ, EXP),
            P(EXP, None),
            P(SEQ, None),
            P(),
            P(None, None, EXP),
            P(EXP, None),
            P(),
            P(SEQ, None, None, EXP),
            P(SEQ, EXP, None),
            P(SEQ, None),
            P(SEQ, None),
        ),
        out_specs=(P(("sh", "sl", "zl", "co"), None), P(("sh", "sl", "zl", "co"), None), P(SEQ, EXP)),
        check_vma=False,
    )
```

```python
import math

import jax
import jax.numpy as jnp
from jax import lax
from jax.sharding import Mesh, PartitionSpec as P
from jax.experimental import pallas as pl
from jax.experimental.pallas import tpu as pltpu

HD = 128
HEADS = 16
MOST = 6144
TOPK = 4
SLOTS = 64
CAP = 32


rope_base = 1000000.0
neg_fill = -1e30
norm_eps = 1e-06


KEY_TILE = 1024


def flash_kernel(bounds_ref, q_ref, k_ref, v_ref, qseg_ref, kseg_ref, o_ref, m_sc, l_sc, acc_sc):
    step = pl.program_id(0)
    first_chunk = bounds_ref[0]
    end_chunk = bounds_ref[1]
    query_first = bounds_ref[2]
    chunk = first_chunk + step
    rows = q_ref.shape[0]
    heads = q_ref.shape[1] // HD

    @pl.when(step == 0)
    def _():
        m_sc[...] = jnp.full(m_sc.shape, neg_fill, jnp.float32)
        l_sc[...] = jnp.zeros(l_sc.shape, jnp.float32)
        acc_sc[...] = jnp.zeros(acc_sc.shape, jnp.float32)

    @pl.when(chunk < end_chunk)
    def _():
        key_pos = chunk * KEY_TILE + lax.broadcasted_iota(jnp.int32, (1, KEY_TILE), 1)
        query_pos = query_first + lax.broadcasted_iota(jnp.int32, (rows, 1), 0)
        visible = (key_pos <= query_pos) & (kseg_ref[...] == qseg_ref[...])
        score_scale = 1.0 / math.sqrt(HD)
        for h in range(heads):
            cols = slice(h * HD, (h + 1) * HD)
            scores = (
                lax.dot_general(
                    q_ref[:, cols], k_ref[:, cols], (((1,), (1,)), ((), ())),
                    preferred_element_type=jnp.float32,
                )
                * score_scale
            )
            m_old = m_sc[h]
            m_new = jnp.maximum(
                m_old, jnp.max(jnp.where(visible, scores, neg_fill), axis=1, keepdims=True)
            )
            weights_f = jnp.where(visible, jnp.exp(scores - m_new), 0.0)
            rescale = jnp.exp(m_old - m_new)
            l_sc[h] = l_sc[h] * rescale + jnp.sum(weights_f, axis=1, keepdims=True)
            acc_sc[h] = acc_sc[h] * rescale + jnp.dot(
                weights_f.astype(jnp.bfloat16), v_ref[:, cols], preferred_element_type=jnp.float32
            )
            m_sc[h] = m_new

    @pl.when(step == pl.num_programs(0) - 1)
    def _():
        for h in range(heads):
            o_ref[:, h * HD:(h + 1) * HD] = (acc_sc[h] / l_sc[h]).astype(o_ref.dtype)


def flash_attention(
    rotated_q, key_all, value_all, query_seg, segment_ids, query_first, seg_first, place, groups
):
    rows, width = rotated_q.shape
    heads = width // HD
    key_count = key_all.shape[0]
    chunks = key_count // KEY_TILE
    first_chunk = seg_first // KEY_TILE
    end_chunk = (query_first + rows + KEY_TILE - 1) // KEY_TILE
    bounds = jnp.stack([first_chunk, end_chunk, query_first, place]).astype(jnp.int32)
    per_group = chunks // groups

    def kv_map(c, b):
        chunk = jnp.minimum(b[0] + c, b[1] - 1)
        turned = (chunk // per_group - b[3] + groups) % groups
        return (turned * per_group + chunk % per_group, 0)

    def kseg_map(c, b):
        return (0, jnp.minimum(b[0] + c, b[1] - 1))

    grid_spec = pltpu.PrefetchScalarGridSpec(
        num_scalar_prefetch=1,
        grid=(chunks,),
        in_specs=[
            pl.BlockSpec((rows, width), lambda c, b: (0, 0)),
            pl.BlockSpec((KEY_TILE, width), kv_map),
            pl.BlockSpec((KEY_TILE, width), kv_map),
            pl.BlockSpec((rows, 1), lambda c, b: (0, 0)),
            pl.BlockSpec((1, KEY_TILE), kseg_map),
        ],
        out_specs=pl.BlockSpec((rows, width), lambda c, b: (0, 0)),
        scratch_shapes=[
            pltpu.VMEM((heads, rows, 1), jnp.float32),
            pltpu.VMEM((heads, rows, 1), jnp.float32),
            pltpu.VMEM((heads, rows, HD), jnp.float32),
        ],
    )
    flops = 4 * rows * key_count * width
    return pl.pallas_call(
        flash_kernel,
        grid_spec=grid_spec,
        out_shape=jax.ShapeDtypeStruct((rows, width), jnp.bfloat16),
        compiler_params=pltpu.CompilerParams(
            dimension_semantics=("arbitrary",), vmem_limit_bytes=48 * 1024 * 1024
        ),
        cost_estimate=pl.CostEstimate(
            flops=flops,
            transcendentals=rows * key_count * heads,
            bytes_accessed=2 * key_count * width * 2 + 2 * rows * width * 2,
        ),
    )(
        bounds,
        rotated_q,
        key_all,
        value_all,
        query_seg.reshape(rows, 1).astype(jnp.int32),
        segment_ids.reshape(1, key_count).astype(jnp.int32),
    )


def shifted_copies(x, axis_name, count):
    moved = [x]
    for shift in range(1, count):
        pairs = [(i, (i + shift) % count) for i in range(count)]
        moved.append(lax.ppermute(x, axis_name, pairs))
    return moved


def sum_by_permutes(x, axis_name, count):
    total = x.astype(jnp.float32)
    for part in shifted_copies(x, axis_name, count)[1:]:
        total = total + part.astype(jnp.float32)
    return total


def causal_copies(x, axis_name, count, reach):
    moved = [x]
    for shift in range(1, count):
        pairs = [(i, i + shift) for i in range(count - shift)] if shift <= reach else []
        moved.append(lax.ppermute(x, axis_name, pairs) if pairs else jnp.zeros_like(x))
    return moved


def sum_over_chip_pairs(x):
    half = x.shape[1] // 2
    core = lax.axis_index("co")
    swap = [(0, 1), (1, 0)]
    pair = x.astype(jnp.float32) + lax.ppermute(x, "co", swap).astype(jnp.float32)
    mine = lax.dynamic_slice_in_dim(pair, core * half, half, 1).astype(jnp.bfloat16)
    done = (mine.astype(jnp.float32) + lax.ppermute(mine, "zl", swap).astype(jnp.float32)).astype(
        jnp.bfloat16
    )
    other = lax.ppermute(done, "co", swap)
    whole = jnp.where(
        core == 0, jnp.concatenate([done, other], axis=1), jnp.concatenate([other, done], axis=1)
    )
    return whole.astype(jnp.float32)


def gather_by_permutes(x, axis_name, count, place, reach):
    moved = causal_copies(x, axis_name, count, reach)
    return jnp.stack([moved[0]] + moved[1:][::-1])


def token_positions(segment_ids):
    stream_len = segment_ids.shape[0]
    token_index = jnp.arange(stream_len, dtype=jnp.int32)
    boundary = jnp.concatenate([jnp.ones((1,), jnp.bool_), segment_ids[1:] != segment_ids[:-1]])
    seg_start = lax.cummax(jnp.where(boundary, token_index, 0), axis=0)
    return (token_index - seg_start, seg_start)


def rotate(values_in, positions, head_count):
    half_dim = HD // 2
    frequency = rope_base ** (-(2.0 * jnp.arange(half_dim, dtype=jnp.float32)) / HD)
    angle_all = positions.astype(jnp.float32)[:, None] * frequency[None, :]
    cosine = jnp.cos(angle_all)[:, None, :]
    sine_part = jnp.sin(angle_all)[:, None, :]
    shaped = values_in.astype(jnp.float32).reshape(values_in.shape[0], head_count, HD)
    first_half = shaped[..., :half_dim]
    second_half = shaped[..., half_dim:]
    turned = jnp.concatenate(
        [
            first_half * cosine - second_half * sine_part,
            second_half * cosine + first_half * sine_part,
        ],
        axis=-1,
    )
    return turned.reshape(values_in.shape[0], head_count * HD).astype(jnp.bfloat16)


def rms_norm(hidden_in, norm_gain):
    mean_square = jnp.mean(hidden_in * hidden_in, axis=-1, keepdims=True)
    return (hidden_in * lax.rsqrt(mean_square + norm_eps) * norm_gain.astype(jnp.float32)).astype(
        jnp.bfloat16
    )


def expert_parts(incoming, expert_in, expert_out):
    expert_pre = jnp.einsum(
        "nscd,sgde->nscge", incoming, expert_in, preferred_element_type=jnp.float32
    )
    expert_hidden = (jax.nn.silu(expert_pre[..., 0, :]) * expert_pre[..., 1, :]).astype(
        jnp.bfloat16
    )
    return jnp.einsum(
        "nsce,sed->nscd", expert_hidden, expert_out, preferred_element_type=jnp.float32
    ).astype(jnp.bfloat16)


def body(
    segment_ids,
    queries,
    keys,
    values,
    out_weight,
    residual,
    norm_gain,
    shared_in,
    shared_out,
    shared_gate,
    expert_in,
    expert_out,
    expert_ids,
    gate_weights,
):
    seq_count = lax.axis_size("sh") * lax.axis_size("sl")
    exp_count = lax.axis_size("zl") * lax.axis_size("co")
    group_place = lax.axis_index("sh")
    sub_count = lax.axis_size("sl")
    seq_place = group_place * sub_count + lax.axis_index("sl")
    exp_place = lax.axis_index("zl") * lax.axis_size("co") + lax.axis_index("co")
    block_len = queries.shape[0]
    local_heads = queries.shape[1] // HD
    block_first = seq_place * block_len
    query_seg = lax.dynamic_slice_in_dim(segment_ids, block_first, block_len, 0)
    local_start = jnp.sum((segment_ids[None, :] < query_seg[:, None]).astype(jnp.int32), axis=1)
    local_pos = block_first + jnp.arange(block_len, dtype=jnp.int32) - local_start
    rotated_q = rotate(queries, local_pos, local_heads)
    key_cache = rotate(keys, local_pos, local_heads)
    sub_heads = (block_len, local_heads, HD)
    span = block_len * sub_count
    group_count = lax.axis_size("sh")
    reach = -(-(MOST + span - 1) // span) - 1
    value_moved = lax.all_to_all(
        values.reshape(sub_heads), "sl", split_axis=1, concat_axis=0, tiled=True
    ).reshape(span, HD)
    value_all = gather_by_permutes(value_moved, "sh", group_count, group_place, reach)
    stacked = jnp.stack([rotated_q, key_cache]).reshape((2,) + sub_heads)
    moved = lax.all_to_all(stacked, "sl", split_axis=2, concat_axis=1, tiled=True)
    head_q = moved[0].reshape(span, HD)
    key_all = gather_by_permutes(moved[1].reshape(span, HD), "sh", group_count, group_place, reach)
    span_first = group_place * span
    span_seg = lax.dynamic_slice_in_dim(segment_ids, span_first, span, 0)
    seg_first = jnp.sum((segment_ids < span_seg[0]).astype(jnp.int32))
    head_out = flash_attention(
        head_q,
        key_all.reshape(group_count * span, HD),
        value_all.reshape(group_count * span, HD),
        span_seg,
        segment_ids,
        span_first,
        seg_first,
        group_place,
        group_count,
    )
    attended = lax.all_to_all(
        head_out.reshape(sub_count, block_len, 1, HD), "sl", split_axis=0, concat_axis=2, tiled=True
    ).reshape(block_len, local_heads * HD)
    attn_part = jnp.dot(attended, out_weight, preferred_element_type=jnp.float32)
    row_count = block_len // exp_count
    row_first = exp_place * row_count
    residual_f = residual.astype(jnp.float32)
    attn_sum = sum_over_chip_pairs(attn_part.astype(jnp.bfloat16))
    after_attn = residual_f + attn_sum
    normed = rms_norm(after_attn, norm_gain)
    attn_rows = lax.dynamic_slice_in_dim(attn_sum, row_first, row_count, 0).astype(jnp.bfloat16)
    after_rows = lax.dynamic_slice_in_dim(after_attn, row_first, row_count, 0)
    shared_pre = jnp.einsum("td,gde->tge", normed, shared_in, preferred_element_type=jnp.float32)
    shared_hidden = (jax.nn.silu(shared_pre[:, 0]) * shared_pre[:, 1]).astype(jnp.bfloat16)
    shared_term = jnp.dot(shared_hidden, shared_out, preferred_element_type=jnp.float32)
    shared_factor = jax.nn.sigmoid(jnp.dot(normed, shared_gate, preferred_element_type=jnp.float32))
    flat_ids = expert_ids.reshape(-1)
    flat_index = jnp.arange(flat_ids.shape[0], dtype=jnp.int32)
    earlier_same = (flat_ids[None, :] == flat_ids[:, None]) & (flat_index[None, :] < flat_index[:, None])
    slot_rank = jnp.sum(earlier_same.astype(jnp.int32), axis=1)
    slot_place = flat_ids * CAP + slot_rank
    slot_local = SLOTS // seq_count
    model_width = normed.shape[1]
    core_count = lax.axis_size("co")
    col_count = model_width // core_count
    col_first = lax.axis_index("co") * col_count
    slot_rows = jnp.arange(SLOTS * CAP, dtype=jnp.int32)
    place_hit = (slot_place[None, :] == slot_rows[:, None]).reshape(SLOTS * CAP, block_len, TOPK)
    dispatch = jnp.any(place_hit, axis=2).astype(jnp.bfloat16)
    normed_part = lax.dynamic_slice_in_dim(normed, col_first, col_count, 1)
    outgoing_part = (
        jnp.dot(dispatch, normed_part, preferred_element_type=jnp.float32)
        .astype(jnp.bfloat16)
        .reshape(seq_count, slot_local, CAP, col_count)
    )
    arrived = lax.all_to_all(outgoing_part, SEQ, split_axis=0, concat_axis=0, tiled=True)
    core = lax.axis_index("co")
    partner = lax.ppermute(arrived, "co", [(0, 1), (1, 0)])
    incoming = jnp.where(
        core == 0,
        jnp.concatenate([arrived, partner], axis=3),
        jnp.concatenate([partner, arrived], axis=3),
    )
    expert_part = expert_parts(incoming, expert_in, expert_out)
    keep = lax.dynamic_slice_in_dim(expert_part, core * col_count, col_count, 3)
    give = lax.dynamic_slice_in_dim(expert_part, (1 - core) * col_count, col_count, 3)
    summed = (
        keep.astype(jnp.float32)
        + lax.ppermute(give, "co", [(0, 1), (1, 0)]).astype(jnp.float32)
    ).astype(jnp.bfloat16).astype(jnp.float32)
    returned = lax.all_to_all(
        summed.astype(jnp.bfloat16), SEQ, split_axis=0, concat_axis=0, tiled=True
    ).astype(summed.dtype)
    select_rows = (slot_place[:, None] == slot_rows[None, :]).astype(jnp.bfloat16)
    picked = jnp.dot(
        select_rows,
        returned.reshape(SLOTS * CAP, col_count).astype(jnp.bfloat16),
        preferred_element_type=jnp.float32,
    ).reshape(block_len, TOPK, col_count)
    moe_cols = jnp.sum(gate_weights[:, :, None] * picked, axis=1)
    moe_term = lax.dynamic_update_slice_in_dim(
        jnp.zeros((block_len, model_width), jnp.float32), moe_cols, col_first, 1
    )
    combined = shared_factor[:, None] * shared_term + moe_term
    moe_rows = lax.psum_scatter(
        combined.astype(jnp.bfloat16), EXP, scatter_dimension=0, tiled=True
    ).astype(jnp.float32)
    mixed_out = (after_rows + moe_rows).astype(jnp.bfloat16)
    return (mixed_out, attn_rows, key_cache)


SEQ = ("sh", "sl")
EXP = ("zl", "co")


def solution(mesh):
    exp_count = mesh.shape["exp"]
    seq_count = mesh.shape["seq"]
    sub_count = HEADS // exp_count
    grid = mesh.devices.reshape(seq_count // sub_count, sub_count, exp_count // 2, 2)
    split_mesh = Mesh(grid, ("sh", "sl", "zl", "co"))
    return jax.shard_map(
        body,
        mesh=split_mesh,
        in_specs=(
            P(),
            P(SEQ, EXP),
            P(SEQ, EXP),
            P(SEQ, EXP),
            P(EXP, None),
            P(SEQ, None),
            P(),
            P(None, None, EXP),
            P(EXP, None),
            P(),
            P(SEQ, None, None, EXP),
            P(SEQ, EXP, None),
            P(SEQ, None),
            P(SEQ, None),
        ),
        out_specs=(P(("sh", "sl", "zl", "co"), None), P(("sh", "sl", "zl", "co"), None), P(SEQ, EXP)),
        check_vma=False,
    )
```
